128 devices in a mesh: row: 16 (over z, x), col: 8 (over y, core).
Axes of the slice: x: 4, y: 4, z: 4, core: 2. Of those that a mesh axis runs over, the one named last changes fastest.
Arguments:
- pixels: bfloat16 [256, 128, 768], P('row', 'col'), may hold values from -6 to 6
- conv_weight: bfloat16 [3, 3, 64, 128], replicated, may hold values from -0.25 to 0.25
- time_weight: bfloat16 [3, 16, 8, 8], replicated, may hold values from -1.25 to 1.25
- class_weight: bfloat16 [128, 20], replicated, may hold values from -0.5 to 0.5
- pixel_slot: int32 [256, 128], P('row', 'col'), may hold values from 0 to 63, as said below
- straddle_dir: int32 [16, 8, 32], P('row', 'col'), may hold values from 0 to 8, as said below
- straddle_slot: int32 [16, 8, 32], P('row', 'col'), may hold values from 0 to 31
- labels: int32 [16, 8, 32], P('row', 'col'), may hold values from 0 to 19
Outputs:
- input_grad: bfloat16 [256, 128, 768], P('row', 'col')
- conv_grad: float32 [3, 3, 64, 128], replicated
- time_grad: float32 [3, 16, 8, 8], replicated
- class_grad: float32 [128, 20], replicated
The draws below stay inside these ranges and needn't reach their ends.
Inputs may be any that keep to these rules, and one draw needn't show every extreme that they name: `pixel_slot`: below 32 a pixel is in the tile's own parcel of that number, from 32 on in its straddling entry of that number minus 32. Every index of a tile's list is held by at least one pixel of that tile. The owner of entry e of tile (r, c) is tile (r + q // 3 - 1, c + q % 3 - 1) with q = straddle_dir[r, c, e]; q is never 4 and the owner lies within the scene.
All inputs are finite; a program needn't handle non-finite values.
Results may differ from the reference program's by a relative error of at most 0.012.
Values may be sent and summed in bfloat16 or wider, within the bound.
No kernel may reach another device: no remote copies, remote signals or barrier semaphores. Data moves between devices by JAX's collectives and lax.ppermute only.
A program may use at most 64 MiB of HBM per device.

```python
import jax
import jax.numpy as jnp
from jax import lax

HT = 16
WT = 16
DATES = 12
C_IN = 64
C_OUT = 128
GROUPS = 16
CLASSES = 20
P_OWN = 32
S_STR = 32
CPG = 8
NH = 256
NW = 128
PARCELS = 4096
N_ROW = 16
N_COL = 8


def draw_pixel_slot(key, part):
    row_tiles = NH // HT
    col_tiles = NW // WT
    slot_count = P_OWN + S_STR
    key_base = jax.random.fold_in(key, 11)
    key_rank = jax.random.fold_in(key, 12)
    base_slot = jax.random.randint(key_base, (row_tiles, col_tiles, HT * WT), 0, slot_count)
    local_index = jnp.arange(HT * WT, dtype=jnp.int32)
    scores = jax.random.randint(key_rank, (row_tiles, col_tiles, HT * WT), 0, 32768) * (HT * WT) + local_index
    ranking = jnp.argsort(jnp.argsort(scores, axis=-1), axis=-1)
    slot_map = jnp.where(ranking < slot_count, ranking, base_slot)
    slot_map = slot_map.reshape(row_tiles, col_tiles, HT, WT).transpose(0, 2, 1, 3).reshape(NH, NW)
    return slot_map.astype(jnp.int32)


def draw_straddle_dir(key, part):
    row_tiles = NH // HT
    col_tiles = NW // WT
    key_row = jax.random.fold_in(key, 21)
    key_col = jax.random.fold_in(key, 22)
    shape_out = (row_tiles, col_tiles, S_STR)
    row_step = jax.random.randint(key_row, shape_out, -1, 2)
    col_step = jax.random.randint(key_col, shape_out, -1, 2)
    tile_row = jnp.arange(row_tiles, dtype=jnp.int32)[:, None, None]
    tile_col = jnp.arange(col_tiles, dtype=jnp.int32)[None, :, None]
    row_step = jnp.where(tile_row + row_step < 0, 1, jnp.where(tile_row + row_step >= row_tiles, -1, row_step))
    col_step = jnp.where(tile_col + col_step < 0, 1, jnp.where(tile_col + col_step >= col_tiles, -1, col_step))
    itself = (row_step == 0) & (col_step == 0)
    col_step = jnp.where(itself, jnp.where(tile_col + 1 < col_tiles, 1, -1), col_step)
    return ((row_step + 1) * 3 + col_step + 1).astype(jnp.int32)


def with_ends(values, stream_key, smallest, largest):
    shape = values.shape
    index_at = [jax.random.randint(jax.random.fold_in(stream_key, axis), (), 0, shape[axis]) for axis in range(len(shape))]
    values = values.at[tuple(index_at)].set(smallest)
    longest = shape.index(max(shape))
    index_at[longest] = (index_at[longest] + 1) % shape[longest]
    return values.at[tuple(index_at)].set(largest)


def levels(rng, shape, split, low, largest):
    factor_of = 1.0
    for position, blocks in split:
        heights = jax.random.uniform(jax.random.fold_in(jax.random.fold_in(rng, 6), position), (blocks,), jnp.float32, low / len(split), largest / len(split))
        factor_of = factor_of * jnp.repeat(jnp.exp(heights), shape[position] // blocks).reshape((-1,) + (1,) * (len(shape) - 1 - position))
    return factor_of


def scatter_about(own_key, dims, spread, most, cuts=(), kind=jnp.bfloat16):
    factor_of = levels(own_key, dims, cuts, -0.22, 0.18) if cuts else 1.0
    values = jax.random.normal(own_key, dims, jnp.float32) * spread * factor_of
    return jnp.minimum(jnp.maximum(values, -most), most).astype(kind)


def setup_inputs(seed: int = 0) -> dict:
    key_list = jax.random.split(jax.random.key(seed), 9)
    pixels = scatter_about(key_list[0], (NH, NW, DATES * C_IN), 1.0, 6.0, ((0, 16), (1, 8)))
    conv_weight = scatter_about(key_list[1], (3, 3, C_IN, C_OUT), (9 * C_IN) ** -0.5, 0.25)
    time_weight = scatter_about(key_list[2], (3, GROUPS, CPG, CPG), (3 * CPG) ** -0.5, 1.25)
    class_weight = scatter_about(key_list[3], (C_OUT, CLASSES), C_OUT ** -0.5, 0.5)
    pixel_slot = draw_pixel_slot(jax.random.fold_in(key_list[8], 71), 0)
    straddle_dir = draw_straddle_dir(jax.random.fold_in(key_list[8], 71), 0)
    straddle_slot = with_ends(jax.random.randint(key_list[6], (N_ROW, N_COL, S_STR), 0, P_OWN), jax.random.fold_in(key_list[6], 1), 0, P_OWN - 1).astype(jnp.int32)
    labels = with_ends(jax.random.randint(key_list[7], (N_ROW, N_COL, P_OWN), 0, CLASSES), jax.random.fold_in(key_list[7], 1), 0, CLASSES - 1).astype(jnp.int32)
    return {"pixels": pixels, "conv_weight": conv_weight, "time_weight": time_weight, "class_weight": class_weight, "pixel_slot": pixel_slot, "straddle_dir": straddle_dir, "straddle_slot": straddle_slot, "labels": labels}


EPSILON = 1e-05
PRECISE = lax.Precision.HIGHEST

def silu_slope(value):
    sig = jax.nn.sigmoid(value)
    return sig * (1.0 + value * (1.0 - sig))

def spatial_conv(padded, conv_weight, out_rows, out_cols):
    running_sum = jnp.zeros((out_rows, out_cols, DATES, C_OUT), jnp.float32)
    for row_tap in range(3):
        for col_tap in range(3):
            window = padded[row_tap:row_tap + out_rows, col_tap:col_tap + out_cols].astype(jnp.float32)
            running_sum = running_sum + jnp.einsum('ijtc,cd->ijtd', window, conv_weight[row_tap, col_tap].astype(jnp.float32), precision=PRECISE)
    return running_sum

def temporal_conv(hidden, time_weight):
    band_rows, band_cols = (hidden.shape[0], hidden.shape[1])
    grouped = hidden.astype(jnp.float32).reshape(band_rows, band_cols, DATES, GROUPS, CPG)
    padded = jnp.pad(grouped, ((0, 0), (0, 0), (1, 1), (0, 0), (0, 0)))
    running_sum = jnp.zeros((band_rows, band_cols, DATES, GROUPS, CPG), jnp.float32)
    for time_tap in range(3):
        running_sum = running_sum + jnp.einsum('ijtgc,gcd->ijtgd', padded[:, :, time_tap:time_tap + DATES], time_weight[time_tap].astype(jnp.float32), precision=PRECISE)
    return running_sum.reshape(band_rows, band_cols, DATES, C_OUT)

def temporal_back(grad_mixed, time_weight):
    band_rows, band_cols = (grad_mixed.shape[0], grad_mixed.shape[1])
    grouped = grad_mixed.astype(jnp.float32).reshape(band_rows, band_cols, DATES, GROUPS, CPG)
    padded = jnp.pad(grouped, ((0, 0), (0, 0), (1, 1), (0, 0), (0, 0)))
    running_sum = jnp.zeros((band_rows, band_cols, DATES, GROUPS, CPG), jnp.float32)
    for time_tap in range(3):
        running_sum = running_sum + jnp.einsum('ijtgd,gcd->ijtgc', padded[:, :, 2 - time_tap:2 - time_tap + DATES], time_weight[time_tap].astype(jnp.float32), precision=PRECISE)
    return running_sum.reshape(band_rows, band_cols, DATES, C_OUT)

def temporal_weight_grad(hidden, grad_mixed):
    band_rows, band_cols = (hidden.shape[0], hidden.shape[1])
    grouped = hidden.astype(jnp.float32).reshape(band_rows, band_cols, DATES, GROUPS, CPG)
    padded = jnp.pad(grouped, ((0, 0), (0, 0), (1, 1), (0, 0), (0, 0)))
    grad_grouped = grad_mixed.astype(jnp.float32).reshape(band_rows, band_cols, DATES, GROUPS, CPG)
    taps = [jnp.einsum('ijtgc,ijtgd->gcd', padded[:, :, time_tap:time_tap + DATES], grad_grouped, precision=PRECISE) for time_tap in range(3)]
    return jnp.stack(taps)

def parcel_index(pixel_slot, straddle_dir, straddle_slot):
    tile_row = jnp.broadcast_to((jnp.arange(NH, dtype=jnp.int32) // HT)[:, None], (NH, NW))
    tile_col = jnp.broadcast_to((jnp.arange(NW, dtype=jnp.int32) // WT)[None, :], (NH, NW))
    home_tile = tile_row * N_COL + tile_col
    foreign = jnp.clip(pixel_slot - P_OWN, 0, S_STR - 1).astype(jnp.int32)
    direction = straddle_dir[tile_row, tile_col, foreign]
    owner_slot = straddle_slot[tile_row, tile_col, foreign]
    owner_tile = (tile_row + direction // 3 - 1) * N_COL + tile_col + direction % 3 - 1
    return jnp.where(pixel_slot < P_OWN, home_tile * P_OWN + pixel_slot, owner_tile * P_OWN + owner_slot).astype(jnp.int32)

def reference(pixels, conv_weight, time_weight, class_weight, pixel_slot, straddle_dir, straddle_slot, labels):
    padded_pixels = jnp.pad(pixels.reshape(NH, NW, DATES, C_IN), ((2, 2), (1, 1), (0, 0), (0, 0)))

    def forward_band(band_index):
        first_row = band_index * HT
        row_block = lax.dynamic_slice_in_dim(padded_pixels, first_row + 1, HT + 2, 0)
        pre_act = spatial_conv(row_block, conv_weight, HT, NW)
        hidden = jax.nn.silu(pre_act).astype(jnp.bfloat16)
        mixed_time = temporal_conv(hidden, time_weight)
        return lax.optimization_barrier(jnp.mean(jax.nn.silu(mixed_time), axis=2)).astype(jnp.bfloat16)
    embedded = lax.map(forward_band, jnp.arange(N_ROW, dtype=jnp.int32)).reshape(NH * NW, C_OUT)
    parcel_of = parcel_index(pixel_slot, straddle_dir, straddle_slot).reshape(NH * NW)
    parcel_sums = jax.ops.segment_sum(embedded.astype(jnp.float32), parcel_of, num_segments=PARCELS)
    centered = parcel_sums - lax.optimization_barrier(jnp.mean(parcel_sums, axis=-1, keepdims=True))
    variance = lax.optimization_barrier(jnp.mean(centered * centered, axis=-1, keepdims=True))
    inverse = lax.rsqrt(variance + EPSILON)
    normed = centered * inverse
    rounded = normed.astype(jnp.bfloat16)
    logits = jnp.dot(rounded, class_weight, preferred_element_type=jnp.float32)
    exp_logits = jnp.exp(logits)
    probability = exp_logits / lax.optimization_barrier(jnp.sum(exp_logits, axis=-1, keepdims=True))
    label_hot = (labels.reshape(PARCELS)[:, None] == jnp.arange(CLASSES, dtype=jnp.int32)[None, :]).astype(jnp.float32)
    grad_logits = (probability - label_hot) / PARCELS
    class_grad = jnp.dot(rounded.astype(jnp.float32).T, grad_logits, precision=PRECISE)
    grad_normed = jnp.dot(grad_logits, class_weight.astype(jnp.float32).T, precision=PRECISE)
    parcel_grad = (inverse * (grad_normed - lax.optimization_barrier(jnp.mean(grad_normed, axis=-1, keepdims=True)) - normed * lax.optimization_barrier(jnp.mean(grad_normed * normed, axis=-1, keepdims=True)))).astype(jnp.bfloat16)
    pixel_grad = jnp.take(parcel_grad, parcel_of, axis=0).reshape(NH, NW, C_OUT)
    padded_grad = jnp.pad(pixel_grad, ((1, 1), (0, 0), (0, 0)))

    def backward_band(running, band_index):
        conv_acc, time_acc = running
        first_row = band_index * HT
        row_block = lax.dynamic_slice_in_dim(padded_pixels, first_row, HT + 4, 0)
        pre_act = spatial_conv(row_block, conv_weight, HT + 2, NW)
        hidden = jax.nn.silu(pre_act).astype(jnp.bfloat16)
        mixed_time = temporal_conv(hidden, time_weight)
        grad_rows = lax.dynamic_slice_in_dim(padded_grad, first_row, HT + 2, 0)
        grad_mixed = ((grad_rows.astype(jnp.float32) / DATES)[:, :, None, :] * silu_slope(mixed_time)).astype(jnp.bfloat16)
        grad_hidden = temporal_back(grad_mixed, time_weight)
        grad_pre = (grad_hidden * silu_slope(pre_act)).astype(jnp.bfloat16)
        time_acc = time_acc + temporal_weight_grad(hidden[1:HT + 1], grad_mixed[1:HT + 1])
        own_block = row_block[1:HT + 3].astype(jnp.float32)
        grad_own = grad_pre[1:HT + 1].astype(jnp.float32)
        conv_taps = jnp.stack([jnp.stack([jnp.einsum('ijtc,ijtd->cd', own_block[row_tap:row_tap + HT, col_tap:col_tap + NW], grad_own, precision=PRECISE) for col_tap in range(3)]) for row_tap in range(3)])
        conv_acc = conv_acc + conv_taps
        first_keep = jnp.where(band_index == 0, 0.0, 1.0).astype(jnp.float32)
        last_keep = jnp.where(band_index == N_ROW - 1, 0.0, 1.0).astype(jnp.float32)
        row_keep = jnp.concatenate([first_keep[None], jnp.ones((HT,), jnp.float32), last_keep[None]])
        grad_masked = grad_pre.astype(jnp.float32) * row_keep[:, None, None, None]
        grad_padded = jnp.pad(grad_masked, ((0, 0), (1, 1), (0, 0), (0, 0)))
        band_grad = jnp.zeros((HT, NW, DATES, C_IN), jnp.float32)
        for row_tap in range(3):
            for col_tap in range(3):
                band_grad = band_grad + jnp.einsum('ijtd,cd->ijtc', grad_padded[2 - row_tap:2 - row_tap + HT, 2 - col_tap:2 - col_tap + NW], conv_weight[row_tap, col_tap].astype(jnp.float32), precision=PRECISE)
        return ((conv_acc, time_acc), band_grad.astype(jnp.bfloat16))
    initial = (jnp.zeros((3, 3, C_IN, C_OUT), jnp.float32), jnp.zeros((3, GROUPS, CPG, CPG), jnp.float32))
    (conv_grad, time_grad), bands = lax.scan(backward_band, initial, jnp.arange(N_ROW, dtype=jnp.int32))
    input_grad = bands.reshape(NH, NW, DATES * C_IN)
    return (input_grad, conv_grad, time_grad, class_grad)
```

```python
import jax
import jax.numpy as jnp
from jax import lax
from jax.sharding import PartitionSpec as P

DATES = 12
C_IN = 64
C_OUT = 128
GROUPS = 16
CLASSES = 20
P_OWN = 32
S_STR = 32
CPG = 8


EPSILON = 1e-05
PRECISE = lax.Precision.HIGHEST


def with_halo(cells, sides, width):
    for axis, dim in sides:
        count = lax.axis_size(axis)
        ends = count - 1
        head = lax.slice_in_dim(cells, 0, width, axis=dim)
        tail = lax.slice_in_dim(cells, cells.shape[dim] - width, cells.shape[dim], axis=dim)
        cells = jnp.concatenate(
            [
                lax.ppermute(tail, axis, [(i, (i + 1) % count) for i in range(ends)]),
                cells,
                lax.ppermute(head, axis, [((i + 1) % count, i) for i in range(ends)]),
            ],
            axis=dim,
        )
    return cells


def butterfly_sum(flat):
    for axis in ("col", "row"):
        size = lax.axis_size(axis)
        bit = 1
        while bit < size:
            flat = flat + lax.ppermute(flat, axis, [(i, i ^ bit) for i in range(size)])
            bit *= 2
    return flat


def silu_slope(value):
    sig = jax.nn.sigmoid(value)
    return sig * (1.0 + value * (1.0 - sig))


def spatial_forward(padded, conv_weight, tile_rows, tile_cols):
    running_sum = None
    for row_tap in range(3):
        tap_patch = jnp.concatenate(
            [
                padded[row_tap : row_tap + tile_rows, col_tap : col_tap + tile_cols]
                for col_tap in range(3)
            ],
            axis=-1,
        )
        tap_term = jnp.dot(
            tap_patch,
            conv_weight[row_tap].reshape(3 * C_IN, C_OUT),
            preferred_element_type=jnp.float32,
        )
        running_sum = tap_term if running_sum is None else running_sum + tap_term
    return running_sum


def transposed_conv(padded_grad, conv_weight, out_rows, out_cols):
    input_sum = None
    for row_tap in range(3):
        grad_patch = jnp.concatenate(
            [
                padded_grad[
                    2 - row_tap : 2 - row_tap + out_rows, 2 - col_tap : 2 - col_tap + out_cols
                ]
                for col_tap in range(3)
            ],
            axis=-1,
        )
        flipped = jnp.concatenate([conv_weight[row_tap, col_tap].T for col_tap in range(3)], axis=0)
        tap_term = jnp.dot(grad_patch, flipped, preferred_element_type=jnp.float32)
        input_sum = tap_term if input_sum is None else input_sum + tap_term
    return input_sum


def block_weights(time_weight):
    group_eye = jnp.eye(GROUPS, dtype=jnp.bfloat16)
    return jnp.einsum("kgco,gh->kgcho", time_weight, group_eye).reshape(3, C_OUT, C_OUT)


def per_device(
    pixels, conv_weight, time_weight, class_weight, pixel_slot, straddle_dir, straddle_slot, labels
):
    tile_rows, tile_cols = (pixels.shape[0], pixels.shape[1])
    slot_count = P_OWN + S_STR
    padded_pixels = with_halo(pixels, (("row", 0), ("col", 1)), 1).reshape(
        tile_rows + 2, tile_cols + 2, DATES, C_IN
    )
    pre_act = spatial_forward(padded_pixels, conv_weight, tile_rows, tile_cols)
    hidden = jax.nn.silu(pre_act).astype(jnp.bfloat16)
    dense_time = block_weights(time_weight)
    padded_hidden = jnp.pad(hidden, ((0, 0), (0, 0), (1, 1), (0, 0)))
    mixed_time = None
    for time_tap in range(3):
        tap_term = jnp.dot(
            padded_hidden[:, :, time_tap : time_tap + DATES],
            dense_time[time_tap],
            preferred_element_type=jnp.float32,
        )
        mixed_time = tap_term if mixed_time is None else mixed_time + tap_term
    embedded = (
        jnp.mean(jax.nn.silu(mixed_time), axis=2)
        .astype(jnp.bfloat16)
        .reshape(tile_rows * tile_cols, C_OUT)
    )
    flat_slot = pixel_slot.reshape(tile_rows * tile_cols)
    membership = (jnp.arange(slot_count, dtype=jnp.int32)[:, None] == flat_slot[None, :]).astype(
        jnp.bfloat16
    )
    partial_value = jnp.dot(membership, embedded, preferred_element_type=jnp.float32)
    direction = straddle_dir.reshape(S_STR)
    owner_slot = straddle_slot.reshape(S_STR)
    own_slots = jnp.arange(P_OWN, dtype=jnp.int32)
    target = jnp.concatenate([4 * P_OWN + own_slots, direction * P_OWN + owner_slot])
    select = (jnp.arange(9 * P_OWN, dtype=jnp.int32)[:, None] == target[None, :]).astype(
        jnp.float32
    )
    outgoing = jnp.dot(select, partial_value, precision=PRECISE).reshape(3, 3, P_OWN, C_OUT)
    border = with_halo(outgoing.astype(jnp.bfloat16), (("row", 0), ("col", 1)), 1).astype(
        outgoing.dtype
    )
    parcel_sums = jnp.sum(border[0::2, 0::2], axis=(0, 1))
    centered = parcel_sums - jnp.mean(parcel_sums, axis=-1, keepdims=True)
    variance = jnp.mean(centered * centered, axis=-1, keepdims=True)
    inverse = lax.rsqrt(variance + EPSILON)
    normed = centered * inverse
    rounded = normed.astype(jnp.bfloat16)
    logits = jnp.dot(rounded, class_weight, preferred_element_type=jnp.float32)
    exp_logits = jnp.exp(logits)
    probability = exp_logits / jnp.sum(exp_logits, axis=-1, keepdims=True)
    label_hot = (
        labels.reshape(P_OWN)[:, None] == jnp.arange(CLASSES, dtype=jnp.int32)[None, :]
    ).astype(jnp.float32)
    parcel_total = P_OWN * lax.axis_size("row") * lax.axis_size("col")
    grad_logits = (probability - label_hot) / parcel_total
    class_term = jnp.dot(rounded.astype(jnp.float32).T, grad_logits, precision=PRECISE)
    grad_normed = jnp.dot(grad_logits, class_weight.astype(jnp.float32).T, precision=PRECISE)
    parcel_grad = (
        inverse
        * (
            grad_normed
            - jnp.mean(grad_normed, axis=-1, keepdims=True)
            - normed * jnp.mean(grad_normed * normed, axis=-1, keepdims=True)
        )
    ).astype(jnp.bfloat16)
    beside_all = with_halo(
        parcel_grad.reshape(1, 1, P_OWN, C_OUT), (("row", 0), ("col", 1)), 1
    ).reshape(9 * P_OWN, C_OUT)
    picker = (target[:, None] == jnp.arange(9 * P_OWN, dtype=jnp.int32)[None, :]).astype(
        jnp.bfloat16
    )
    slot_grad = jnp.dot(picker, beside_all, preferred_element_type=jnp.float32).astype(jnp.bfloat16)
    pixel_grad = jnp.dot(membership.T, slot_grad, preferred_element_type=jnp.float32).reshape(
        tile_rows, tile_cols, C_OUT
    )
    grad_mixed = ((pixel_grad / DATES)[:, :, None, :] * silu_slope(mixed_time)).astype(jnp.bfloat16)
    group_eye = jnp.eye(GROUPS, dtype=jnp.float32)
    time_taps = []
    for time_tap in range(3):
        dense_grad = jnp.einsum(
            "ijtc,ijtd->cd",
            padded_hidden[:, :, time_tap : time_tap + DATES],
            grad_mixed,
            preferred_element_type=jnp.float32,
        )
        reshaped = dense_grad.reshape(GROUPS, CPG, GROUPS, CPG)
        time_taps.append(jnp.einsum("gchd,gh->gcd", reshaped, group_eye, precision=PRECISE))
    time_term = jnp.stack(time_taps)
    padded_mixed = jnp.pad(grad_mixed, ((0, 0), (0, 0), (1, 1), (0, 0)))
    grad_hidden = None
    for time_tap in range(3):
        tap_term = jnp.dot(
            padded_mixed[:, :, 2 - time_tap : 2 - time_tap + DATES],
            dense_time[time_tap].T,
            preferred_element_type=jnp.float32,
        )
        grad_hidden = tap_term if grad_hidden is None else grad_hidden + tap_term
    grad_pre = (grad_hidden * silu_slope(pre_act)).astype(jnp.bfloat16)
    conv_rows = []
    for row_tap in range(3):
        tap_patch = jnp.concatenate(
            [
                padded_pixels[row_tap : row_tap + tile_rows, col_tap : col_tap + tile_cols]
                for col_tap in range(3)
            ],
            axis=-1,
        )
        conv_rows.append(
            jnp.einsum(
                "ijtc,ijtd->cd", tap_patch, grad_pre, preferred_element_type=jnp.float32
            ).reshape(3, C_IN, C_OUT)
        )
    conv_term = jnp.stack(conv_rows)
    padded_grad = with_halo(
        grad_pre.reshape(tile_rows, tile_cols, DATES * C_OUT), (("row", 0), ("col", 1)), 1
    ).reshape(tile_rows + 2, tile_cols + 2, DATES, C_OUT)
    input_sum = transposed_conv(padded_grad, conv_weight, tile_rows, tile_cols)
    input_grad = input_sum.astype(jnp.bfloat16).reshape(tile_rows, tile_cols, DATES * C_IN)
    flat = butterfly_sum(
        jnp.concatenate([conv_term.reshape(-1), time_term.reshape(-1), class_term.reshape(-1)])
    )
    conv_size, time_size = (conv_term.size, time_term.size)
    conv_grad = flat[:conv_size].reshape(conv_term.shape)
    time_grad = flat[conv_size : conv_size + time_size].reshape(time_term.shape)
    class_grad = flat[conv_size + time_size :].reshape(class_term.shape)
    return (input_grad, conv_grad, time_grad, class_grad)


def solution(mesh):
    in_specs = (
        P("row", "col", None),
        P(),
        P(),
        P(),
        P("row", "col"),
        P("row", "col", None),
        P("row", "col", None),
        P("row", "col", None),
    )
    out_specs = (P("row", "col", None), P(), P(), P())
    return jax.shard_map(
        per_device, mesh=mesh, in_specs=in_specs, out_specs=out_specs, check_vma=False
    )
```

```python
import jax
import jax.numpy as jnp
from jax import lax
from jax.sharding import PartitionSpec as P

DATES = 12
C_IN = 64
C_OUT = 128
GROUPS = 16
CLASSES = 20
P_OWN = 32
S_STR = 32
CPG = 8


EPSILON = 1e-05
PRECISE = lax.Precision.HIGHEST


def with_halo(cells, sides, width):
    for axis, dim in sides:
        count = lax.axis_size(axis)
        ends = count - 1
        head = lax.slice_in_dim(cells, 0, width, axis=dim)
        tail = lax.slice_in_dim(cells, cells.shape[dim] - width, cells.shape[dim], axis=dim)
        cells = jnp.concatenate(
            [
                lax.ppermute(tail, axis, [(i, (i + 1) % count) for i in range(ends)]),
                cells,
                lax.ppermute(head, axis, [((i + 1) % count, i) for i in range(ends)]),
            ],
            axis=dim,
        )
    return cells


def exchange(value, axis, bit):
    size = lax.axis_size(axis)
    return lax.ppermute(value, axis, [(i, i ^ bit) for i in range(size)])


def butterfly_sum(flat, halvings=2):
    steps = []
    for axis in ("col", "row"):
        bit = 1
        while bit < lax.axis_size(axis):
            steps.append((axis, bit))
            bit *= 2
    for axis, bit in steps[:halvings]:
        upper = (lax.axis_index(axis) // bit) % 2 == 1
        half = flat.shape[0] // 2
        low, high = flat[:half], flat[half:]
        keep = jnp.where(upper, high, low)
        flat = keep + exchange(jnp.where(upper, low, high), axis, bit)
    for axis, bit in steps[halvings:]:
        flat = flat + exchange(flat, axis, bit)
    for axis, bit in reversed(steps[:halvings]):
        upper = (lax.axis_index(axis) // bit) % 2 == 1
        other = exchange(flat, axis, bit)
        flat = jnp.where(upper, jnp.concatenate([other, flat]), jnp.concatenate([flat, other]))
    return flat


def silu_slope(value):
    sig = jax.nn.sigmoid(value)
    return sig * (1.0 + value * (1.0 - sig))


def spatial_forward(padded, conv_weight, tile_rows, tile_cols):
    running_sum = None
    for row_tap in range(3):
        tap_patch = jnp.concatenate(
            [
                padded[row_tap : row_tap + tile_rows, col_tap : col_tap + tile_cols]
                for col_tap in range(3)
            ],
            axis=-1,
        )
        tap_term = jnp.dot(
            tap_patch,
            conv_weight[row_tap].reshape(3 * C_IN, C_OUT),
            preferred_element_type=jnp.float32,
        )
        running_sum = tap_term if running_sum is None else running_sum + tap_term
    return running_sum


def transposed_conv(padded_grad, conv_weight, out_rows, out_cols):
    input_sum = None
    for row_tap in range(3):
        grad_patch = jnp.concatenate(
            [
                padded_grad[
                    2 - row_tap : 2 - row_tap + out_rows, 2 - col_tap : 2 - col_tap + out_cols
                ]
                for col_tap in range(3)
            ],
            axis=-1,
        )
        flipped = jnp.concatenate([conv_weight[row_tap, col_tap].T for col_tap in range(3)], axis=0)
        tap_term = jnp.dot(grad_patch, flipped, preferred_element_type=jnp.float32)
        input_sum = tap_term if input_sum is None else input_sum + tap_term
    return input_sum


def block_weights(time_weight):
    group_eye = jnp.eye(GROUPS, dtype=jnp.bfloat16)
    return jnp.einsum("kgco,gh->kgcho", time_weight, group_eye).reshape(3, C_OUT, C_OUT)


def per_device(
    pixels, conv_weight, time_weight, class_weight, pixel_slot, straddle_dir, straddle_slot, labels
):
    tile_rows, tile_cols = (pixels.shape[0], pixels.shape[1])
    slot_count = P_OWN + S_STR
    padded_pixels = with_halo(pixels, (("row", 0), ("col", 1)), 1).reshape(
        tile_rows + 2, tile_cols + 2, DATES, C_IN
    )
    pre_act = spatial_forward(padded_pixels, conv_weight, tile_rows, tile_cols)
    hidden = jax.nn.silu(pre_act).astype(jnp.bfloat16)
    dense_time = block_weights(time_weight)
    padded_hidden = jnp.pad(hidden, ((0, 0), (0, 0), (1, 1), (0, 0)))
    mixed_time = None
    for time_tap in range(3):
        tap_term = jnp.dot(
            padded_hidden[:, :, time_tap : time_tap + DATES],
            dense_time[time_tap],
            preferred_element_type=jnp.float32,
        )
        mixed_time = tap_term if mixed_time is None else mixed_time + tap_term
    embedded = (
        jnp.mean(jax.nn.silu(mixed_time), axis=2)
        .astype(jnp.bfloat16)
        .reshape(tile_rows * tile_cols, C_OUT)
    )
    flat_slot = pixel_slot.reshape(tile_rows * tile_cols)
    membership = (jnp.arange(slot_count, dtype=jnp.int32)[:, None] == flat_slot[None, :]).astype(
        jnp.bfloat16
    )
    partial_value = jnp.dot(membership, embedded, preferred_element_type=jnp.float32)
    direction = straddle_dir.reshape(S_STR)
    owner_slot = straddle_slot.reshape(S_STR)
    own_slots = jnp.arange(P_OWN, dtype=jnp.int32)
    target = jnp.concatenate([4 * P_OWN + own_slots, direction * P_OWN + owner_slot])
    select = (jnp.arange(9 * P_OWN, dtype=jnp.int32)[:, None] == target[None, :]).astype(
        jnp.float32
    )
    outgoing = jnp.dot(select, partial_value, precision=PRECISE).reshape(3, 3, P_OWN, C_OUT)
    border = with_halo(outgoing.astype(jnp.bfloat16), (("row", 0), ("col", 1)), 1).astype(
        outgoing.dtype
    )
    parcel_sums = jnp.sum(border[0::2, 0::2], axis=(0, 1))
    centered = parcel_sums - jnp.mean(parcel_sums, axis=-1, keepdims=True)
    variance = jnp.mean(centered * centered, axis=-1, keepdims=True)
    inverse = lax.rsqrt(variance + EPSILON)
    normed = centered * inverse
    rounded = normed.astype(jnp.bfloat16)
    logits = jnp.dot(rounded, class_weight, preferred_element_type=jnp.float32)
    exp_logits = jnp.exp(logits)
    probability = exp_logits / jnp.sum(exp_logits, axis=-1, keepdims=True)
    label_hot = (
        labels.reshape(P_OWN)[:, None] == jnp.arange(CLASSES, dtype=jnp.int32)[None, :]
    ).astype(jnp.float32)
    parcel_total = P_OWN * lax.axis_size("row") * lax.axis_size("col")
    grad_logits = (probability - label_hot) / parcel_total
    class_term = jnp.dot(rounded.astype(jnp.float32).T, grad_logits, precision=PRECISE)
    grad_normed = jnp.dot(grad_logits, class_weight.astype(jnp.float32).T, precision=PRECISE)
    parcel_grad = (
        inverse
        * (
            grad_normed
            - jnp.mean(grad_normed, axis=-1, keepdims=True)
            - normed * jnp.mean(grad_normed * normed, axis=-1, keepdims=True)
        )
    ).astype(jnp.bfloat16)
    beside_all = with_halo(
        parcel_grad.reshape(1, 1, P_OWN, C_OUT), (("row", 0), ("col", 1)), 1
    ).reshape(9 * P_OWN, C_OUT)
    picker = (target[:, None] == jnp.arange(9 * P_OWN, dtype=jnp.int32)[None, :]).astype(
        jnp.bfloat16
    )
    slot_grad = jnp.dot(picker, beside_all, preferred_element_type=jnp.float32).astype(jnp.bfloat16)
    pixel_grad = jnp.dot(membership.T, slot_grad, preferred_element_type=jnp.float32).reshape(
        tile_rows, tile_cols, C_OUT
    )
    grad_mixed = ((pixel_grad / DATES)[:, :, None, :] * silu_slope(mixed_time)).astype(jnp.bfloat16)
    group_eye = jnp.eye(GROUPS, dtype=jnp.float32)
    time_taps = []
    for time_tap in range(3):
        dense_grad = jnp.einsum(
            "ijtc,ijtd->cd",
            padded_hidden[:, :, time_tap : time_tap + DATES],
            grad_mixed,
            preferred_element_type=jnp.float32,
        )
        reshaped = dense_grad.reshape(GROUPS, CPG, GROUPS, CPG)
        time_taps.append(jnp.einsum("gchd,gh->gcd", reshaped, group_eye, precision=PRECISE))
    time_term = jnp.stack(time_taps)
    padded_mixed = jnp.pad(grad_mixed, ((0, 0), (0, 0), (1, 1), (0, 0)))
    grad_hidden = None
    for time_tap in range(3):
        tap_term = jnp.dot(
            padded_mixed[:, :, 2 - time_tap : 2 - time_tap + DATES],
            dense_time[time_tap].T,
            preferred_element_type=jnp.float32,
        )
        grad_hidden = tap_term if grad_hidden is None else grad_hidden + tap_term
    grad_pre = (grad_hidden * silu_slope(pre_act)).astype(jnp.bfloat16)
    conv_rows = []
    for row_tap in range(3):
        tap_patch = jnp.concatenate(
            [
                padded_pixels[row_tap : row_tap + tile_rows, col_tap : col_tap + tile_cols]
                for col_tap in range(3)
            ],
            axis=-1,
        )
        conv_rows.append(
            jnp.einsum(
                "ijtc,ijtd->cd", tap_patch, grad_pre, preferred_element_type=jnp.float32
            ).reshape(3, C_IN, C_OUT)
        )
    conv_term = jnp.stack(conv_rows)
    padded_grad = with_halo(
        grad_pre.reshape(tile_rows, tile_cols, DATES * C_OUT), (("row", 0), ("col", 1)), 1
    ).reshape(tile_rows + 2, tile_cols + 2, DATES, C_OUT)
    input_sum = transposed_conv(padded_grad, conv_weight, tile_rows, tile_cols)
    input_grad = input_sum.astype(jnp.bfloat16).reshape(tile_rows, tile_cols, DATES * C_IN)
    flat = butterfly_sum(
        jnp.concatenate([conv_term.reshape(-1), time_term.reshape(-1), class_term.reshape(-1)])
    )
    conv_size, time_size = (conv_term.size, time_term.size)
    conv_grad = flat[:conv_size].reshape(conv_term.shape)
    time_grad = flat[conv_size : conv_size + time_size].reshape(time_term.shape)
    class_grad = flat[conv_size + time_size :].reshape(class_term.shape)
    return (input_grad, conv_grad, time_grad, class_grad)


def solution(mesh):
    in_specs = (
        P("row", "col", None),
        P(),
        P(),
        P(),
        P("row", "col"),
        P("row", "col", None),
        P("row", "col", None),
        P("row", "col", None),
    )
    out_specs = (P("row", "col", None), P(), P(), P())
    return jax.shard_map(
        per_device, mesh=mesh, in_specs=in_specs, out_specs=out_specs, check_vma=False
    )
```

```python
import jax
import jax.numpy as jnp
from jax import lax
from jax.sharding import PartitionSpec as P

DATES = 12
C_IN = 64
C_OUT = 128
GROUPS = 16
CLASSES = 20
P_OWN = 32
S_STR = 32
CPG = 8


EPSILON = 1e-05
PRECISE = lax.Precision.HIGHEST


def with_halo(cells, sides, width):
    for axis, dim in sides:
        count = lax.axis_size(axis)
        odd = lax.axis_index(axis) % 2 == 1
        head = lax.slice_in_dim(cells, 0, width, axis=dim)
        tail = lax.slice_in_dim(cells, cells.shape[dim] - width, cells.shape[dim], axis=dim)
        inner = lax.ppermute(jnp.where(odd, head, tail), axis, [(i, i ^ 1) for i in range(count)])
        outer = lax.ppermute(
            jnp.where(odd, tail, head),
            axis,
            [pair for k in range(1, count - 1, 2) for pair in ((k, k + 1), (k + 1, k))],
        )
        cells = jnp.concatenate(
            [jnp.where(odd, inner, outer), cells, jnp.where(odd, outer, inner)], axis=dim
        )
    return cells


def exchange(value, axis, bit):
    size = lax.axis_size(axis)
    return lax.ppermute(value, axis, [(i, i ^ bit) for i in range(size)])


def butterfly_sum(flat, halvings=2):
    steps = []
    for axis in ("col", "row"):
        bit = 1
        while bit < lax.axis_size(axis):
            steps.append((axis, bit))
            bit *= 2
    for axis, bit in steps[:halvings]:
        upper = (lax.axis_index(axis) // bit) % 2 == 1
        half = flat.shape[0] // 2
        low, high = flat[:half], flat[half:]
        keep = jnp.where(upper, high, low)
        flat = keep + exchange(jnp.where(upper, low, high), axis, bit)
    for axis, bit in steps[halvings:]:
        flat = flat + exchange(flat, axis, bit)
    for axis, bit in reversed(steps[:halvings]):
        upper = (lax.axis_index(axis) // bit) % 2 == 1
        other = exchange(flat, axis, bit)
        flat = jnp.where(upper, jnp.concatenate([other, flat]), jnp.concatenate([flat, other]))
    return flat


def silu_slope(value):
    sig = jax.nn.sigmoid(value)
    return sig * (1.0 + value * (1.0 - sig))


def spatial_forward(padded, conv_weight, tile_rows, tile_cols):
    running_sum = None
    for row_tap in range(3):
        tap_patch = jnp.concatenate(
            [
                padded[row_tap : row_tap + tile_rows, col_tap : col_tap + tile_cols]
                for col_tap in range(3)
            ],
            axis=-1,
        )
        tap_term = jnp.dot(
            tap_patch,
            conv_weight[row_tap].reshape(3 * C_IN, C_OUT),
            preferred_element_type=jnp.float32,
        )
        running_sum = tap_term if running_sum is None else running_sum + tap_term
    return running_sum


def transposed_conv(padded_grad, conv_weight, out_rows, out_cols):
    input_sum = None
    for row_tap in range(3):
        grad_patch = jnp.concatenate(
            [
                padded_grad[
                    2 - row_tap : 2 - row_tap + out_rows, 2 - col_tap : 2 - col_tap + out_cols
                ]
                for col_tap in range(3)
            ],
            axis=-1,
        )
        flipped = jnp.concatenate([conv_weight[row_tap, col_tap].T for col_tap in range(3)], axis=0)
        tap_term = jnp.dot(grad_patch, flipped, preferred_element_type=jnp.float32)
        input_sum = tap_term if input_sum is None else input_sum + tap_term
    return input_sum


def block_weights(time_weight):
    group_eye = jnp.eye(GROUPS, dtype=jnp.bfloat16)
    return jnp.einsum("kgco,gh->kgcho", time_weight, group_eye).reshape(3, C_OUT, C_OUT)


def per_device(
    pixels, conv_weight, time_weight, class_weight, pixel_slot, straddle_dir, straddle_slot, labels
):
    tile_rows, tile_cols = (pixels.shape[0], pixels.shape[1])
    slot_count = P_OWN + S_STR
    padded_pixels = with_halo(pixels, (("row", 0), ("col", 1)), 1).reshape(
        tile_rows + 2, tile_cols + 2, DATES, C_IN
    )
    pre_act = spatial_forward(padded_pixels, conv_weight, tile_rows, tile_cols)
    hidden = jax.nn.silu(pre_act).astype(jnp.bfloat16)
    dense_time = block_weights(time_weight)
    padded_hidden = jnp.pad(hidden, ((0, 0), (0, 0), (1, 1), (0, 0)))
    mixed_time = None
    for time_tap in range(3):
        tap_term = jnp.dot(
            padded_hidden[:, :, time_tap : time_tap + DATES],
            dense_time[time_tap],
            preferred_element_type=jnp.float32,
        )
        mixed_time = tap_term if mixed_time is None else mixed_time + tap_term
    embedded = (
        jnp.mean(jax.nn.silu(mixed_time), axis=2)
        .astype(jnp.bfloat16)
        .reshape(tile_rows * tile_cols, C_OUT)
    )
    flat_slot = pixel_slot.reshape(tile_rows * tile_cols)
    membership = (jnp.arange(slot_count, dtype=jnp.int32)[:, None] == flat_slot[None, :]).astype(
        jnp.bfloat16
    )
    partial_value = jnp.dot(membership, embedded, preferred_element_type=jnp.float32)
    direction = straddle_dir.reshape(S_STR)
    owner_slot = straddle_slot.reshape(S_STR)
    own_slots = jnp.arange(P_OWN, dtype=jnp.int32)
    target = jnp.concatenate([4 * P_OWN + own_slots, direction * P_OWN + owner_slot])
    select = (jnp.arange(9 * P_OWN, dtype=jnp.int32)[:, None] == target[None, :]).astype(
        jnp.float32
    )
    outgoing = jnp.dot(select, partial_value, precision=PRECISE).reshape(3, 3, P_OWN, C_OUT)
    border = with_halo(outgoing.astype(jnp.bfloat16), (("row", 0), ("col", 1)), 1).astype(
        outgoing.dtype
    )
    parcel_sums = jnp.sum(border[0::2, 0::2], axis=(0, 1))
    centered = parcel_sums - jnp.mean(parcel_sums, axis=-1, keepdims=True)
    variance = jnp.mean(centered * centered, axis=-1, keepdims=True)
    inverse = lax.rsqrt(variance + EPSILON)
    normed = centered * inverse
    rounded = normed.astype(jnp.bfloat16)
    logits = jnp.dot(rounded, class_weight, preferred_element_type=jnp.float32)
    exp_logits = jnp.exp(logits)
    probability = exp_logits / jnp.sum(exp_logits, axis=-1, keepdims=True)
    label_hot = (
        labels.reshape(P_OWN)[:, None] == jnp.arange(CLASSES, dtype=jnp.int32)[None, :]
    ).astype(jnp.float32)
    parcel_total = P_OWN * lax.axis_size("row") * lax.axis_size("col")
    grad_logits = (probability - label_hot) / parcel_total
    class_term = jnp.dot(rounded.astype(jnp.float32).T, grad_logits, precision=PRECISE)
    grad_normed = jnp.dot(grad_logits, class_weight.astype(jnp.float32).T, precision=PRECISE)
    parcel_grad = (
        inverse
        * (
            grad_normed
            - jnp.mean(grad_normed, axis=-1, keepdims=True)
            - normed * jnp.mean(grad_normed * normed, axis=-1, keepdims=True)
        )
    ).astype(jnp.bfloat16)
    beside_all = with_halo(
        parcel_grad.reshape(1, 1, P_OWN, C_OUT), (("row", 0), ("col", 1)), 1
    ).reshape(9 * P_OWN, C_OUT)
    picker = (target[:, None] == jnp.arange(9 * P_OWN, dtype=jnp.int32)[None, :]).astype(
        jnp.bfloat16
    )
    slot_grad = jnp.dot(picker, beside_all, preferred_element_type=jnp.float32).astype(jnp.bfloat16)
    pixel_grad = jnp.dot(membership.T, slot_grad, preferred_element_type=jnp.float32).reshape(
        tile_rows, tile_cols, C_OUT
    )
    grad_mixed = ((pixel_grad / DATES)[:, :, None, :] * silu_slope(mixed_time)).astype(jnp.bfloat16)
    group_eye = jnp.eye(GROUPS, dtype=jnp.float32)
    time_taps = []
    for time_tap in range(3):
        dense_grad = jnp.einsum(
            "ijtc,ijtd->cd",
            padded_hidden[:, :, time_tap : time_tap + DATES],
            grad_mixed,
            preferred_element_type=jnp.float32,
        )
        reshaped = dense_grad.reshape(GROUPS, CPG, GROUPS, CPG)
        time_taps.append(jnp.einsum("gchd,gh->gcd", reshaped, group_eye, precision=PRECISE))
    time_term = jnp.stack(time_taps)
    padded_mixed = jnp.pad(grad_mixed, ((0, 0), (0, 0), (1, 1), (0, 0)))
    grad_hidden = None
    for time_tap in range(3):
        tap_term = jnp.dot(
            padded_mixed[:, :, 2 - time_tap : 2 - time_tap + DATES],
            dense_time[time_tap].T,
            preferred_element_type=jnp.float32,
        )
        grad_hidden = tap_term if grad_hidden is None else grad_hidden + tap_term
    grad_pre = (grad_hidden * silu_slope(pre_act)).astype(jnp.bfloat16)
    conv_rows = []
    for row_tap in range(3):
        tap_patch = jnp.concatenate(
            [
                padded_pixels[row_tap : row_tap + tile_rows, col_tap : col_tap + tile_cols]
                for col_tap in range(3)
            ],
            axis=-1,
        )
        conv_rows.append(
            jnp.einsum(
                "ijtc,ijtd->cd", tap_patch, grad_pre, preferred_element_type=jnp.float32
            ).reshape(3, C_IN, C_OUT)
        )
    conv_term = jnp.stack(conv_rows)
    padded_grad = with_halo(
        grad_pre.reshape(tile_rows, tile_cols, DATES * C_OUT), (("row", 0), ("col", 1)), 1
    ).reshape(tile_rows + 2, tile_cols + 2, DATES, C_OUT)
    input_sum = transposed_conv(padded_grad, conv_weight, tile_rows, tile_cols)
    input_grad = input_sum.astype(jnp.bfloat16).reshape(tile_rows, tile_cols, DATES * C_IN)
    flat = butterfly_sum(
        jnp.concatenate([conv_term.reshape(-1), time_term.reshape(-1), class_term.reshape(-1)])
    )
    conv_size, time_size = (conv_term.size, time_term.size)
    conv_grad = flat[:conv_size].reshape(conv_term.shape)
    time_grad = flat[conv_size : conv_size + time_size].reshape(time_term.shape)
    class_grad = flat[conv_size + time_size :].reshape(class_term.shape)
    return (input_grad, conv_grad, time_grad, class_grad)


def solution(mesh):
    in_specs = (
        P("row", "col", None),
        P(),
        P(),
        P(),
        P("row", "col"),
        P("row", "col", None),
        P("row", "col", None),
        P("row", "col", None),
    )
    out_specs = (P("row", "col", None), P(), P(), P())
    return jax.shard_map(
        per_device, mesh=mesh, in_specs=in_specs, out_specs=out_specs, check_vma=False
    )
```

```python
import jax
import jax.numpy as jnp
from jax import lax
from jax.sharding import PartitionSpec as P

DATES = 12
C_IN = 64
C_OUT = 128
GROUPS = 16
CLASSES = 20
P_OWN = 32
S_STR = 32
CPG = 8


EPSILON = 1e-05
PRECISE = lax.Precision.HIGHEST


def with_halo(cells, sides, width):
    for axis, dim in sides:
        count = lax.axis_size(axis)
        odd = lax.axis_index(axis) % 2 == 1
        head = lax.slice_in_dim(cells, 0, width, axis=dim)
        tail = lax.slice_in_dim(cells, cells.shape[dim] - width, cells.shape[dim], axis=dim)
        inner = lax.ppermute(jnp.where(odd, head, tail), axis, [(i, i ^ 1) for i in range(count)])
        outer = lax.ppermute(
            jnp.where(odd, tail, head),
            axis,
            [pair for k in range(1, count - 1, 2) for pair in ((k, k + 1), (k + 1, k))],
        )
        cells = jnp.concatenate(
            [jnp.where(odd, inner, outer), cells, jnp.where(odd, outer, inner)], axis=dim
        )
    return cells


def exchange(value, axis, bit):
    size = lax.axis_size(axis)
    return lax.ppermute(value, axis, [(i, i ^ bit) for i in range(size)])


def swap_with(value, axis, bit, extra):
    size = value.shape[0]
    both = exchange(jnp.concatenate([value, extra.astype(value.dtype).reshape(-1)]), axis, bit)
    return both[:size], both[size:].reshape(extra.shape).astype(extra.dtype)


def halo_ends(cells, axis, dim):
    odd = lax.axis_index(axis) % 2 == 1
    head = lax.slice_in_dim(cells, 0, 1, axis=dim)
    tail = lax.slice_in_dim(cells, cells.shape[dim] - 1, cells.shape[dim], axis=dim)
    return odd, jnp.where(odd, head, tail), jnp.where(odd, tail, head)


def outer_swap(piece, axis):
    count = lax.axis_size(axis)
    return lax.ppermute(
        piece, axis, [pair for k in range(1, count - 1, 2) for pair in ((k, k + 1), (k + 1, k))]
    )


def halo_join(cells, odd, inner, outer, dim):
    return jnp.concatenate(
        [jnp.where(odd, inner, outer), cells, jnp.where(odd, outer, inner)], axis=dim
    )


def butterfly_sum(flat, cells, halvings=2):
    steps = []
    for axis in ("col", "row"):
        bit = 1
        while bit < lax.axis_size(axis):
            steps.append((axis, bit))
            bit *= 2
    for axis, bit in steps[:halvings]:
        upper = (lax.axis_index(axis) // bit) % 2 == 1
        half = flat.shape[0] // 2
        low, high = flat[:half], flat[half:]
        keep = jnp.where(upper, high, low)
        give = jnp.where(upper, low, high)
        if (axis, bit) == ("col", 1):
            odd, inner_piece, outer_piece = halo_ends(cells, "col", 1)
            outer = outer_swap(outer_piece, "col")
            got, inner = swap_with(give, axis, bit, inner_piece)
            cells = halo_join(cells, odd, inner, outer, 1)
        else:
            got = exchange(give, axis, bit)
        flat = keep + got
    for axis, bit in steps[halvings:]:
        if (axis, bit) == ("row", 1):
            odd, inner_piece, outer_piece = halo_ends(cells, "row", 0)
            outer = outer_swap(outer_piece, "row")
            got, inner = swap_with(flat, axis, bit, inner_piece)
            cells = halo_join(cells, odd, inner, outer, 0)
        else:
            got = exchange(flat, axis, bit)
        flat = flat + got
    for axis, bit in reversed(steps[:halvings]):
        upper = (lax.axis_index(axis) // bit) % 2 == 1
        other = exchange(flat, axis, bit)
        flat = jnp.where(upper, jnp.concatenate([other, flat]), jnp.concatenate([flat, other]))
    return flat, cells


def silu_slope(value):
    sig = jax.nn.sigmoid(value)
    return sig * (1.0 + value * (1.0 - sig))


def spatial_forward(padded, conv_weight, tile_rows, tile_cols):
    running_sum = None
    for row_tap in range(3):
        tap_patch = jnp.concatenate(
            [
                padded[row_tap : row_tap + tile_rows, col_tap : col_tap + tile_cols]
                for col_tap in range(3)
            ],
            axis=-1,
        )
        tap_term = jnp.dot(
            tap_patch,
            conv_weight[row_tap].reshape(3 * C_IN, C_OUT),
            preferred_element_type=jnp.float32,
        )
        running_sum = tap_term if running_sum is None else running_sum + tap_term
    return running_sum


def transposed_conv(padded_grad, conv_weight, out_rows, out_cols):
    input_sum = None
    for row_tap in range(3):
        grad_patch = jnp.concatenate(
            [
                padded_grad[
                    2 - row_tap : 2 - row_tap + out_rows, 2 - col_tap : 2 - col_tap + out_cols
                ]
                for col_tap in range(3)
            ],
            axis=-1,
        )
        flipped = jnp.concatenate([conv_weight[row_tap, col_tap].T for col_tap in range(3)], axis=0)
        tap_term = jnp.dot(grad_patch, flipped, preferred_element_type=jnp.float32)
        input_sum = tap_term if input_sum is None else input_sum + tap_term
    return input_sum


def block_weights(time_weight):
    group_eye = jnp.eye(GROUPS, dtype=jnp.bfloat16)
    return jnp.einsum("kgco,gh->kgcho", time_weight, group_eye).reshape(3, C_OUT, C_OUT)


def per_device(
    pixels, conv_weight, time_weight, class_weight, pixel_slot, straddle_dir, straddle_slot, labels
):
    tile_rows, tile_cols = (pixels.shape[0], pixels.shape[1])
    slot_count = P_OWN + S_STR
    padded_pixels = with_halo(pixels, (("row", 0), ("col", 1)), 1).reshape(
        tile_rows + 2, tile_cols + 2, DATES, C_IN
    )
    pre_act = spatial_forward(padded_pixels, conv_weight, tile_rows, tile_cols)
    hidden = jax.nn.silu(pre_act).astype(jnp.bfloat16)
    dense_time = block_weights(time_weight)
    padded_hidden = jnp.pad(hidden, ((0, 0), (0, 0), (1, 1), (0, 0)))
    mixed_time = None
    for time_tap in range(3):
        tap_term = jnp.dot(
            padded_hidden[:, :, time_tap : time_tap + DATES],
            dense_time[time_tap],
            preferred_element_type=jnp.float32,
        )
        mixed_time = tap_term if mixed_time is None else mixed_time + tap_term
    embedded = (
        jnp.mean(jax.nn.silu(mixed_time), axis=2)
        .astype(jnp.bfloat16)
        .reshape(tile_rows * tile_cols, C_OUT)
    )
    flat_slot = pixel_slot.reshape(tile_rows * tile_cols)
    membership = (jnp.arange(slot_count, dtype=jnp.int32)[:, None] == flat_slot[None, :]).astype(
        jnp.bfloat16
    )
    partial_value = jnp.dot(membership, embedded, preferred_element_type=jnp.float32)
    direction = straddle_dir.reshape(S_STR)
    owner_slot = straddle_slot.reshape(S_STR)
    own_slots = jnp.arange(P_OWN, dtype=jnp.int32)
    target = jnp.concatenate([4 * P_OWN + own_slots, direction * P_OWN + owner_slot])
    select = (jnp.arange(9 * P_OWN, dtype=jnp.int32)[:, None] == target[None, :]).astype(
        jnp.float32
    )
    outgoing = jnp.dot(select, partial_value, precision=PRECISE).reshape(3, 3, P_OWN, C_OUT)
    border = with_halo(outgoing.astype(jnp.bfloat16), (("row", 0), ("col", 1)), 1).astype(
        outgoing.dtype
    )
    parcel_sums = jnp.sum(border[0::2, 0::2], axis=(0, 1))
    centered = parcel_sums - jnp.mean(parcel_sums, axis=-1, keepdims=True)
    variance = jnp.mean(centered * centered, axis=-1, keepdims=True)
    inverse = lax.rsqrt(variance + EPSILON)
    normed = centered * inverse
    rounded = normed.astype(jnp.bfloat16)
    logits = jnp.dot(rounded, class_weight, preferred_element_type=jnp.float32)
    exp_logits = jnp.exp(logits)
    probability = exp_logits / jnp.sum(exp_logits, axis=-1, keepdims=True)
    label_hot = (
        labels.reshape(P_OWN)[:, None] == jnp.arange(CLASSES, dtype=jnp.int32)[None, :]
    ).astype(jnp.float32)
    parcel_total = P_OWN * lax.axis_size("row") * lax.axis_size("col")
    grad_logits = (probability - label_hot) / parcel_total
    class_term = jnp.dot(rounded.astype(jnp.float32).T, grad_logits, precision=PRECISE)
    grad_normed = jnp.dot(grad_logits, class_weight.astype(jnp.float32).T, precision=PRECISE)
    parcel_grad = (
        inverse
        * (
            grad_normed
            - jnp.mean(grad_normed, axis=-1, keepdims=True)
            - normed * jnp.mean(grad_normed * normed, axis=-1, keepdims=True)
        )
    ).astype(jnp.bfloat16)
    beside_all = with_halo(
        parcel_grad.reshape(1, 1, P_OWN, C_OUT), (("row", 0), ("col", 1)), 1
    ).reshape(9 * P_OWN, C_OUT)
    picker = (target[:, None] == jnp.arange(9 * P_OWN, dtype=jnp.int32)[None, :]).astype(
        jnp.bfloat16
    )
    slot_grad = jnp.dot(picker, beside_all, preferred_element_type=jnp.float32).astype(jnp.bfloat16)
    pixel_grad = jnp.dot(membership.T, slot_grad, preferred_element_type=jnp.float32).reshape(
        tile_rows, tile_cols, C_OUT
    )
    grad_mixed = ((pixel_grad / DATES)[:, :, None, :] * silu_slope(mixed_time)).astype(jnp.bfloat16)
    group_eye = jnp.eye(GROUPS, dtype=jnp.float32)
    time_taps = []
    for time_tap in range(3):
        dense_grad = jnp.einsum(
            "ijtc,ijtd->cd",
            padded_hidden[:, :, time_tap : time_tap + DATES],
            grad_mixed,
            preferred_element_type=jnp.float32,
        )
        reshaped = dense_grad.reshape(GROUPS, CPG, GROUPS, CPG)
        time_taps.append(jnp.einsum("gchd,gh->gcd", reshaped, group_eye, precision=PRECISE))
    time_term = jnp.stack(time_taps)
    padded_mixed = jnp.pad(grad_mixed, ((0, 0), (0, 0), (1, 1), (0, 0)))
    grad_hidden = None
    for time_tap in range(3):
        tap_term = jnp.dot(
            padded_mixed[:, :, 2 - time_tap : 2 - time_tap + DATES],
            dense_time[time_tap].T,
            preferred_element_type=jnp.float32,
        )
        grad_hidden = tap_term if grad_hidden is None else grad_hidden + tap_term
    grad_pre = (grad_hidden * silu_slope(pre_act)).astype(jnp.bfloat16)
    conv_rows = []
    for row_tap in range(3):
        tap_patch = jnp.concatenate(
            [
                padded_pixels[row_tap : row_tap + tile_rows, col_tap : col_tap + tile_cols]
                for col_tap in range(3)
            ],
            axis=-1,
        )
        conv_rows.append(
            jnp.einsum(
                "ijtc,ijtd->cd", tap_patch, grad_pre, preferred_element_type=jnp.float32
            ).reshape(3, C_IN, C_OUT)
        )
    conv_term = jnp.stack(conv_rows)
    flat, padded_grad = butterfly_sum(
        jnp.concatenate([conv_term.reshape(-1), time_term.reshape(-1), class_term.reshape(-1)]),
        grad_pre.reshape(tile_rows, tile_cols, DATES * C_OUT),
    )
    padded_grad = padded_grad.reshape(tile_rows + 2, tile_cols + 2, DATES, C_OUT)
    input_sum = transposed_conv(padded_grad, conv_weight, tile_rows, tile_cols)
    input_grad = input_sum.astype(jnp.bfloat16).reshape(tile_rows, tile_cols, DATES * C_IN)
    conv_size, time_size = (conv_term.size, time_term.size)
    conv_grad = flat[:conv_size].reshape(conv_term.shape)
    time_grad = flat[conv_size : conv_size + time_size].reshape(time_term.shape)
    class_grad = flat[conv_size + time_size :].reshape(class_term.shape)
    return (input_grad, conv_grad, time_grad, class_grad)


def solution(mesh):
    in_specs = (
        P("row", "col", None),
        P(),
        P(),
        P(),
        P("row", "col"),
        P("row", "col", None),
        P("row", "col", None),
        P("row", "col", None),
    )
    out_specs = (P("row", "col", None), P(), P(), P())
    return jax.shard_map(
        per_device, mesh=mesh, in_specs=in_specs, out_specs=out_specs, check_vma=False
    )
```

```python
import jax
import jax.numpy as jnp
from jax import lax
from jax.sharding import PartitionSpec as P

DATES = 12
C_IN = 64
C_OUT = 128
GROUPS = 16
CLASSES = 20
P_OWN = 32
S_STR = 32
CPG = 8


EPSILON = 1e-05
PRECISE = lax.Precision.HIGHEST


def with_halo(cells, sides, width, extra=None):
    for axis, dim in sides:
        count = lax.axis_size(axis)
        odd = lax.axis_index(axis) % 2 == 1
        head = lax.slice_in_dim(cells, 0, width, axis=dim)
        tail = lax.slice_in_dim(cells, cells.shape[dim] - width, cells.shape[dim], axis=dim)
        first, second = (jnp.where(odd, head, tail), jnp.where(odd, tail, head))
        if extra is not None:
            size = first.size
            tag = extra.astype(cells.dtype).reshape(-1)
            first = jnp.concatenate([first.reshape(-1), tag])
            second = jnp.concatenate([second.reshape(-1), tag])
        inner = lax.ppermute(first, axis, [(i, i ^ 1) for i in range(count)])
        outer = lax.ppermute(
            second,
            axis,
            [pair for k in range(1, count - 1, 2) for pair in ((k, k + 1), (k + 1, k))],
        )
        if extra is not None:
            piece_shape = head.shape
            inner_tag = inner[size:].reshape(extra.shape).astype(extra.dtype)
            outer_tag = outer[size:].reshape(extra.shape).astype(extra.dtype)
            inner, outer = (inner[:size].reshape(piece_shape), outer[:size].reshape(piece_shape))
            extra = jnp.concatenate(
                [jnp.where(odd, inner_tag, outer_tag), extra, jnp.where(odd, outer_tag, inner_tag)],
                axis=dim,
            )
        cells = jnp.concatenate(
            [jnp.where(odd, inner, outer), cells, jnp.where(odd, outer, inner)], axis=dim
        )
    return cells if extra is None else (cells, extra)


def matching(count, dist, first):
    return [
        pair
        for r in range(count)
        if (r // dist) % 2 == first and r + dist < count
        for pair in ((r, r + dist), (r + dist, r))
    ]


def owner_sums(grid, axis, dim):
    count = lax.axis_size(axis)
    place = lax.axis_index(axis)
    take = lambda lo, hi: lax.slice_in_dim(grid, lo, hi, axis=dim)
    near, far = [], []
    for dist, pieces, into in ((1, (take(1, 3), take(0, 2)), near), (2, (take(2, 3), take(0, 1)), far)):
        for first in (0, 1):
            below = (place // dist) % 2 == first
            got = lax.ppermute(jnp.where(below, *pieces), axis, matching(count, dist, first))
            into.append((below, got))
    (below_a, got_a), (_, got_b) = near
    from_below = jnp.where(below_a, got_a, got_b)
    from_above = jnp.where(below_a, got_b, got_a)
    (below_c, got_c), (_, got_d) = far
    from_below2 = jnp.where(below_c, got_c, got_d)
    from_above2 = jnp.where(below_c, got_d, got_c)
    one = lambda part, k: lax.slice_in_dim(part, k, k + 1, axis=dim)
    return jnp.concatenate(
        [
            take(0, 1) + one(from_above, 0) + from_above2,
            take(1, 2) + one(from_above, 1) + one(from_below, 0),
            take(2, 3) + one(from_below, 1) + from_below2,
        ],
        axis=dim,
    )


def exchange(value, axis, bit):
    size = lax.axis_size(axis)
    return lax.ppermute(value, axis, [(i, i ^ bit) for i in range(size)])


def swap_with(value, axis, bit, extra):
    size = value.shape[0]
    both = exchange(jnp.concatenate([value, extra.astype(value.dtype).reshape(-1)]), axis, bit)
    return both[:size], both[size:].reshape(extra.shape).astype(extra.dtype)


def halo_ends(cells, axis, dim):
    odd = lax.axis_index(axis) % 2 == 1
    head = lax.slice_in_dim(cells, 0, 1, axis=dim)
    tail = lax.slice_in_dim(cells, cells.shape[dim] - 1, cells.shape[dim], axis=dim)
    return odd, jnp.where(odd, head, tail), jnp.where(odd, tail, head)


def outer_swap(piece, axis):
    count = lax.axis_size(axis)
    return lax.ppermute(
        piece, axis, [pair for k in range(1, count - 1, 2) for pair in ((k, k + 1), (k + 1, k))]
    )


def halo_join(cells, odd, inner, outer, dim):
    return jnp.concatenate(
        [jnp.where(odd, inner, outer), cells, jnp.where(odd, outer, inner)], axis=dim
    )


def butterfly_sum(flat, cells, halvings=2):
    steps = []
    for axis in ("col", "row"):
        bit = 1
        while bit < lax.axis_size(axis):
            steps.append((axis, bit))
            bit *= 2
    for axis, bit in steps[:halvings]:
        upper = (lax.axis_index(axis) // bit) % 2 == 1
        half = flat.shape[0] // 2
        low, high = flat[:half], flat[half:]
        keep = jnp.where(upper, high, low)
        give = jnp.where(upper, low, high)
        if (axis, bit) == ("col", 1):
            odd, inner_piece, outer_piece = halo_ends(cells, "col", 1)
            outer = outer_swap(outer_piece, "col")
            got, inner = swap_with(give, axis, bit, inner_piece)
            cells = halo_join(cells, odd, inner, outer, 1)
        else:
            got = exchange(give, axis, bit)
        flat = keep + got
    for axis, bit in steps[halvings:]:
        if (axis, bit) == ("row", 1):
            odd, inner_piece, outer_piece = halo_ends(cells, "row", 0)
            outer = outer_swap(outer_piece, "row")
            got, inner = swap_with(flat, axis, bit, inner_piece)
            cells = halo_join(cells, odd, inner, outer, 0)
        else:
            got = exchange(flat, axis, bit)
        flat = flat + got
    for axis, bit in reversed(steps[:halvings]):
        upper = (lax.axis_index(axis) // bit) % 2 == 1
        other = exchange(flat, axis, bit)
        flat = jnp.where(upper, jnp.concatenate([other, flat]), jnp.concatenate([flat, other]))
    return flat, cells


def silu_slope(value):
    sig = jax.nn.sigmoid(value)
    return sig * (1.0 + value * (1.0 - sig))


def spatial_forward(padded, conv_weight, tile_rows, tile_cols):
    running_sum = None
    for row_tap in range(3):
        tap_patch = jnp.concatenate(
            [
                padded[row_tap : row_tap + tile_rows, col_tap : col_tap + tile_cols]
                for col_tap in range(3)
            ],
            axis=-1,
        )
        tap_term = jnp.dot(
            tap_patch,
            conv_weight[row_tap].reshape(3 * C_IN, C_OUT),
            preferred_element_type=jnp.float32,
        )
        running_sum = tap_term if running_sum is None else running_sum + tap_term
    return running_sum


def transposed_conv(padded_grad, conv_weight, out_rows, out_cols):
    input_sum = None
    for row_tap in range(3):
        grad_patch = jnp.concatenate(
            [
                padded_grad[
                    2 - row_tap : 2 - row_tap + out_rows, 2 - col_tap : 2 - col_tap + out_cols
                ]
                for col_tap in range(3)
            ],
            axis=-1,
        )
        flipped = jnp.concatenate([conv_weight[row_tap, col_tap].T for col_tap in range(3)], axis=0)
        tap_term = jnp.dot(grad_patch, flipped, preferred_element_type=jnp.float32)
        input_sum = tap_term if input_sum is None else input_sum + tap_term
    return input_sum


def block_weights(time_weight):
    group_eye = jnp.eye(GROUPS, dtype=jnp.bfloat16)
    return jnp.einsum("kgco,gh->kgcho", time_weight, group_eye).reshape(3, C_OUT, C_OUT)


def per_device(
    pixels, conv_weight, time_weight, class_weight, pixel_slot, straddle_dir, straddle_slot, labels
):
    tile_rows, tile_cols = (pixels.shape[0], pixels.shape[1])
    slot_count = P_OWN + S_STR
    padded_pixels, label_grid = with_halo(
        pixels, (("row", 0), ("col", 1)), 1, extra=labels.reshape(1, 1, P_OWN)
    )
    padded_pixels = padded_pixels.reshape(tile_rows + 2, tile_cols + 2, DATES, C_IN)
    pre_act = spatial_forward(padded_pixels, conv_weight, tile_rows, tile_cols)
    hidden = jax.nn.silu(pre_act).astype(jnp.bfloat16)
    dense_time = block_weights(time_weight)
    padded_hidden = jnp.pad(hidden, ((0, 0), (0, 0), (1, 1), (0, 0)))
    mixed_time = None
    for time_tap in range(3):
        tap_term = jnp.dot(
            padded_hidden[:, :, time_tap : time_tap + DATES],
            dense_time[time_tap],
            preferred_element_type=jnp.float32,
        )
        mixed_time = tap_term if mixed_time is None else mixed_time + tap_term
    embedded = (
        jnp.mean(jax.nn.silu(mixed_time), axis=2)
        .astype(jnp.bfloat16)
        .reshape(tile_rows * tile_cols, C_OUT)
    )
    flat_slot = pixel_slot.reshape(tile_rows * tile_cols)
    membership = (jnp.arange(slot_count, dtype=jnp.int32)[:, None] == flat_slot[None, :]).astype(
        jnp.bfloat16
    )
    partial_value = jnp.dot(membership, embedded, preferred_element_type=jnp.float32)
    direction = straddle_dir.reshape(S_STR)
    owner_slot = straddle_slot.reshape(S_STR)
    own_slots = jnp.arange(P_OWN, dtype=jnp.int32)
    target = jnp.concatenate([4 * P_OWN + own_slots, direction * P_OWN + owner_slot])
    select = (jnp.arange(9 * P_OWN, dtype=jnp.int32)[:, None] == target[None, :]).astype(
        jnp.float32
    )
    outgoing = jnp.dot(select, partial_value, precision=PRECISE).reshape(3, 3, P_OWN, C_OUT)
    parcel_sums = owner_sums(owner_sums(outgoing, "row", 0), "col", 1).reshape(9 * P_OWN, C_OUT)
    centered = parcel_sums - jnp.mean(parcel_sums, axis=-1, keepdims=True)
    variance = jnp.mean(centered * centered, axis=-1, keepdims=True)
    inverse = lax.rsqrt(variance + EPSILON)
    normed = centered * inverse
    rounded = normed.astype(jnp.bfloat16)
    logits = jnp.dot(rounded, class_weight, preferred_element_type=jnp.float32)
    exp_logits = jnp.exp(logits)
    probability = exp_logits / jnp.sum(exp_logits, axis=-1, keepdims=True)
    label_hot = (
        label_grid.reshape(9 * P_OWN)[:, None] == jnp.arange(CLASSES, dtype=jnp.int32)[None, :]
    ).astype(jnp.float32)
    parcel_total = P_OWN * lax.axis_size("row") * lax.axis_size("col")
    grad_logits = (probability - label_hot) / parcel_total
    own = slice(4 * P_OWN, 5 * P_OWN)
    class_term = jnp.dot(
        rounded[own].astype(jnp.float32).T, grad_logits[own], precision=PRECISE
    )
    grad_normed = jnp.dot(grad_logits, class_weight.astype(jnp.float32).T, precision=PRECISE)
    beside_all = (
        inverse
        * (
            grad_normed
            - jnp.mean(grad_normed, axis=-1, keepdims=True)
            - normed * jnp.mean(grad_normed * normed, axis=-1, keepdims=True)
        )
    ).astype(jnp.bfloat16)
    picker = (target[:, None] == jnp.arange(9 * P_OWN, dtype=jnp.int32)[None, :]).astype(
        jnp.bfloat16
    )
    slot_grad = jnp.dot(picker, beside_all, preferred_element_type=jnp.float32).astype(jnp.bfloat16)
    pixel_grad = jnp.dot(membership.T, slot_grad, preferred_element_type=jnp.float32).reshape(
        tile_rows, tile_cols, C_OUT
    )
    grad_mixed = ((pixel_grad / DATES)[:, :, None, :] * silu_slope(mixed_time)).astype(jnp.bfloat16)
    group_eye = jnp.eye(GROUPS, dtype=jnp.float32)
    time_taps = []
    for time_tap in range(3):
        dense_grad = jnp.einsum(
            "ijtc,ijtd->cd",
            padded_hidden[:, :, time_tap : time_tap + DATES],
            grad_mixed,
            preferred_element_type=jnp.float32,
        )
        reshaped = dense_grad.reshape(GROUPS, CPG, GROUPS, CPG)
        time_taps.append(jnp.einsum("gchd,gh->gcd", reshaped, group_eye, precision=PRECISE))
    time_term = jnp.stack(time_taps)
    padded_mixed = jnp.pad(grad_mixed, ((0, 0), (0, 0), (1, 1), (0, 0)))
    grad_hidden = None
    for time_tap in range(3):
        tap_term = jnp.dot(
            padded_mixed[:, :, 2 - time_tap : 2 - time_tap + DATES],
            dense_time[time_tap].T,
            preferred_element_type=jnp.float32,
        )
        grad_hidden = tap_term if grad_hidden is None else grad_hidden + tap_term
    grad_pre = (grad_hidden * silu_slope(pre_act)).astype(jnp.bfloat16)
    conv_rows = []
    for row_tap in range(3):
        tap_patch = jnp.concatenate(
            [
                padded_pixels[row_tap : row_tap + tile_rows, col_tap : col_tap + tile_cols]
                for col_tap in range(3)
            ],
            axis=-1,
        )
        conv_rows.append(
            jnp.einsum(
                "ijtc,ijtd->cd", tap_patch, grad_pre, preferred_element_type=jnp.float32
            ).reshape(3, C_IN, C_OUT)
        )
    conv_term = jnp.stack(conv_rows)
    flat, padded_grad = butterfly_sum(
        jnp.concatenate([conv_term.reshape(-1), time_term.reshape(-1), class_term.reshape(-1)]),
        grad_pre.reshape(tile_rows, tile_cols, DATES * C_OUT),
    )
    padded_grad = padded_grad.reshape(tile_rows + 2, tile_cols + 2, DATES, C_OUT)
    input_sum = transposed_conv(padded_grad, conv_weight, tile_rows, tile_cols)
    input_grad = input_sum.astype(jnp.bfloat16).reshape(tile_rows, tile_cols, DATES * C_IN)
    conv_size, time_size = (conv_term.size, time_term.size)
    conv_grad = flat[:conv_size].reshape(conv_term.shape)
    time_grad = flat[conv_size : conv_size + time_size].reshape(time_term.shape)
    class_grad = flat[conv_size + time_size :].reshape(class_term.shape)
    return (input_grad, conv_grad, time_grad, class_grad)


def solution(mesh):
    in_specs = (
        P("row", "col", None),
        P(),
        P(),
        P(),
        P("row", "col"),
        P("row", "col", None),
        P("row", "col", None),
        P("row", "col", None),
    )
    out_specs = (P("row", "col", None), P(), P(), P())
    return jax.shard_map(
        per_device, mesh=mesh, in_specs=in_specs, out_specs=out_specs, check_vma=False
    )
```

```python
import jax
import jax.numpy as jnp
from jax import lax
from jax.sharding import PartitionSpec as P

DATES = 12
C_IN = 64
C_OUT = 128
GROUPS = 16
CLASSES = 20
P_OWN = 32
S_STR = 32
CPG = 8


EPSILON = 1e-05
PRECISE = lax.Precision.HIGHEST


def with_halo(cells, sides, width):
    for axis, dim in sides:
        count = lax.axis_size(axis)
        odd = lax.axis_index(axis) % 2 == 1
        head = lax.slice_in_dim(cells, 0, width, axis=dim)
        tail = lax.slice_in_dim(cells, cells.shape[dim] - width, cells.shape[dim], axis=dim)
        inner = lax.ppermute(jnp.where(odd, head, tail), axis, [(i, i ^ 1) for i in range(count)])
        outer = lax.ppermute(
            jnp.where(odd, tail, head),
            axis,
            [pair for k in range(1, count - 1, 2) for pair in ((k, k + 1), (k + 1, k))],
        )
        cells = jnp.concatenate(
            [jnp.where(odd, inner, outer), cells, jnp.where(odd, outer, inner)], axis=dim
        )
    return cells


def exchange(value, axis, bit):
    size = lax.axis_size(axis)
    return lax.ppermute(value, axis, [(i, i ^ bit) for i in range(size)])


def swap_with(value, axis, bit, extra):
    size = value.shape[0]
    both = exchange(jnp.concatenate([value, extra.astype(value.dtype).reshape(-1)]), axis, bit)
    return both[:size], both[size:].reshape(extra.shape).astype(extra.dtype)


def halo_ends(cells, axis, dim):
    odd = lax.axis_index(axis) % 2 == 1
    head = lax.slice_in_dim(cells, 0, 1, axis=dim)
    tail = lax.slice_in_dim(cells, cells.shape[dim] - 1, cells.shape[dim], axis=dim)
    return odd, jnp.where(odd, head, tail), jnp.where(odd, tail, head)


def outer_swap(piece, axis):
    count = lax.axis_size(axis)
    return lax.ppermute(
        piece, axis, [pair for k in range(1, count - 1, 2) for pair in ((k, k + 1), (k + 1, k))]
    )


def halo_join(cells, odd, inner, outer, dim):
    return jnp.concatenate(
        [jnp.where(odd, inner, outer), cells, jnp.where(odd, outer, inner)], axis=dim
    )


def butterfly_sum(flat, cells, halvings=2):
    steps = []
    for axis in ("col", "row"):
        bit = 1
        while bit < lax.axis_size(axis):
            steps.append((axis, bit))
            bit *= 2
    for axis, bit in steps[:halvings]:
        upper = (lax.axis_index(axis) // bit) % 2 == 1
        half = flat.shape[0] // 2
        low, high = flat[:half], flat[half:]
        keep = jnp.where(upper, high, low)
        give = jnp.where(upper, low, high)
        if (axis, bit) == ("col", 1):
            odd, inner_piece, outer_piece = halo_ends(cells, "col", 1)
            outer = outer_swap(outer_piece, "col")
            got, inner = swap_with(give, axis, bit, inner_piece)
            cells = halo_join(cells, odd, inner, outer, 1)
        else:
            got = exchange(give, axis, bit)
        flat = keep + got
    for axis, bit in steps[halvings:]:
        if (axis, bit) == ("row", 1):
            odd, inner_piece, outer_piece = halo_ends(cells, "row", 0)
            outer = outer_swap(outer_piece, "row")
            got, inner = swap_with(flat, axis, bit, inner_piece)
            cells = halo_join(cells, odd, inner, outer, 0)
        else:
            got = exchange(flat, axis, bit)
        flat = flat + got
    for axis, bit in reversed(steps[:halvings]):
        upper = (lax.axis_index(axis) // bit) % 2 == 1
        other = exchange(flat, axis, bit)
        flat = jnp.where(upper, jnp.concatenate([other, flat]), jnp.concatenate([flat, other]))
    return flat, cells


def silu_slope(value):
    sig = jax.nn.sigmoid(value)
    return sig * (1.0 + value * (1.0 - sig))


def spatial_forward(padded, conv_weight, tile_rows, tile_cols):
    running_sum = None
    for row_tap in range(3):
        tap_patch = jnp.concatenate(
            [
                padded[row_tap : row_tap + tile_rows, col_tap : col_tap + tile_cols]
                for col_tap in range(3)
            ],
            axis=-1,
        )
        tap_term = jnp.dot(
            tap_patch,
            conv_weight[row_tap].reshape(3 * C_IN, C_OUT),
            preferred_element_type=jnp.float32,
        )
        running_sum = tap_term if running_sum is None else running_sum + tap_term
    return running_sum


def transposed_conv(padded_grad, conv_weight, out_rows, out_cols):
    input_sum = None
    for row_tap in range(3):
        grad_patch = jnp.concatenate(
            [
                padded_grad[
                    2 - row_tap : 2 - row_tap + out_rows, 2 - col_tap : 2 - col_tap + out_cols
                ]
                for col_tap in range(3)
            ],
            axis=-1,
        )
        flipped = jnp.concatenate([conv_weight[row_tap, col_tap].T for col_tap in range(3)], axis=0)
        tap_term = jnp.dot(grad_patch, flipped, preferred_element_type=jnp.float32)
        input_sum = tap_term if input_sum is None else input_sum + tap_term
    return input_sum


def same_group():
    rows = lax.broadcasted_iota(jnp.int32, (C_OUT, C_OUT), 0) // CPG
    cols = lax.broadcasted_iota(jnp.int32, (C_OUT, C_OUT), 1) // CPG
    return rows == cols


def block_weights(time_weight):
    tiled = jnp.tile(time_weight.reshape(3, C_OUT, CPG), (1, 1, GROUPS))
    return jnp.where(same_group()[None], tiled, jnp.zeros_like(tiled))


def group_blocks(dense):
    masked = jnp.where(same_group()[None], dense, jnp.zeros_like(dense))
    pick = (
        lax.broadcasted_iota(jnp.int32, (C_OUT, CPG), 0) % CPG
        == lax.broadcasted_iota(jnp.int32, (C_OUT, CPG), 1)
    ).astype(jnp.float32)
    return jnp.dot(masked, pick, precision=PRECISE).reshape(3, GROUPS, CPG, CPG)


def per_device(
    pixels, conv_weight, time_weight, class_weight, pixel_slot, straddle_dir, straddle_slot, labels
):
    tile_rows, tile_cols = (pixels.shape[0], pixels.shape[1])
    slot_count = P_OWN + S_STR
    padded_pixels = with_halo(pixels, (("row", 0), ("col", 1)), 1).reshape(
        tile_rows + 2, tile_cols + 2, DATES, C_IN
    )
    pre_act = spatial_forward(padded_pixels, conv_weight, tile_rows, tile_cols)
    hidden = jax.nn.silu(pre_act).astype(jnp.bfloat16)
    dense_time = block_weights(time_weight)
    padded_hidden = jnp.pad(hidden, ((0, 0), (0, 0), (1, 1), (0, 0)))
    mixed_time = None
    for time_tap in range(3):
        tap_term = jnp.dot(
            padded_hidden[:, :, time_tap : time_tap + DATES],
            dense_time[time_tap],
            preferred_element_type=jnp.float32,
        )
        mixed_time = tap_term if mixed_time is None else mixed_time + tap_term
    embedded = (
        jnp.mean(jax.nn.silu(mixed_time), axis=2)
        .astype(jnp.bfloat16)
        .reshape(tile_rows * tile_cols, C_OUT)
    )
    flat_slot = pixel_slot.reshape(tile_rows * tile_cols)
    membership = (jnp.arange(slot_count, dtype=jnp.int32)[:, None] == flat_slot[None, :]).astype(
        jnp.bfloat16
    )
    partial_value = jnp.dot(membership, embedded, preferred_element_type=jnp.float32)
    direction = straddle_dir.reshape(S_STR)
    owner_slot = straddle_slot.reshape(S_STR)
    own_slots = jnp.arange(P_OWN, dtype=jnp.int32)
    target = jnp.concatenate([4 * P_OWN + own_slots, direction * P_OWN + owner_slot])
    select = (jnp.arange(9 * P_OWN, dtype=jnp.int32)[:, None] == target[None, :]).astype(
        jnp.float32
    )
    outgoing = jnp.dot(select, partial_value, precision=PRECISE).reshape(3, 3, P_OWN, C_OUT)
    border = with_halo(outgoing.astype(jnp.bfloat16), (("row", 0), ("col", 1)), 1).astype(
        outgoing.dtype
    )
    parcel_sums = jnp.sum(border[0::2, 0::2], axis=(0, 1))
    centered = parcel_sums - jnp.mean(parcel_sums, axis=-1, keepdims=True)
    variance = jnp.mean(centered * centered, axis=-1, keepdims=True)
    inverse = lax.rsqrt(variance + EPSILON)
    normed = centered * inverse
    rounded = normed.astype(jnp.bfloat16)
    logits = jnp.dot(rounded, class_weight, preferred_element_type=jnp.float32)
    exp_logits = jnp.exp(logits)
    probability = exp_logits / jnp.sum(exp_logits, axis=-1, keepdims=True)
    label_hot = (
        labels.reshape(P_OWN)[:, None] == jnp.arange(CLASSES, dtype=jnp.int32)[None, :]
    ).astype(jnp.float32)
    parcel_total = P_OWN * lax.axis_size("row") * lax.axis_size("col")
    grad_logits = (probability - label_hot) / parcel_total
    class_term = jnp.dot(rounded.astype(jnp.float32).T, grad_logits, precision=PRECISE)
    grad_normed = jnp.dot(grad_logits, class_weight.astype(jnp.float32).T, precision=PRECISE)
    parcel_grad = (
        inverse
        * (
            grad_normed
            - jnp.mean(grad_normed, axis=-1, keepdims=True)
            - normed * jnp.mean(grad_normed * normed, axis=-1, keepdims=True)
        )
    ).astype(jnp.bfloat16)
    beside_all = with_halo(
        parcel_grad.reshape(1, 1, P_OWN, C_OUT), (("row", 0), ("col", 1)), 1
    ).reshape(9 * P_OWN, C_OUT)
    picker = (target[:, None] == jnp.arange(9 * P_OWN, dtype=jnp.int32)[None, :]).astype(
        jnp.bfloat16
    )
    slot_grad = jnp.dot(picker, beside_all, preferred_element_type=jnp.float32).astype(jnp.bfloat16)
    pixel_grad = jnp.dot(membership.T, slot_grad, preferred_element_type=jnp.float32).reshape(
        tile_rows, tile_cols, C_OUT
    )
    grad_mixed = ((pixel_grad / DATES)[:, :, None, :] * silu_slope(mixed_time)).astype(jnp.bfloat16)
    time_term = group_blocks(
        jnp.stack(
            [
                jnp.einsum(
                    "ijtc,ijtd->cd",
                    padded_hidden[:, :, time_tap : time_tap + DATES],
                    grad_mixed,
                    preferred_element_type=jnp.float32,
                )
                for time_tap in range(3)
            ]
        )
    )
    padded_mixed = jnp.pad(grad_mixed, ((0, 0), (0, 0), (1, 1), (0, 0)))
    grad_hidden = None
    for time_tap in range(3):
        tap_term = jnp.dot(
            padded_mixed[:, :, 2 - time_tap : 2 - time_tap + DATES],
            dense_time[time_tap].T,
            preferred_element_type=jnp.float32,
        )
        grad_hidden = tap_term if grad_hidden is None else grad_hidden + tap_term
    grad_pre = (grad_hidden * silu_slope(pre_act)).astype(jnp.bfloat16)
    conv_rows = []
    for row_tap in range(3):
        tap_patch = jnp.concatenate(
            [
                padded_pixels[row_tap : row_tap + tile_rows, col_tap : col_tap + tile_cols]
                for col_tap in range(3)
            ],
            axis=-1,
        )
        conv_rows.append(
            jnp.einsum(
                "ijtc,ijtd->cd", tap_patch, grad_pre, preferred_element_type=jnp.float32
            ).reshape(3, C_IN, C_OUT)
        )
    conv_term = jnp.stack(conv_rows)
    flat, padded_grad = butterfly_sum(
        jnp.concatenate([conv_term.reshape(-1), time_term.reshape(-1), class_term.reshape(-1)]),
        grad_pre.reshape(tile_rows, tile_cols, DATES * C_OUT),
    )
    padded_grad = padded_grad.reshape(tile_rows + 2, tile_cols + 2, DATES, C_OUT)
    input_sum = transposed_conv(padded_grad, conv_weight, tile_rows, tile_cols)
    input_grad = input_sum.astype(jnp.bfloat16).reshape(tile_rows, tile_cols, DATES * C_IN)
    conv_size, time_size = (conv_term.size, time_term.size)
    conv_grad = flat[:conv_size].reshape(conv_term.shape)
    time_grad = flat[conv_size : conv_size + time_size].reshape(time_term.shape)
    class_grad = flat[conv_size + time_size :].reshape(class_term.shape)
    return (input_grad, conv_grad, time_grad, class_grad)


def solution(mesh):
    in_specs = (
        P("row", "col", None),
        P(),
        P(),
        P(),
        P("row", "col"),
        P("row", "col", None),
        P("row", "col", None),
        P("row", "col", None),
    )
    out_specs = (P("row", "col", None), P(), P(), P())
    return jax.shard_map(
        per_device, mesh=mesh, in_specs=in_specs, out_specs=out_specs, check_vma=False
    )
```

```python
import jax
import jax.numpy as jnp
from jax import lax
from jax.sharding import PartitionSpec as P

DATES = 12
C_IN = 64
C_OUT = 128
GROUPS = 16
CLASSES = 20
P_OWN = 32
S_STR = 32
CPG = 8


EPSILON = 1e-05
PRECISE = lax.Precision.HIGHEST


def with_halo(cells, sides, width):
    for axis, dim in sides:
        count = lax.axis_size(axis)
        odd = lax.axis_index(axis) % 2 == 1
        head = lax.slice_in_dim(cells, 0, width, axis=dim)
        tail = lax.slice_in_dim(cells, cells.shape[dim] - width, cells.shape[dim], axis=dim)
        inner = lax.ppermute(jnp.where(odd, head, tail), axis, [(i, i ^ 1) for i in range(count)])
        outer = lax.ppermute(
            jnp.where(odd, tail, head),
            axis,
            [pair for k in range(1, count - 1, 2) for pair in ((k, k + 1), (k + 1, k))],
        )
        cells = jnp.concatenate(
            [jnp.where(odd, inner, outer), cells, jnp.where(odd, outer, inner)], axis=dim
        )
    return cells


def exchange(value, axis, bit):
    size = lax.axis_size(axis)
    return lax.ppermute(value, axis, [(i, i ^ bit) for i in range(size)])


def swap_with(value, axis, bit, extra):
    size = value.shape[0]
    lanes = value.shape[1]
    both = exchange(
        jnp.concatenate([value, extra.astype(value.dtype).reshape(-1, lanes)]), axis, bit
    )
    return both[:size], both[size:].reshape(extra.shape).astype(extra.dtype)


def halo_ends(cells, axis, dim):
    odd = lax.axis_index(axis) % 2 == 1
    head = lax.slice_in_dim(cells, 0, 1, axis=dim)
    tail = lax.slice_in_dim(cells, cells.shape[dim] - 1, cells.shape[dim], axis=dim)
    return odd, jnp.where(odd, head, tail), jnp.where(odd, tail, head)


def outer_swap(piece, axis):
    count = lax.axis_size(axis)
    return lax.ppermute(
        piece, axis, [pair for k in range(1, count - 1, 2) for pair in ((k, k + 1), (k + 1, k))]
    )


def halo_join(cells, odd, inner, outer, dim):
    return jnp.concatenate(
        [jnp.where(odd, inner, outer), cells, jnp.where(odd, outer, inner)], axis=dim
    )


def butterfly_sum(flat, cells, halvings=2):
    steps = []
    for axis in ("col", "row"):
        bit = 1
        while bit < lax.axis_size(axis):
            steps.append((axis, bit))
            bit *= 2
    for axis, bit in steps[:halvings]:
        upper = (lax.axis_index(axis) // bit) % 2 == 1
        half = flat.shape[0] // 2
        low, high = flat[:half], flat[half:]
        keep = jnp.where(upper, high, low)
        give = jnp.where(upper, low, high)
        if (axis, bit) == ("col", 1):
            odd, inner_piece, outer_piece = halo_ends(cells, "col", 1)
            outer = outer_swap(outer_piece, "col")
            got, inner = swap_with(give, axis, bit, inner_piece)
            cells = halo_join(cells, odd, inner, outer, 1)
        else:
            got = exchange(give, axis, bit)
        flat = keep + got
    for axis, bit in steps[halvings:]:
        if (axis, bit) == ("row", 1):
            odd, inner_piece, outer_piece = halo_ends(cells, "row", 0)
            outer = outer_swap(outer_piece, "row")
            got, inner = swap_with(flat, axis, bit, inner_piece)
            cells = halo_join(cells, odd, inner, outer, 0)
        else:
            got = exchange(flat, axis, bit)
        flat = flat + got
    for axis, bit in reversed(steps[:halvings]):
        upper = (lax.axis_index(axis) // bit) % 2 == 1
        other = exchange(flat, axis, bit)
        flat = jnp.where(upper, jnp.concatenate([other, flat]), jnp.concatenate([flat, other]))
    return flat, cells


def silu_slope(value):
    sig = jax.nn.sigmoid(value)
    return sig * (1.0 + value * (1.0 - sig))


def spatial_forward(padded, conv_weight, tile_rows, tile_cols):
    running_sum = None
    for row_tap in range(3):
        tap_patch = jnp.concatenate(
            [
                padded[row_tap : row_tap + tile_rows, col_tap : col_tap + tile_cols]
                for col_tap in range(3)
            ],
            axis=-1,
        )
        tap_term = jnp.dot(
            tap_patch,
            conv_weight[row_tap].reshape(3 * C_IN, C_OUT),
            preferred_element_type=jnp.float32,
        )
        running_sum = tap_term if running_sum is None else running_sum + tap_term
    return running_sum


def transposed_conv(padded_grad, conv_weight, out_rows, out_cols):
    input_sum = None
    for row_tap in range(3):
        grad_patch = jnp.concatenate(
            [
                padded_grad[
                    2 - row_tap : 2 - row_tap + out_rows, 2 - col_tap : 2 - col_tap + out_cols
                ]
                for col_tap in range(3)
            ],
            axis=-1,
        )
        flipped = jnp.concatenate([conv_weight[row_tap, col_tap].T for col_tap in range(3)], axis=0)
        tap_term = jnp.dot(grad_patch, flipped, preferred_element_type=jnp.float32)
        input_sum = tap_term if input_sum is None else input_sum + tap_term
    return input_sum


def same_group():
    rows = lax.broadcasted_iota(jnp.int32, (C_OUT, C_OUT), 0) // CPG
    cols = lax.broadcasted_iota(jnp.int32, (C_OUT, C_OUT), 1) // CPG
    return rows == cols


def block_weights(time_weight):
    tiled = jnp.tile(time_weight.reshape(3, C_OUT, CPG), (1, 1, GROUPS))
    return jnp.where(same_group()[None], tiled, jnp.zeros_like(tiled))


def group_blocks(dense):
    masked = jnp.where(same_group()[None], dense, jnp.zeros_like(dense))
    pick = (
        lax.broadcasted_iota(jnp.int32, (C_OUT, CPG), 0) % CPG
        == lax.broadcasted_iota(jnp.int32, (C_OUT, CPG), 1)
    ).astype(jnp.float32)
    return jnp.dot(masked, pick, precision=PRECISE).reshape(3, GROUPS, CPG, CPG)


def per_device(
    pixels, conv_weight, time_weight, class_weight, pixel_slot, straddle_dir, straddle_slot, labels
):
    tile_rows, tile_cols = (pixels.shape[0], pixels.shape[1])
    slot_count = P_OWN + S_STR
    padded_pixels = with_halo(pixels, (("row", 0), ("col", 1)), 1).reshape(
        tile_rows + 2, tile_cols + 2, DATES, C_IN
    )
    pre_act = spatial_forward(padded_pixels, conv_weight, tile_rows, tile_cols)
    hidden = jax.nn.silu(pre_act).astype(jnp.bfloat16)
    dense_time = block_weights(time_weight)
    padded_hidden = jnp.pad(hidden, ((0, 0), (0, 0), (1, 1), (0, 0)))
    mixed_time = None
    for time_tap in range(3):
        tap_term = jnp.dot(
            padded_hidden[:, :, time_tap : time_tap + DATES],
            dense_time[time_tap],
            preferred_element_type=jnp.float32,
        )
        mixed_time = tap_term if mixed_time is None else mixed_time + tap_term
    embedded = (
        jnp.mean(jax.nn.silu(mixed_time), axis=2)
        .astype(jnp.bfloat16)
        .reshape(tile_rows * tile_cols, C_OUT)
    )
    flat_slot = pixel_slot.reshape(tile_rows * tile_cols)
    membership = (jnp.arange(slot_count, dtype=jnp.int32)[:, None] == flat_slot[None, :]).astype(
        jnp.bfloat16
    )
    partial_value = jnp.dot(membership, embedded, preferred_element_type=jnp.float32)
    direction = straddle_dir.reshape(S_STR)
    owner_slot = straddle_slot.reshape(S_STR)
    own_slots = jnp.arange(P_OWN, dtype=jnp.int32)
    target = jnp.concatenate([4 * P_OWN + own_slots, direction * P_OWN + owner_slot])
    select = (jnp.arange(9 * P_OWN, dtype=jnp.int32)[:, None] == target[None, :]).astype(
        jnp.float32
    )
    outgoing = jnp.dot(select, partial_value, precision=PRECISE).reshape(3, 3, P_OWN, C_OUT)
    border = with_halo(outgoing.astype(jnp.bfloat16), (("row", 0), ("col", 1)), 1).astype(
        outgoing.dtype
    )
    parcel_sums = jnp.sum(border[0::2, 0::2], axis=(0, 1))
    centered = parcel_sums - jnp.mean(parcel_sums, axis=-1, keepdims=True)
    variance = jnp.mean(centered * centered, axis=-1, keepdims=True)
    inverse = lax.rsqrt(variance + EPSILON)
    normed = centered * inverse
    rounded = normed.astype(jnp.bfloat16)
    logits = jnp.dot(rounded, class_weight, preferred_element_type=jnp.float32)
    exp_logits = jnp.exp(logits)
    probability = exp_logits / jnp.sum(exp_logits, axis=-1, keepdims=True)
    label_hot = (
        labels.reshape(P_OWN)[:, None] == jnp.arange(CLASSES, dtype=jnp.int32)[None, :]
    ).astype(jnp.float32)
    parcel_total = P_OWN * lax.axis_size("row") * lax.axis_size("col")
    grad_logits = (probability - label_hot) / parcel_total
    class_term = jnp.dot(rounded.astype(jnp.float32).T, grad_logits, precision=PRECISE)
    grad_normed = jnp.dot(grad_logits, class_weight.astype(jnp.float32).T, precision=PRECISE)
    parcel_grad = (
        inverse
        * (
            grad_normed
            - jnp.mean(grad_normed, axis=-1, keepdims=True)
            - normed * jnp.mean(grad_normed * normed, axis=-1, keepdims=True)
        )
    ).astype(jnp.bfloat16)
    beside_all = with_halo(
        parcel_grad.reshape(1, 1, P_OWN, C_OUT), (("row", 0), ("col", 1)), 1
    ).reshape(9 * P_OWN, C_OUT)
    picker = (target[:, None] == jnp.arange(9 * P_OWN, dtype=jnp.int32)[None, :]).astype(
        jnp.bfloat16
    )
    slot_grad = jnp.dot(picker, beside_all, preferred_element_type=jnp.float32).astype(jnp.bfloat16)
    pixel_grad = jnp.dot(membership.T, slot_grad, preferred_element_type=jnp.float32).reshape(
        tile_rows, tile_cols, C_OUT
    )
    grad_mixed = ((pixel_grad / DATES)[:, :, None, :] * silu_slope(mixed_time)).astype(jnp.bfloat16)
    time_term = group_blocks(
        jnp.stack(
            [
                jnp.einsum(
                    "ijtc,ijtd->cd",
                    padded_hidden[:, :, time_tap : time_tap + DATES],
                    grad_mixed,
                    preferred_element_type=jnp.float32,
                )
                for time_tap in range(3)
            ]
        )
    )
    padded_mixed = jnp.pad(grad_mixed, ((0, 0), (0, 0), (1, 1), (0, 0)))
    grad_hidden = None
    for time_tap in range(3):
        tap_term = jnp.dot(
            padded_mixed[:, :, 2 - time_tap : 2 - time_tap + DATES],
            dense_time[time_tap].T,
            preferred_element_type=jnp.float32,
        )
        grad_hidden = tap_term if grad_hidden is None else grad_hidden + tap_term
    grad_pre = (grad_hidden * silu_slope(pre_act)).astype(jnp.bfloat16)
    conv_rows = []
    for row_tap in range(3):
        tap_patch = jnp.concatenate(
            [
                padded_pixels[row_tap : row_tap + tile_rows, col_tap : col_tap + tile_cols]
                for col_tap in range(3)
            ],
            axis=-1,
        )
        conv_rows.append(
            jnp.einsum(
                "ijtc,ijtd->cd", tap_patch, grad_pre, preferred_element_type=jnp.float32
            ).reshape(3, C_IN, C_OUT)
        )
    conv_term = jnp.stack(conv_rows)
    lanes = C_OUT
    conv_rows, time_rows, class_rows = (
        conv_term.size // lanes,
        time_term.size // lanes,
        class_term.size // lanes,
    )
    used = conv_rows + time_rows + class_rows
    total = -(-used // 32) * 32
    flat, padded_grad = butterfly_sum(
        jnp.concatenate(
            [
                conv_term.reshape(conv_rows, lanes),
                time_term.reshape(time_rows, lanes),
                class_term.reshape(class_rows, lanes),
                jnp.zeros((total - used, lanes), jnp.float32),
            ]
        ),
        grad_pre.reshape(tile_rows, tile_cols, DATES * C_OUT),
    )
    padded_grad = padded_grad.reshape(tile_rows + 2, tile_cols + 2, DATES, C_OUT)
    input_sum = transposed_conv(padded_grad, conv_weight, tile_rows, tile_cols)
    input_grad = input_sum.astype(jnp.bfloat16).reshape(tile_rows, tile_cols, DATES * C_IN)
    conv_grad = flat[:conv_rows].reshape(conv_term.shape)
    time_grad = flat[conv_rows : conv_rows + time_rows].reshape(time_term.shape)
    class_grad = flat[conv_rows + time_rows : used].reshape(class_term.shape)
    return (input_grad, conv_grad, time_grad, class_grad)


def solution(mesh):
    in_specs = (
        P("row", "col", None),
        P(),
        P(),
        P(),
        P("row", "col"),
        P("row", "col", None),
        P("row", "col", None),
        P("row", "col", None),
    )
    out_specs = (P("row", "col", None), P(), P(), P())
    return jax.shard_map(
        per_device, mesh=mesh, in_specs=in_specs, out_specs=out_specs, check_vma=False
    )
```

```python
import jax
import jax.numpy as jnp
from jax import lax
from jax.sharding import PartitionSpec as P

DATES = 12
C_IN = 64
C_OUT = 128
GROUPS = 16
CLASSES = 20
P_OWN = 32
S_STR = 32
CPG = 8


EPSILON = 1e-05
PRECISE = lax.Precision.HIGHEST


def with_halo(cells, sides, width):
    for axis, dim in sides:
        count = lax.axis_size(axis)
        odd = lax.axis_index(axis) % 2 == 1
        head = lax.slice_in_dim(cells, 0, width, axis=dim)
        tail = lax.slice_in_dim(cells, cells.shape[dim] - width, cells.shape[dim], axis=dim)
        inner = lax.ppermute(jnp.where(odd, head, tail), axis, [(i, i ^ 1) for i in range(count)])
        outer = lax.ppermute(
            jnp.where(odd, tail, head),
            axis,
            [pair for k in range(1, count - 1, 2) for pair in ((k, k + 1), (k + 1, k))],
        )
        cells = jnp.concatenate(
            [jnp.where(odd, inner, outer), cells, jnp.where(odd, outer, inner)], axis=dim
        )
    return cells


def exchange(value, axis, bit):
    size = lax.axis_size(axis)
    return lax.ppermute(value, axis, [(i, i ^ bit) for i in range(size)])


def swap_with(value, axis, bit, extra):
    size = value.shape[0]
    lanes = value.shape[1]
    both = exchange(
        jnp.concatenate([value, extra.astype(value.dtype).reshape(-1, lanes)]), axis, bit
    )
    return both[:size], both[size:].reshape(extra.shape).astype(extra.dtype)


def halo_ends(cells, axis, dim):
    odd = lax.axis_index(axis) % 2 == 1
    head = lax.slice_in_dim(cells, 0, 1, axis=dim)
    tail = lax.slice_in_dim(cells, cells.shape[dim] - 1, cells.shape[dim], axis=dim)
    return odd, jnp.where(odd, head, tail), jnp.where(odd, tail, head)


def outer_swap(piece, axis):
    count = lax.axis_size(axis)
    return lax.ppermute(
        piece, axis, [pair for k in range(1, count - 1, 2) for pair in ((k, k + 1), (k + 1, k))]
    )


def halo_join(cells, odd, inner, outer, dim):
    return jnp.concatenate(
        [jnp.where(odd, inner, outer), cells, jnp.where(odd, outer, inner)], axis=dim
    )


def butterfly_sum(flat, cells, halvings=2):
    steps = []
    for axis in ("col", "row"):
        bit = 1
        while bit < lax.axis_size(axis):
            steps.append((axis, bit))
            bit *= 2
    for axis, bit in steps[:halvings]:
        upper = (lax.axis_index(axis) // bit) % 2 == 1
        half = flat.shape[0] // 2
        low, high = flat[:half], flat[half:]
        keep = jnp.where(upper, high, low)
        give = jnp.where(upper, low, high)
        if (axis, bit) == ("col", 1):
            odd, inner_piece, outer_piece = halo_ends(cells, "col", 1)
            outer = outer_swap(outer_piece, "col")
            got, inner = swap_with(give, axis, bit, inner_piece)
            cells = halo_join(cells, odd, inner, outer, 1)
        else:
            got = exchange(give, axis, bit)
        flat = keep + got
    for axis, bit in steps[halvings:]:
        if (axis, bit) == ("row", 1):
            odd, inner_piece, outer_piece = halo_ends(cells, "row", 0)
            outer = outer_swap(outer_piece, "row")
            got, inner = swap_with(flat, axis, bit, inner_piece)
            cells = halo_join(cells, odd, inner, outer, 0)
        else:
            got = exchange(flat, axis, bit)
        flat = flat + got
    for axis, bit in reversed(steps[:halvings]):
        upper = (lax.axis_index(axis) // bit) % 2 == 1
        other = exchange(flat, axis, bit)
        flat = jnp.where(upper, jnp.concatenate([other, flat]), jnp.concatenate([flat, other]))
    return flat, cells


def silu_slope(value):
    sig = jax.nn.sigmoid(value)
    return sig * (1.0 + value * (1.0 - sig))


def spatial_forward(padded, conv_weight, tile_rows, tile_cols):
    running_sum = None
    for row_tap in range(3):
        tap_patch = jnp.concatenate(
            [
                padded[row_tap : row_tap + tile_rows, col_tap : col_tap + tile_cols]
                for col_tap in range(3)
            ],
            axis=-1,
        )
        tap_term = jnp.dot(
            tap_patch,
            conv_weight[row_tap].reshape(3 * C_IN, C_OUT),
            preferred_element_type=jnp.float32,
        )
        running_sum = tap_term if running_sum is None else running_sum + tap_term
    return running_sum


def window_conv(padded, kernel):
    return lax.conv_general_dilated(
        padded,
        kernel,
        window_strides=(1, 1),
        padding="VALID",
        dimension_numbers=("HWNC", "HWIO", "HWNC"),
        preferred_element_type=jnp.float32,
    )


def transposed_conv(padded_grad, conv_weight, out_rows, out_cols):
    input_sum = None
    for row_tap in range(3):
        grad_patch = jnp.concatenate(
            [
                padded_grad[
                    2 - row_tap : 2 - row_tap + out_rows, 2 - col_tap : 2 - col_tap + out_cols
                ]
                for col_tap in range(3)
            ],
            axis=-1,
        )
        flipped = jnp.concatenate([conv_weight[row_tap, col_tap].T for col_tap in range(3)], axis=0)
        tap_term = jnp.dot(grad_patch, flipped, preferred_element_type=jnp.float32)
        input_sum = tap_term if input_sum is None else input_sum + tap_term
    return input_sum


def same_group():
    rows = lax.broadcasted_iota(jnp.int32, (C_OUT, C_OUT), 0) // CPG
    cols = lax.broadcasted_iota(jnp.int32, (C_OUT, C_OUT), 1) // CPG
    return rows == cols


def block_weights(time_weight):
    tiled = jnp.tile(time_weight.reshape(3, C_OUT, CPG), (1, 1, GROUPS))
    return jnp.where(same_group()[None], tiled, jnp.zeros_like(tiled))


def group_blocks(dense):
    masked = jnp.where(same_group()[None], dense, jnp.zeros_like(dense))
    pick = (
        lax.broadcasted_iota(jnp.int32, (C_OUT, CPG), 0) % CPG
        == lax.broadcasted_iota(jnp.int32, (C_OUT, CPG), 1)
    ).astype(jnp.float32)
    return jnp.dot(masked, pick, precision=PRECISE).reshape(3, GROUPS, CPG, CPG)


def per_device(
    pixels, conv_weight, time_weight, class_weight, pixel_slot, straddle_dir, straddle_slot, labels
):
    tile_rows, tile_cols = (pixels.shape[0], pixels.shape[1])
    slot_count = P_OWN + S_STR
    padded_pixels = with_halo(pixels, (("row", 0), ("col", 1)), 1).reshape(
        tile_rows + 2, tile_cols + 2, DATES, C_IN
    )
    pre_act = window_conv(padded_pixels, conv_weight)
    hidden = jax.nn.silu(pre_act).astype(jnp.bfloat16)
    dense_time = block_weights(time_weight)
    padded_hidden = jnp.pad(hidden, ((0, 0), (0, 0), (1, 1), (0, 0)))
    mixed_time = None
    for time_tap in range(3):
        tap_term = jnp.dot(
            padded_hidden[:, :, time_tap : time_tap + DATES],
            dense_time[time_tap],
            preferred_element_type=jnp.float32,
        )
        mixed_time = tap_term if mixed_time is None else mixed_time + tap_term
    embedded = (
        jnp.mean(jax.nn.silu(mixed_time), axis=2)
        .astype(jnp.bfloat16)
        .reshape(tile_rows * tile_cols, C_OUT)
    )
    flat_slot = pixel_slot.reshape(tile_rows * tile_cols)
    membership = (jnp.arange(slot_count, dtype=jnp.int32)[:, None] == flat_slot[None, :]).astype(
        jnp.bfloat16
    )
    partial_value = jnp.dot(membership, embedded, preferred_element_type=jnp.float32)
    direction = straddle_dir.reshape(S_STR)
    owner_slot = straddle_slot.reshape(S_STR)
    own_slots = jnp.arange(P_OWN, dtype=jnp.int32)
    target = jnp.concatenate([4 * P_OWN + own_slots, direction * P_OWN + owner_slot])
    select = (jnp.arange(9 * P_OWN, dtype=jnp.int32)[:, None] == target[None, :]).astype(
        jnp.float32
    )
    outgoing = jnp.dot(select, partial_value, precision=PRECISE).reshape(3, 3, P_OWN, C_OUT)
    border = with_halo(outgoing.astype(jnp.bfloat16), (("row", 0), ("col", 1)), 1).astype(
        outgoing.dtype
    )
    parcel_sums = jnp.sum(border[0::2, 0::2], axis=(0, 1))
    centered = parcel_sums - jnp.mean(parcel_sums, axis=-1, keepdims=True)
    variance = jnp.mean(centered * centered, axis=-1, keepdims=True)
    inverse = lax.rsqrt(variance + EPSILON)
    normed = centered * inverse
    rounded = normed.astype(jnp.bfloat16)
    logits = jnp.dot(rounded, class_weight, preferred_element_type=jnp.float32)
    exp_logits = jnp.exp(logits)
    probability = exp_logits / jnp.sum(exp_logits, axis=-1, keepdims=True)
    label_hot = (
        labels.reshape(P_OWN)[:, None] == jnp.arange(CLASSES, dtype=jnp.int32)[None, :]
    ).astype(jnp.float32)
    parcel_total = P_OWN * lax.axis_size("row") * lax.axis_size("col")
    grad_logits = (probability - label_hot) / parcel_total
    class_term = jnp.dot(rounded.astype(jnp.float32).T, grad_logits, precision=PRECISE)
    grad_normed = jnp.dot(grad_logits, class_weight.astype(jnp.float32).T, precision=PRECISE)
    parcel_grad = (
        inverse
        * (
            grad_normed
            - jnp.mean(grad_normed, axis=-1, keepdims=True)
            - normed * jnp.mean(grad_normed * normed, axis=-1, keepdims=True)
        )
    ).astype(jnp.bfloat16)
    beside_all = with_halo(
        parcel_grad.reshape(1, 1, P_OWN, C_OUT), (("row", 0), ("col", 1)), 1
    ).reshape(9 * P_OWN, C_OUT)
    picker = (target[:, None] == jnp.arange(9 * P_OWN, dtype=jnp.int32)[None, :]).astype(
        jnp.bfloat16
    )
    slot_grad = jnp.dot(picker, beside_all, preferred_element_type=jnp.float32).astype(jnp.bfloat16)
    pixel_grad = jnp.dot(membership.T, slot_grad, preferred_element_type=jnp.float32).reshape(
        tile_rows, tile_cols, C_OUT
    )
    grad_mixed = ((pixel_grad / DATES)[:, :, None, :] * silu_slope(mixed_time)).astype(jnp.bfloat16)
    time_term = group_blocks(
        jnp.stack(
            [
                jnp.einsum(
                    "ijtc,ijtd->cd",
                    padded_hidden[:, :, time_tap : time_tap + DATES],
                    grad_mixed,
                    preferred_element_type=jnp.float32,
                )
                for time_tap in range(3)
            ]
        )
    )
    padded_mixed = jnp.pad(grad_mixed, ((0, 0), (0, 0), (1, 1), (0, 0)))
    grad_hidden = None
    for time_tap in range(3):
        tap_term = jnp.dot(
            padded_mixed[:, :, 2 - time_tap : 2 - time_tap + DATES],
            dense_time[time_tap].T,
            preferred_element_type=jnp.float32,
        )
        grad_hidden = tap_term if grad_hidden is None else grad_hidden + tap_term
    grad_pre = (grad_hidden * silu_slope(pre_act)).astype(jnp.bfloat16)
    conv_rows = []
    for row_tap in range(3):
        tap_patch = jnp.concatenate(
            [
                padded_pixels[row_tap : row_tap + tile_rows, col_tap : col_tap + tile_cols]
                for col_tap in range(3)
            ],
            axis=-1,
        )
        conv_rows.append(
            jnp.einsum(
                "ijtc,ijtd->cd", tap_patch, grad_pre, preferred_element_type=jnp.float32
            ).reshape(3, C_IN, C_OUT)
        )
    conv_term = jnp.stack(conv_rows)
    lanes = C_OUT
    conv_rows, time_rows, class_rows = (
        conv_term.size // lanes,
        time_term.size // lanes,
        class_term.size // lanes,
    )
    used = conv_rows + time_rows + class_rows
    total = -(-used // 32) * 32
    flat, padded_grad = butterfly_sum(
        jnp.concatenate(
            [
                conv_term.reshape(conv_rows, lanes),
                time_term.reshape(time_rows, lanes),
                class_term.reshape(class_rows, lanes),
                jnp.zeros((total - used, lanes), jnp.float32),
            ]
        ),
        grad_pre.reshape(tile_rows, tile_cols, DATES * C_OUT),
    )
    padded_grad = padded_grad.reshape(tile_rows + 2, tile_cols + 2, DATES, C_OUT)
    input_sum = window_conv(padded_grad, jnp.swapaxes(conv_weight[::-1, ::-1], 2, 3))
    input_grad = input_sum.astype(jnp.bfloat16).reshape(tile_rows, tile_cols, DATES * C_IN)
    conv_grad = flat[:conv_rows].reshape(conv_term.shape)
    time_grad = flat[conv_rows : conv_rows + time_rows].reshape(time_term.shape)
    class_grad = flat[conv_rows + time_rows : used].reshape(class_term.shape)
    return (input_grad, conv_grad, time_grad, class_grad)


def solution(mesh):
    in_specs = (
        P("row", "col", None),
        P(),
        P(),
        P(),
        P("row", "col"),
        P("row", "col", None),
        P("row", "col", None),
        P("row", "col", None),
    )
    out_specs = (P("row", "col", None), P(), P(), P())
    return jax.shard_map(
        per_device, mesh=mesh, in_specs=in_specs, out_specs=out_specs, check_vma=False
    )
```

```python
import jax
import jax.numpy as jnp
from jax import lax
from jax.sharding import PartitionSpec as P

DATES = 12
C_IN = 64
C_OUT = 128
GROUPS = 16
CLASSES = 20
P_OWN = 32
S_STR = 32
CPG = 8


EPSILON = 1e-05
PRECISE = lax.Precision.HIGHEST


def with_halo(cells, sides, width):
    for axis, dim in sides:
        count = lax.axis_size(axis)
        odd = lax.axis_index(axis) % 2 == 1
        head = lax.slice_in_dim(cells, 0, width, axis=dim)
        tail = lax.slice_in_dim(cells, cells.shape[dim] - width, cells.shape[dim], axis=dim)
        inner = lax.ppermute(jnp.where(odd, head, tail), axis, [(i, i ^ 1) for i in range(count)])
        outer = lax.ppermute(
            jnp.where(odd, tail, head),
            axis,
            [pair for k in range(1, count - 1, 2) for pair in ((k, k + 1), (k + 1, k))],
        )
        cells = jnp.concatenate(
            [jnp.where(odd, inner, outer), cells, jnp.where(odd, outer, inner)], axis=dim
        )
    return cells


def exchange(value, axis, bit):
    size = lax.axis_size(axis)
    return lax.ppermute(value, axis, [(i, i ^ bit) for i in range(size)])


def swap_with(value, axis, bit, extra):
    size = value.shape[0]
    lanes = value.shape[1]
    both = exchange(
        jnp.concatenate([value, extra.astype(value.dtype).reshape(-1, lanes)]), axis, bit
    )
    return both[:size], both[size:].reshape(extra.shape).astype(extra.dtype)


def halo_ends(cells, axis, dim):
    odd = lax.axis_index(axis) % 2 == 1
    head = lax.slice_in_dim(cells, 0, 1, axis=dim)
    tail = lax.slice_in_dim(cells, cells.shape[dim] - 1, cells.shape[dim], axis=dim)
    return odd, jnp.where(odd, head, tail), jnp.where(odd, tail, head)


def outer_swap(piece, axis):
    count = lax.axis_size(axis)
    return lax.ppermute(
        piece, axis, [pair for k in range(1, count - 1, 2) for pair in ((k, k + 1), (k + 1, k))]
    )


def halo_join(cells, odd, inner, outer, dim):
    return jnp.concatenate(
        [jnp.where(odd, inner, outer), cells, jnp.where(odd, outer, inner)], axis=dim
    )


def butterfly_sum(flat, cells, halvings=2):
    steps = []
    for axis in ("col", "row"):
        bit = 1
        while bit < lax.axis_size(axis):
            steps.append((axis, bit))
            bit *= 2
    for axis, bit in steps[:halvings]:
        upper = (lax.axis_index(axis) // bit) % 2 == 1
        half = flat.shape[0] // 2
        low, high = flat[:half], flat[half:]
        keep = jnp.where(upper, high, low)
        give = jnp.where(upper, low, high)
        if (axis, bit) == ("col", 1):
            odd, inner_piece, outer_piece = halo_ends(cells, "col", 1)
            outer = outer_swap(outer_piece, "col")
            got, inner = swap_with(give, axis, bit, inner_piece)
            cells = halo_join(cells, odd, inner, outer, 1)
        else:
            got = exchange(give, axis, bit)
        flat = keep + got
    for axis, bit in steps[halvings:]:
        if (axis, bit) == ("row", 1):
            odd, inner_piece, outer_piece = halo_ends(cells, "row", 0)
            outer = outer_swap(outer_piece, "row")
            got, inner = swap_with(flat, axis, bit, inner_piece)
            cells = halo_join(cells, odd, inner, outer, 0)
        else:
            got = exchange(flat, axis, bit)
        flat = flat + got
    for axis, bit in reversed(steps[:halvings]):
        upper = (lax.axis_index(axis) // bit) % 2 == 1
        other = exchange(flat, axis, bit)
        flat = jnp.where(upper, jnp.concatenate([other, flat]), jnp.concatenate([flat, other]))
    return flat, cells


def silu_slope(value):
    sig = jax.nn.sigmoid(value)
    return sig * (1.0 + value * (1.0 - sig))


def spatial_forward(padded, conv_weight, tile_rows, tile_cols):
    running_sum = None
    for row_tap in range(3):
        tap_patch = jnp.concatenate(
            [
                padded[row_tap : row_tap + tile_rows, col_tap : col_tap + tile_cols]
                for col_tap in range(3)
            ],
            axis=-1,
        )
        tap_term = jnp.dot(
            tap_patch,
            conv_weight[row_tap].reshape(3 * C_IN, C_OUT),
            preferred_element_type=jnp.float32,
        )
        running_sum = tap_term if running_sum is None else running_sum + tap_term
    return running_sum


def window_conv(padded, kernel):
    return lax.conv_general_dilated(
        padded,
        kernel,
        window_strides=(1, 1),
        padding="VALID",
        dimension_numbers=("HWNC", "HWIO", "HWNC"),
        preferred_element_type=jnp.float32,
    )


def transposed_conv(padded_grad, conv_weight, out_rows, out_cols):
    input_sum = None
    for row_tap in range(3):
        grad_patch = jnp.concatenate(
            [
                padded_grad[
                    2 - row_tap : 2 - row_tap + out_rows, 2 - col_tap : 2 - col_tap + out_cols
                ]
                for col_tap in range(3)
            ],
            axis=-1,
        )
        flipped = jnp.concatenate([conv_weight[row_tap, col_tap].T for col_tap in range(3)], axis=0)
        tap_term = jnp.dot(grad_patch, flipped, preferred_element_type=jnp.float32)
        input_sum = tap_term if input_sum is None else input_sum + tap_term
    return input_sum


def same_group():
    rows = lax.broadcasted_iota(jnp.int32, (C_OUT, C_OUT), 0) // CPG
    cols = lax.broadcasted_iota(jnp.int32, (C_OUT, C_OUT), 1) // CPG
    return rows == cols


def block_weights(time_weight):
    tiled = jnp.tile(time_weight.reshape(3, C_OUT, CPG), (1, 1, GROUPS))
    return jnp.where(same_group()[None], tiled, jnp.zeros_like(tiled))


def group_blocks(dense):
    masked = jnp.where(same_group()[None], dense, jnp.zeros_like(dense))
    pick = (
        lax.broadcasted_iota(jnp.int32, (C_OUT, CPG), 0) % CPG
        == lax.broadcasted_iota(jnp.int32, (C_OUT, CPG), 1)
    ).astype(jnp.float32)
    return jnp.dot(masked, pick, precision=PRECISE).reshape(3, GROUPS, CPG, CPG)


def per_device(
    pixels, conv_weight, time_weight, class_weight, pixel_slot, straddle_dir, straddle_slot, labels
):
    tile_rows, tile_cols = (pixels.shape[0], pixels.shape[1])
    slot_count = P_OWN + S_STR
    padded_pixels = with_halo(pixels, (("row", 0), ("col", 1)), 1).reshape(
        tile_rows + 2, tile_cols + 2, DATES, C_IN
    )
    pre_act = window_conv(padded_pixels, conv_weight)
    hidden = jax.nn.silu(pre_act).astype(jnp.bfloat16)
    dense_time = block_weights(time_weight)
    padded_hidden = jnp.pad(hidden, ((0, 0), (0, 0), (1, 1), (0, 0)))
    mixed_time = None
    for time_tap in range(3):
        tap_term = jnp.dot(
            padded_hidden[:, :, time_tap : time_tap + DATES],
            dense_time[time_tap],
            preferred_element_type=jnp.float32,
        )
        mixed_time = tap_term if mixed_time is None else mixed_time + tap_term
    embedded = (
        jnp.mean(jax.nn.silu(mixed_time), axis=2)
        .astype(jnp.bfloat16)
        .reshape(tile_rows * tile_cols, C_OUT)
    )
    flat_slot = pixel_slot.reshape(tile_rows * tile_cols)
    membership = (jnp.arange(slot_count, dtype=jnp.int32)[:, None] == flat_slot[None, :]).astype(
        jnp.bfloat16
    )
    partial_value = jnp.dot(membership, embedded, preferred_element_type=jnp.float32)
    direction = straddle_dir.reshape(S_STR)
    owner_slot = straddle_slot.reshape(S_STR)
    own_slots = jnp.arange(P_OWN, dtype=jnp.int32)
    target = jnp.concatenate([4 * P_OWN + own_slots, direction * P_OWN + owner_slot])
    select = (jnp.arange(9 * P_OWN, dtype=jnp.int32)[:, None] == target[None, :]).astype(
        jnp.float32
    )
    outgoing = jnp.dot(select, partial_value, precision=PRECISE).reshape(3, 3, P_OWN, C_OUT)
    border = with_halo(outgoing.astype(jnp.bfloat16), (("row", 0), ("col", 1)), 1).astype(
        outgoing.dtype
    )
    parcel_sums = jnp.sum(border[0::2, 0::2], axis=(0, 1))
    centered = parcel_sums - jnp.mean(parcel_sums, axis=-1, keepdims=True)
    variance = jnp.mean(centered * centered, axis=-1, keepdims=True)
    inverse = lax.rsqrt(variance + EPSILON)
    normed = centered * inverse
    rounded = normed.astype(jnp.bfloat16)
    logits = jnp.dot(rounded, class_weight, preferred_element_type=jnp.float32)
    exp_logits = jnp.exp(logits)
    probability = exp_logits / jnp.sum(exp_logits, axis=-1, keepdims=True)
    label_hot = (
        labels.reshape(P_OWN)[:, None] == jnp.arange(CLASSES, dtype=jnp.int32)[None, :]
    ).astype(jnp.float32)
    parcel_total = P_OWN * lax.axis_size("row") * lax.axis_size("col")
    grad_logits = (probability - label_hot) / parcel_total
    class_term = jnp.dot(rounded.astype(jnp.float32).T, grad_logits, precision=PRECISE)
    grad_normed = jnp.dot(grad_logits, class_weight.astype(jnp.float32).T, precision=PRECISE)
    parcel_grad = (
        inverse
        * (
            grad_normed
            - jnp.mean(grad_normed, axis=-1, keepdims=True)
            - normed * jnp.mean(grad_normed * normed, axis=-1, keepdims=True)
        )
    ).astype(jnp.bfloat16)
    beside_all = with_halo(
        parcel_grad.reshape(1, 1, P_OWN, C_OUT), (("row", 0), ("col", 1)), 1
    ).reshape(9 * P_OWN, C_OUT)
    picker = (target[:, None] == jnp.arange(9 * P_OWN, dtype=jnp.int32)[None, :]).astype(
        jnp.bfloat16
    )
    slot_grad = jnp.dot(picker, beside_all, preferred_element_type=jnp.float32).astype(jnp.bfloat16)
    pixel_grad = jnp.dot(membership.T, slot_grad, preferred_element_type=jnp.float32).reshape(
        tile_rows, tile_cols, C_OUT
    )
    grad_mixed = ((pixel_grad / DATES)[:, :, None, :] * silu_slope(mixed_time)).astype(jnp.bfloat16)
    time_term = group_blocks(
        jnp.stack(
            [
                jnp.einsum(
                    "ijtc,ijtd->cd",
                    padded_hidden[:, :, time_tap : time_tap + DATES],
                    grad_mixed,
                    preferred_element_type=jnp.float32,
                )
                for time_tap in range(3)
            ]
        )
    )
    padded_mixed = jnp.pad(grad_mixed, ((0, 0), (0, 0), (1, 1), (0, 0)))
    grad_hidden = None
    for time_tap in range(3):
        tap_term = jnp.dot(
            padded_mixed[:, :, 2 - time_tap : 2 - time_tap + DATES],
            dense_time[time_tap].T,
            preferred_element_type=jnp.float32,
        )
        grad_hidden = tap_term if grad_hidden is None else grad_hidden + tap_term
    grad_pre = (grad_hidden * silu_slope(pre_act)).astype(jnp.bfloat16)
    conv_rows = []
    for row_tap in range(3):
        tap_patch = jnp.concatenate(
            [
                padded_pixels[row_tap : row_tap + tile_rows, col_tap : col_tap + tile_cols]
                for col_tap in range(3)
            ],
            axis=-1,
        )
        conv_rows.append(
            jnp.einsum(
                "ijtc,ijtd->cd", tap_patch, grad_pre, preferred_element_type=jnp.float32
            ).reshape(3, C_IN, C_OUT)
        )
    conv_term = jnp.stack(conv_rows)
    lanes = C_OUT
    conv_rows, time_rows, class_rows = (
        conv_term.size // lanes,
        time_term.size // lanes,
        class_term.size // lanes,
    )
    used = conv_rows + time_rows + class_rows
    total = -(-used // 32) * 32
    flat, padded_grad = butterfly_sum(
        jnp.concatenate(
            [
                conv_term.reshape(conv_rows, lanes),
                time_term.reshape(time_rows, lanes),
                class_term.reshape(class_rows, lanes),
                jnp.zeros((total - used, lanes), jnp.float32),
            ]
        ),
        grad_pre.reshape(tile_rows, tile_cols, DATES * C_OUT),
    )
    padded_grad = padded_grad.reshape(tile_rows + 2, tile_cols + 2, DATES, C_OUT)
    input_sum = transposed_conv(padded_grad, conv_weight, tile_rows, tile_cols)
    input_grad = input_sum.astype(jnp.bfloat16).reshape(tile_rows, tile_cols, DATES * C_IN)
    conv_grad = flat[:conv_rows].reshape(conv_term.shape)
    time_grad = flat[conv_rows : conv_rows + time_rows].reshape(time_term.shape)
    class_grad = flat[conv_rows + time_rows : used].reshape(class_term.shape)
    return (input_grad, conv_grad, time_grad, class_grad)


def solution(mesh):
    in_specs = (
        P("row", "col", None),
        P(),
        P(),
        P(),
        P("row", "col"),
        P("row", "col", None),
        P("row", "col", None),
        P("row", "col", None),
    )
    out_specs = (P("row", "col", None), P(), P(), P())
    return jax.shard_map(
        per_device, mesh=mesh, in_specs=in_specs, out_specs=out_specs, check_vma=False
    )
```

```python
import jax
import jax.numpy as jnp
from jax import lax
from jax.sharding import PartitionSpec as P

DATES = 12
C_IN = 64
C_OUT = 128
GROUPS = 16
CLASSES = 20
P_OWN = 32
S_STR = 32
CPG = 8


EPSILON = 1e-05
PRECISE = lax.Precision.HIGHEST


def with_halo(cells, sides, width):
    for axis, dim in sides:
        count = lax.axis_size(axis)
        odd = lax.axis_index(axis) % 2 == 1
        head = lax.slice_in_dim(cells, 0, width, axis=dim)
        tail = lax.slice_in_dim(cells, cells.shape[dim] - width, cells.shape[dim], axis=dim)
        inner = lax.ppermute(jnp.where(odd, head, tail), axis, [(i, i ^ 1) for i in range(count)])
        outer = lax.ppermute(
            jnp.where(odd, tail, head),
            axis,
            [pair for k in range(1, count - 1, 2) for pair in ((k, k + 1), (k + 1, k))],
        )
        cells = jnp.concatenate(
            [jnp.where(odd, inner, outer), cells, jnp.where(odd, outer, inner)], axis=dim
        )
    return cells


def exchange(value, axis, bit):
    size = lax.axis_size(axis)
    return lax.ppermute(value, axis, [(i, i ^ bit) for i in range(size)])


def swap_with(value, axis, bit, extra):
    size = value.shape[0]
    lanes = value.shape[1]
    both = exchange(
        jnp.concatenate([value, extra.astype(value.dtype).reshape(-1, lanes)]), axis, bit
    )
    return both[:size], both[size:].reshape(extra.shape).astype(extra.dtype)


def halo_ends(cells, axis, dim):
    odd = lax.axis_index(axis) % 2 == 1
    head = lax.slice_in_dim(cells, 0, 1, axis=dim)
    tail = lax.slice_in_dim(cells, cells.shape[dim] - 1, cells.shape[dim], axis=dim)
    return odd, jnp.where(odd, head, tail), jnp.where(odd, tail, head)


def outer_swap(piece, axis):
    count = lax.axis_size(axis)
    return lax.ppermute(
        piece, axis, [pair for k in range(1, count - 1, 2) for pair in ((k, k + 1), (k + 1, k))]
    )


def halo_join(cells, odd, inner, outer, dim):
    return jnp.concatenate(
        [jnp.where(odd, inner, outer), cells, jnp.where(odd, outer, inner)], axis=dim
    )


def butterfly_sum(flat, cells, halvings=2):
    steps = []
    for axis in ("col", "row"):
        bit = 1
        while bit < lax.axis_size(axis):
            steps.append((axis, bit))
            bit *= 2
    for axis, bit in steps[:halvings]:
        upper = (lax.axis_index(axis) // bit) % 2 == 1
        half = flat.shape[0] // 2
        low, high = flat[:half], flat[half:]
        keep = jnp.where(upper, high, low)
        give = jnp.where(upper, low, high)
        if (axis, bit) == ("col", 1):
            odd, inner_piece, outer_piece = halo_ends(cells, "col", 1)
            outer = outer_swap(outer_piece, "col")
            got, inner = swap_with(give, axis, bit, inner_piece)
            cells = halo_join(cells, odd, inner, outer, 1)
        else:
            got = exchange(give, axis, bit)
        flat = keep + got
    for axis, bit in steps[halvings:]:
        if (axis, bit) == ("row", 1):
            odd, inner_piece, outer_piece = halo_ends(cells, "row", 0)
            outer = outer_swap(outer_piece, "row")
            got, inner = swap_with(flat, axis, bit, inner_piece)
            cells = halo_join(cells, odd, inner, outer, 0)
        else:
            got = exchange(flat, axis, bit)
        flat = flat + got
    for axis, bit in reversed(steps[:halvings]):
        upper = (lax.axis_index(axis) // bit) % 2 == 1
        other = exchange(flat, axis, bit)
        flat = jnp.where(upper, jnp.concatenate([other, flat]), jnp.concatenate([flat, other]))
    return flat, cells


def silu_slope(value):
    sig = jax.nn.sigmoid(value)
    return sig * (1.0 + value * (1.0 - sig))


def spatial_forward(padded, conv_weight, tile_rows, tile_cols):
    running_sum = None
    for row_tap in range(3):
        tap_patch = jnp.concatenate(
            [
                padded[row_tap : row_tap + tile_rows, col_tap : col_tap + tile_cols]
                for col_tap in range(3)
            ],
            axis=-1,
        )
        tap_term = jnp.dot(
            tap_patch,
            conv_weight[row_tap].reshape(3 * C_IN, C_OUT),
            preferred_element_type=jnp.float32,
        )
        running_sum = tap_term if running_sum is None else running_sum + tap_term
    return running_sum


def window_conv(padded, kernel):
    return lax.conv_general_dilated(
        padded,
        kernel,
        window_strides=(1, 1),
        padding="VALID",
        dimension_numbers=("HWNC", "HWIO", "HWNC"),
        preferred_element_type=jnp.float32,
    )


def transposed_conv(padded_grad, conv_weight, out_rows, out_cols):
    input_sum = None
    for row_tap in range(3):
        grad_patch = jnp.concatenate(
            [
                padded_grad[
                    2 - row_tap : 2 - row_tap + out_rows, 2 - col_tap : 2 - col_tap + out_cols
                ]
                for col_tap in range(3)
            ],
            axis=-1,
        )
        flipped = jnp.concatenate([conv_weight[row_tap, col_tap].T for col_tap in range(3)], axis=0)
        tap_term = jnp.dot(grad_patch, flipped, preferred_element_type=jnp.float32)
        input_sum = tap_term if input_sum is None else input_sum + tap_term
    return input_sum


def same_group():
    rows = lax.broadcasted_iota(jnp.int32, (C_OUT, C_OUT), 0) // CPG
    cols = lax.broadcasted_iota(jnp.int32, (C_OUT, C_OUT), 1) // CPG
    return rows == cols


def block_weights(time_weight):
    tiled = jnp.tile(time_weight.reshape(3, C_OUT, CPG), (1, 1, GROUPS))
    return jnp.where(same_group()[None], tiled, jnp.zeros_like(tiled))


def group_blocks(dense):
    masked = jnp.where(same_group()[None], dense, jnp.zeros_like(dense))
    pick = (
        lax.broadcasted_iota(jnp.int32, (C_OUT, CPG), 0) % CPG
        == lax.broadcasted_iota(jnp.int32, (C_OUT, CPG), 1)
    ).astype(jnp.float32)
    return jnp.dot(masked, pick, precision=PRECISE).reshape(3, GROUPS, CPG, CPG)


def per_device(
    pixels, conv_weight, time_weight, class_weight, pixel_slot, straddle_dir, straddle_slot, labels
):
    tile_rows, tile_cols = (pixels.shape[0], pixels.shape[1])
    slot_count = P_OWN + S_STR
    padded_pixels = with_halo(pixels, (("row", 0), ("col", 1)), 1).reshape(
        tile_rows + 2, tile_cols + 2, DATES, C_IN
    )
    pre_act = window_conv(padded_pixels, conv_weight)
    hidden = jax.nn.silu(pre_act).astype(jnp.bfloat16)
    dense_time = block_weights(time_weight)
    padded_hidden = jnp.pad(hidden, ((0, 0), (0, 0), (1, 1), (0, 0)))
    mixed_time = None
    for time_tap in range(3):
        tap_term = jnp.dot(
            padded_hidden[:, :, time_tap : time_tap + DATES],
            dense_time[time_tap],
            preferred_element_type=jnp.float32,
        )
        mixed_time = tap_term if mixed_time is None else mixed_time + tap_term
    embedded = (
        jnp.mean(jax.nn.silu(mixed_time), axis=2)
        .astype(jnp.bfloat16)
        .reshape(tile_rows * tile_cols, C_OUT)
    )
    flat_slot = pixel_slot.reshape(tile_rows * tile_cols)
    membership = (jnp.arange(slot_count, dtype=jnp.int32)[:, None] == flat_slot[None, :]).astype(
        jnp.bfloat16
    )
    partial_value = jnp.dot(membership, embedded, preferred_element_type=jnp.float32)
    direction = straddle_dir.reshape(S_STR)
    owner_slot = straddle_slot.reshape(S_STR)
    own_slots = jnp.arange(P_OWN, dtype=jnp.int32)
    target = jnp.concatenate([4 * P_OWN + own_slots, direction * P_OWN + owner_slot])
    select = (jnp.arange(9 * P_OWN, dtype=jnp.int32)[:, None] == target[None, :]).astype(
        jnp.float32
    )
    outgoing = jnp.dot(select, partial_value, precision=PRECISE).reshape(3, 3, P_OWN, C_OUT)
    border = with_halo(outgoing.astype(jnp.bfloat16), (("row", 0), ("col", 1)), 1).astype(
        outgoing.dtype
    )
    parcel_sums = jnp.sum(border[0::2, 0::2], axis=(0, 1))
    centered = parcel_sums - jnp.mean(parcel_sums, axis=-1, keepdims=True)
    variance = jnp.mean(centered * centered, axis=-1, keepdims=True)
    inverse = lax.rsqrt(variance + EPSILON)
    normed = centered * inverse
    rounded = normed.astype(jnp.bfloat16)
    logits = jnp.dot(rounded, class_weight, preferred_element_type=jnp.float32)
    exp_logits = jnp.exp(logits)
    probability = exp_logits / jnp.sum(exp_logits, axis=-1, keepdims=True)
    label_hot = (
        labels.reshape(P_OWN)[:, None] == jnp.arange(CLASSES, dtype=jnp.int32)[None, :]
    ).astype(jnp.float32)
    parcel_total = P_OWN * lax.axis_size("row") * lax.axis_size("col")
    grad_logits = (probability - label_hot) / parcel_total
    class_term = jnp.dot(rounded.astype(jnp.float32).T, grad_logits, precision=PRECISE)
    grad_normed = jnp.dot(grad_logits, class_weight.astype(jnp.float32).T, precision=PRECISE)
    parcel_grad = (
        inverse
        * (
            grad_normed
            - jnp.mean(grad_normed, axis=-1, keepdims=True)
            - normed * jnp.mean(grad_normed * normed, axis=-1, keepdims=True)
        )
    ).astype(jnp.bfloat16)
    beside_all = with_halo(
        parcel_grad.reshape(1, 1, P_OWN, C_OUT), (("row", 0), ("col", 1)), 1
    ).reshape(9 * P_OWN, C_OUT)
    picker = (target[:, None] == jnp.arange(9 * P_OWN, dtype=jnp.int32)[None, :]).astype(
        jnp.bfloat16
    )
    slot_grad = jnp.dot(picker, beside_all, preferred_element_type=jnp.float32).astype(jnp.bfloat16)
    pixel_grad = jnp.dot(membership.T, slot_grad, preferred_element_type=jnp.float32).reshape(
        tile_rows, tile_cols, C_OUT
    )
    grad_mixed = ((pixel_grad / DATES)[:, :, None, :] * silu_slope(mixed_time)).astype(jnp.bfloat16)
    time_term = group_blocks(
        jnp.stack(
            [
                jnp.einsum(
                    "ijtc,ijtd->cd",
                    padded_hidden[:, :, time_tap : time_tap + DATES],
                    grad_mixed,
                    preferred_element_type=jnp.float32,
                )
                for time_tap in range(3)
            ]
        )
    )
    padded_mixed = jnp.pad(grad_mixed, ((0, 0), (0, 0), (1, 1), (0, 0)))
    grad_hidden = None
    for time_tap in range(3):
        tap_term = jnp.dot(
            padded_mixed[:, :, 2 - time_tap : 2 - time_tap + DATES],
            dense_time[time_tap].T,
            preferred_element_type=jnp.float32,
        )
        grad_hidden = tap_term if grad_hidden is None else grad_hidden + tap_term
    grad_pre = (grad_hidden * silu_slope(pre_act)).astype(jnp.bfloat16)
    conv_term = lax.conv_general_dilated(
        padded_pixels,
        grad_pre,
        window_strides=(1, 1),
        padding="VALID",
        dimension_numbers=("HWCN", "HWIO", "HWNC"),
        preferred_element_type=jnp.float32,
    )
    lanes = C_OUT
    conv_rows, time_rows, class_rows = (
        conv_term.size // lanes,
        time_term.size // lanes,
        class_term.size // lanes,
    )
    used = conv_rows + time_rows + class_rows
    total = -(-used // 32) * 32
    flat, padded_grad = butterfly_sum(
        jnp.concatenate(
            [
                conv_term.reshape(conv_rows, lanes),
                time_term.reshape(time_rows, lanes),
                class_term.reshape(class_rows, lanes),
                jnp.zeros((total - used, lanes), jnp.float32),
            ]
        ),
        grad_pre.reshape(tile_rows, tile_cols, DATES * C_OUT),
    )
    padded_grad = padded_grad.reshape(tile_rows + 2, tile_cols + 2, DATES, C_OUT)
    input_sum = transposed_conv(padded_grad, conv_weight, tile_rows, tile_cols)
    input_grad = input_sum.astype(jnp.bfloat16).reshape(tile_rows, tile_cols, DATES * C_IN)
    conv_grad = flat[:conv_rows].reshape(conv_term.shape)
    time_grad = flat[conv_rows : conv_rows + time_rows].reshape(time_term.shape)
    class_grad = flat[conv_rows + time_rows : used].reshape(class_term.shape)
    return (input_grad, conv_grad, time_grad, class_grad)


def solution(mesh):
    in_specs = (
        P("row", "col", None),
        P(),
        P(),
        P(),
        P("row", "col"),
        P("row", "col", None),
        P("row", "col", None),
        P("row", "col", None),
    )
    out_specs = (P("row", "col", None), P(), P(), P())
    return jax.shard_map(
        per_device, mesh=mesh, in_specs=in_specs, out_specs=out_specs, check_vma=False
    )
```

```python
import jax
import jax.numpy as jnp
from jax import lax
from jax.sharding import PartitionSpec as P

DATES = 12
C_IN = 64
C_OUT = 128
GROUPS = 16
CLASSES = 20
P_OWN = 32
S_STR = 32
CPG = 8


EPSILON = 1e-05
PRECISE = lax.Precision.HIGHEST


def with_halo(cells, sides, width):
    for axis, dim in sides:
        count = lax.axis_size(axis)
        odd = lax.axis_index(axis) % 2 == 1
        head = lax.slice_in_dim(cells, 0, width, axis=dim)
        tail = lax.slice_in_dim(cells, cells.shape[dim] - width, cells.shape[dim], axis=dim)
        inner = lax.ppermute(jnp.where(odd, head, tail), axis, [(i, i ^ 1) for i in range(count)])
        outer = lax.ppermute(
            jnp.where(odd, tail, head),
            axis,
            [pair for k in range(1, count - 1, 2) for pair in ((k, k + 1), (k + 1, k))],
        )
        cells = jnp.concatenate(
            [jnp.where(odd, inner, outer), cells, jnp.where(odd, outer, inner)], axis=dim
        )
    return cells


def exchange(value, axis, bit):
    size = lax.axis_size(axis)
    return lax.ppermute(value, axis, [(i, i ^ bit) for i in range(size)])


def swap_with(value, axis, bit, extra):
    size = value.shape[0]
    lanes = value.shape[1]
    both = exchange(
        jnp.concatenate([value, extra.astype(value.dtype).reshape(-1, lanes)]), axis, bit
    )
    return both[:size], both[size:].reshape(extra.shape).astype(extra.dtype)


def halo_ends(cells, axis, dim):
    odd = lax.axis_index(axis) % 2 == 1
    head = lax.slice_in_dim(cells, 0, 1, axis=dim)
    tail = lax.slice_in_dim(cells, cells.shape[dim] - 1, cells.shape[dim], axis=dim)
    return odd, jnp.where(odd, head, tail), jnp.where(odd, tail, head)


def outer_swap(piece, axis):
    count = lax.axis_size(axis)
    return lax.ppermute(
        piece, axis, [pair for k in range(1, count - 1, 2) for pair in ((k, k + 1), (k + 1, k))]
    )


def halo_join(cells, odd, inner, outer, dim):
    return jnp.concatenate(
        [jnp.where(odd, inner, outer), cells, jnp.where(odd, outer, inner)], axis=dim
    )


def butterfly_sum(flat, cells, halvings=2):
    steps = []
    for axis in ("col", "row"):
        bit = 1
        while bit < lax.axis_size(axis):
            steps.append((axis, bit))
            bit *= 2
    for axis, bit in steps[:halvings]:
        upper = (lax.axis_index(axis) // bit) % 2 == 1
        half = flat.shape[0] // 2
        low, high = flat[:half], flat[half:]
        keep = jnp.where(upper, high, low)
        give = jnp.where(upper, low, high)
        if (axis, bit) == ("col", 1):
            odd, inner_piece, outer_piece = halo_ends(cells, "col", 1)
            outer = outer_swap(outer_piece, "col")
            got, inner = swap_with(give, axis, bit, inner_piece)
            cells = halo_join(cells, odd, inner, outer, 1)
        else:
            got = exchange(give, axis, bit)
        flat = keep + got
    for axis, bit in steps[halvings:]:
        if (axis, bit) == ("row", 1):
            odd, inner_piece, outer_piece = halo_ends(cells, "row", 0)
            outer = outer_swap(outer_piece, "row")
            got, inner = swap_with(flat, axis, bit, inner_piece)
            cells = halo_join(cells, odd, inner, outer, 0)
        else:
            got = exchange(flat, axis, bit)
        flat = flat + got
    for axis, bit in reversed(steps[:halvings]):
        upper = (lax.axis_index(axis) // bit) % 2 == 1
        other = exchange(flat, axis, bit)
        flat = jnp.where(upper, jnp.concatenate([other, flat]), jnp.concatenate([flat, other]))
    return flat, cells


def silu_slope(value):
    sig = jax.nn.sigmoid(value)
    return sig * (1.0 + value * (1.0 - sig))


def spatial_forward(padded, conv_weight, tile_rows, tile_cols):
    running_sum = None
    for row_tap in range(3):
        tap_patch = jnp.concatenate(
            [
                padded[row_tap : row_tap + tile_rows, col_tap : col_tap + tile_cols]
                for col_tap in range(3)
            ],
            axis=-1,
        )
        tap_term = jnp.dot(
            tap_patch,
            conv_weight[row_tap].reshape(3 * C_IN, C_OUT),
            preferred_element_type=jnp.float32,
        )
        running_sum = tap_term if running_sum is None else running_sum + tap_term
    return running_sum


def window_conv(padded, kernel):
    return lax.conv_general_dilated(
        padded,
        kernel,
        window_strides=(1, 1),
        padding="VALID",
        dimension_numbers=("HWNC", "HWIO", "HWNC"),
        preferred_element_type=jnp.float32,
    )


def transposed_conv(padded_grad, conv_weight, out_rows, out_cols):
    input_sum = None
    for row_tap in range(3):
        grad_patch = jnp.concatenate(
            [
                padded_grad[
                    2 - row_tap : 2 - row_tap + out_rows, 2 - col_tap : 2 - col_tap + out_cols
                ]
                for col_tap in range(3)
            ],
            axis=-1,
        )
        flipped = jnp.concatenate([conv_weight[row_tap, col_tap].T for col_tap in range(3)], axis=0)
        tap_term = jnp.dot(grad_patch, flipped, preferred_element_type=jnp.float32)
        input_sum = tap_term if input_sum is None else input_sum + tap_term
    return input_sum


def same_group():
    rows = lax.broadcasted_iota(jnp.int32, (C_OUT, C_OUT), 0) // CPG
    cols = lax.broadcasted_iota(jnp.int32, (C_OUT, C_OUT), 1) // CPG
    return rows == cols


def block_weights(time_weight):
    tiled = jnp.tile(time_weight.reshape(3, C_OUT, CPG), (1, 1, GROUPS))
    return jnp.where(same_group()[None], tiled, jnp.zeros_like(tiled))


def group_blocks(dense):
    masked = jnp.where(same_group()[None], dense, jnp.zeros_like(dense))
    pick = (
        lax.broadcasted_iota(jnp.int32, (C_OUT, CPG), 0) % CPG
        == lax.broadcasted_iota(jnp.int32, (C_OUT, CPG), 1)
    ).astype(jnp.float32)
    return jnp.dot(masked, pick, precision=PRECISE).reshape(3, GROUPS, CPG, CPG)


def per_device(
    pixels, conv_weight, time_weight, class_weight, pixel_slot, straddle_dir, straddle_slot, labels
):
    tile_rows, tile_cols = (pixels.shape[0], pixels.shape[1])
    slot_count = P_OWN + S_STR
    padded_pixels = with_halo(pixels, (("row", 0), ("col", 1)), 1).reshape(
        tile_rows + 2, tile_cols + 2, DATES, C_IN
    )
    pre_act = window_conv(padded_pixels, conv_weight)
    hidden = jax.nn.silu(pre_act).astype(jnp.bfloat16)
    dense_time = block_weights(time_weight)
    padded_hidden = jnp.pad(hidden, ((0, 0), (0, 0), (1, 1), (0, 0)))
    mixed_time = None
    for time_tap in range(3):
        tap_term = jnp.dot(
            padded_hidden[:, :, time_tap : time_tap + DATES],
            dense_time[time_tap],
            preferred_element_type=jnp.float32,
        )
        mixed_time = tap_term if mixed_time is None else mixed_time + tap_term
    embedded = (
        jnp.mean(jax.nn.silu(mixed_time), axis=2)
        .astype(jnp.bfloat16)
        .reshape(tile_rows * tile_cols, C_OUT)
    )
    flat_slot = pixel_slot.reshape(tile_rows * tile_cols)
    membership = (jnp.arange(slot_count, dtype=jnp.int32)[:, None] == flat_slot[None, :]).astype(
        jnp.bfloat16
    )
    partial_value = jnp.dot(membership, embedded, preferred_element_type=jnp.float32)
    direction = straddle_dir.reshape(S_STR)
    owner_slot = straddle_slot.reshape(S_STR)
    own_slots = jnp.arange(P_OWN, dtype=jnp.int32)
    target = jnp.concatenate([4 * P_OWN + own_slots, direction * P_OWN + owner_slot])
    select = (jnp.arange(9 * P_OWN, dtype=jnp.int32)[:, None] == target[None, :]).astype(
        jnp.float32
    )
    outgoing = jnp.dot(select, partial_value, precision=PRECISE).reshape(3, 3, P_OWN, C_OUT)
    border = with_halo(outgoing.astype(jnp.bfloat16), (("row", 0), ("col", 1)), 1).astype(
        outgoing.dtype
    )
    parcel_sums = jnp.sum(border[0::2, 0::2], axis=(0, 1))
    centered = parcel_sums - jnp.mean(parcel_sums, axis=-1, keepdims=True)
    variance = jnp.mean(centered * centered, axis=-1, keepdims=True)
    inverse = lax.rsqrt(variance + EPSILON)
    normed = centered * inverse
    rounded = normed.astype(jnp.bfloat16)
    logits = jnp.dot(rounded, class_weight, preferred_element_type=jnp.float32)
    exp_logits = jnp.exp(logits)
    probability = exp_logits / jnp.sum(exp_logits, axis=-1, keepdims=True)
    label_hot = (
        labels.reshape(P_OWN)[:, None] == jnp.arange(CLASSES, dtype=jnp.int32)[None, :]
    ).astype(jnp.float32)
    parcel_total = P_OWN * lax.axis_size("row") * lax.axis_size("col")
    grad_logits = (probability - label_hot) / parcel_total
    class_term = jnp.dot(rounded.astype(jnp.float32).T, grad_logits, precision=PRECISE)
    grad_normed = jnp.dot(grad_logits, class_weight.astype(jnp.float32).T, precision=PRECISE)
    parcel_grad = (
        inverse
        * (
            grad_normed
            - jnp.mean(grad_normed, axis=-1, keepdims=True)
            - normed * jnp.mean(grad_normed * normed, axis=-1, keepdims=True)
        )
    ).astype(jnp.bfloat16)
    beside_all = with_halo(
        parcel_grad.reshape(1, 1, P_OWN, C_OUT), (("row", 0), ("col", 1)), 1
    ).reshape(9 * P_OWN, C_OUT)
    picker = (target[:, None] == jnp.arange(9 * P_OWN, dtype=jnp.int32)[None, :]).astype(
        jnp.bfloat16
    )
    slot_grad = jnp.dot(picker, beside_all, preferred_element_type=jnp.float32).astype(jnp.bfloat16)
    pixel_grad = jnp.dot(membership.T, slot_grad, preferred_element_type=jnp.float32).reshape(
        tile_rows, tile_cols, C_OUT
    )
    grad_mixed = ((pixel_grad / DATES)[:, :, None, :] * silu_slope(mixed_time)).astype(jnp.bfloat16)
    time_term = group_blocks(
        jnp.stack(
            [
                jnp.einsum(
                    "ijtc,ijtd->cd",
                    padded_hidden[:, :, time_tap : time_tap + DATES],
                    grad_mixed,
                    preferred_element_type=jnp.float32,
                )
                for time_tap in range(3)
            ]
        )
    )
    padded_mixed = jnp.pad(grad_mixed, ((0, 0), (0, 0), (1, 1), (0, 0)))
    grad_hidden = None
    for time_tap in range(3):
        tap_term = jnp.dot(
            padded_mixed[:, :, 2 - time_tap : 2 - time_tap + DATES],
            dense_time[time_tap].T,
            preferred_element_type=jnp.float32,
        )
        grad_hidden = tap_term if grad_hidden is None else grad_hidden + tap_term
    grad_pre = (grad_hidden * silu_slope(pre_act)).astype(jnp.bfloat16)
    conv_term = lax.conv_general_dilated(
        padded_pixels,
        grad_pre,
        window_strides=(1, 1),
        padding="VALID",
        dimension_numbers=("HWCN", "HWIO", "HWNC"),
        preferred_element_type=jnp.float32,
    )
    lanes = C_OUT
    conv_rows, time_rows, class_rows = (
        conv_term.size // lanes,
        time_term.size // lanes,
        class_term.size // lanes,
    )
    used = conv_rows + time_rows + class_rows
    total = -(-used // 32) * 32
    flat, padded_grad = butterfly_sum(
        jnp.concatenate(
            [
                conv_term.reshape(conv_rows, lanes),
                time_term.reshape(time_rows, lanes),
                class_term.reshape(class_rows, lanes),
                jnp.zeros((total - used, lanes), jnp.float32),
            ]
        ),
        grad_pre.reshape(tile_rows, tile_cols, DATES * C_OUT),
    )
    padded_grad = padded_grad.reshape(tile_rows + 2, tile_cols + 2, DATES, C_OUT)
    input_sum = window_conv(padded_grad, jnp.swapaxes(conv_weight[::-1, ::-1], 2, 3))
    input_grad = input_sum.astype(jnp.bfloat16).reshape(tile_rows, tile_cols, DATES * C_IN)
    conv_grad = flat[:conv_rows].reshape(conv_term.shape)
    time_grad = flat[conv_rows : conv_rows + time_rows].reshape(time_term.shape)
    class_grad = flat[conv_rows + time_rows : used].reshape(class_term.shape)
    return (input_grad, conv_grad, time_grad, class_grad)


def solution(mesh):
    in_specs = (
        P("row", "col", None),
        P(),
        P(),
        P(),
        P("row", "col"),
        P("row", "col", None),
        P("row", "col", None),
        P("row", "col", None),
    )
    out_specs = (P("row", "col", None), P(), P(), P())
    return jax.shard_map(
        per_device, mesh=mesh, in_specs=in_specs, out_specs=out_specs, check_vma=False
    )
```

```python
import jax
import jax.numpy as jnp
from jax import lax
from jax.sharding import PartitionSpec as P

DATES = 12
C_IN = 64
C_OUT = 128
GROUPS = 16
CLASSES = 20
P_OWN = 32
S_STR = 32
CPG = 8


EPSILON = 1e-05
PRECISE = lax.Precision.HIGHEST


def with_halo(cells, sides, width):
    for axis, dim in sides:
        count = lax.axis_size(axis)
        odd = lax.axis_index(axis) % 2 == 1
        head = lax.slice_in_dim(cells, 0, width, axis=dim)
        tail = lax.slice_in_dim(cells, cells.shape[dim] - width, cells.shape[dim], axis=dim)
        inner = lax.ppermute(jnp.where(odd, head, tail), axis, [(i, i ^ 1) for i in range(count)])
        outer = lax.ppermute(
            jnp.where(odd, tail, head),
            axis,
            [pair for k in range(1, count - 1, 2) for pair in ((k, k + 1), (k + 1, k))],
        )
        cells = jnp.concatenate(
            [jnp.where(odd, inner, outer), cells, jnp.where(odd, outer, inner)], axis=dim
        )
    return cells


def exchange(value, axis, bit):
    size = lax.axis_size(axis)
    return lax.ppermute(value, axis, [(i, i ^ bit) for i in range(size)])


def swap_with(value, axis, bit, extra):
    size = value.shape[0]
    lanes = value.shape[1]
    both = exchange(
        jnp.concatenate([value, extra.astype(value.dtype).reshape(-1, lanes)]), axis, bit
    )
    return both[:size], both[size:].reshape(extra.shape).astype(extra.dtype)


def halo_ends(cells, axis, dim):
    odd = lax.axis_index(axis) % 2 == 1
    head = lax.slice_in_dim(cells, 0, 1, axis=dim)
    tail = lax.slice_in_dim(cells, cells.shape[dim] - 1, cells.shape[dim], axis=dim)
    return odd, jnp.where(odd, head, tail), jnp.where(odd, tail, head)


def outer_swap(piece, axis):
    count = lax.axis_size(axis)
    return lax.ppermute(
        piece, axis, [pair for k in range(1, count - 1, 2) for pair in ((k, k + 1), (k + 1, k))]
    )


def halo_join(cells, odd, inner, outer, dim):
    return jnp.concatenate(
        [jnp.where(odd, inner, outer), cells, jnp.where(odd, outer, inner)], axis=dim
    )


def butterfly_sum(flat, cells, halvings=2):
    steps = []
    for axis in ("col", "row"):
        bit = 1
        while bit < lax.axis_size(axis):
            steps.append((axis, bit))
            bit *= 2
    for axis, bit in steps[:halvings]:
        upper = (lax.axis_index(axis) // bit) % 2 == 1
        half = flat.shape[0] // 2
        low, high = flat[:half], flat[half:]
        keep = jnp.where(upper, high, low)
        give = jnp.where(upper, low, high)
        if (axis, bit) == ("col", 1):
            odd, inner_piece, outer_piece = halo_ends(cells, "col", 1)
            outer = outer_swap(outer_piece, "col")
            got, inner = swap_with(give, axis, bit, inner_piece)
            cells = halo_join(cells, odd, inner, outer, 1)
        else:
            got = exchange(give, axis, bit)
        flat = keep + got
    for axis, bit in steps[halvings:]:
        if (axis, bit) == ("row", 1):
            odd, inner_piece, outer_piece = halo_ends(cells, "row", 0)
            outer = outer_swap(outer_piece, "row")
            got, inner = swap_with(flat, axis, bit, inner_piece)
            cells = halo_join(cells, odd, inner, outer, 0)
        else:
            got = exchange(flat, axis, bit)
        flat = flat + got
    for axis, bit in reversed(steps[1:halvings]):
        upper = (lax.axis_index(axis) // bit) % 2 == 1
        other = exchange(flat, axis, bit)
        flat = jnp.where(upper, jnp.concatenate([other, flat]), jnp.concatenate([flat, other]))
    axis, bit = steps[0]
    upper = (lax.axis_index(axis) // bit) % 2 == 1
    other = exchange(flat, axis, bit)
    return (jnp.where(upper, other, flat), jnp.where(upper, flat, other)), cells


def silu_slope(value):
    sig = jax.nn.sigmoid(value)
    return sig * (1.0 + value * (1.0 - sig))


def spatial_forward(padded, conv_weight, tile_rows, tile_cols):
    running_sum = None
    for row_tap in range(3):
        tap_patch = jnp.concatenate(
            [
                padded[row_tap : row_tap + tile_rows, col_tap : col_tap + tile_cols]
                for col_tap in range(3)
            ],
            axis=-1,
        )
        tap_term = jnp.dot(
            tap_patch,
            conv_weight[row_tap].reshape(3 * C_IN, C_OUT),
            preferred_element_type=jnp.float32,
        )
        running_sum = tap_term if running_sum is None else running_sum + tap_term
    return running_sum


def window_conv(padded, kernel):
    return lax.conv_general_dilated(
        padded,
        kernel,
        window_strides=(1, 1),
        padding="VALID",
        dimension_numbers=("HWNC", "HWIO", "HWNC"),
        preferred_element_type=jnp.float32,
    )


def transposed_conv(padded_grad, conv_weight, out_rows, out_cols):
    input_sum = None
    for row_tap in range(3):
        grad_patch = jnp.concatenate(
            [
                padded_grad[
                    2 - row_tap : 2 - row_tap + out_rows, 2 - col_tap : 2 - col_tap + out_cols
                ]
                for col_tap in range(3)
            ],
            axis=-1,
        )
        flipped = jnp.concatenate([conv_weight[row_tap, col_tap].T for col_tap in range(3)], axis=0)
        tap_term = jnp.dot(grad_patch, flipped, preferred_element_type=jnp.float32)
        input_sum = tap_term if input_sum is None else input_sum + tap_term
    return input_sum


def same_group():
    rows = lax.broadcasted_iota(jnp.int32, (C_OUT, C_OUT), 0) // CPG
    cols = lax.broadcasted_iota(jnp.int32, (C_OUT, C_OUT), 1) // CPG
    return rows == cols


def block_weights(time_weight):
    tiled = jnp.tile(time_weight.reshape(3, C_OUT, CPG), (1, 1, GROUPS))
    return jnp.where(same_group()[None], tiled, jnp.zeros_like(tiled))


def group_blocks(dense):
    masked = jnp.where(same_group()[None], dense, jnp.zeros_like(dense))
    pick = (
        lax.broadcasted_iota(jnp.int32, (C_OUT, CPG), 0) % CPG
        == lax.broadcasted_iota(jnp.int32, (C_OUT, CPG), 1)
    ).astype(jnp.float32)
    return jnp.dot(masked, pick, precision=PRECISE).reshape(3, GROUPS, CPG, CPG)


def per_device(
    pixels, conv_weight, time_weight, class_weight, pixel_slot, straddle_dir, straddle_slot, labels
):
    tile_rows, tile_cols = (pixels.shape[0], pixels.shape[1])
    slot_count = P_OWN + S_STR
    padded_pixels = with_halo(pixels, (("row", 0), ("col", 1)), 1).reshape(
        tile_rows + 2, tile_cols + 2, DATES, C_IN
    )
    pre_act = window_conv(padded_pixels, conv_weight)
    hidden = jax.nn.silu(pre_act).astype(jnp.bfloat16)
    dense_time = block_weights(time_weight)
    padded_hidden = jnp.pad(hidden, ((0, 0), (0, 0), (1, 1), (0, 0)))
    mixed_time = None
    for time_tap in range(3):
        tap_term = jnp.dot(
            padded_hidden[:, :, time_tap : time_tap + DATES],
            dense_time[time_tap],
            preferred_element_type=jnp.float32,
        )
        mixed_time = tap_term if mixed_time is None else mixed_time + tap_term
    embedded = (
        jnp.mean(jax.nn.silu(mixed_time), axis=2)
        .astype(jnp.bfloat16)
        .reshape(tile_rows * tile_cols, C_OUT)
    )
    flat_slot = pixel_slot.reshape(tile_rows * tile_cols)
    membership = (jnp.arange(slot_count, dtype=jnp.int32)[:, None] == flat_slot[None, :]).astype(
        jnp.bfloat16
    )
    partial_value = jnp.dot(membership, embedded, preferred_element_type=jnp.float32)
    direction = straddle_dir.reshape(S_STR)
    owner_slot = straddle_slot.reshape(S_STR)
    own_slots = jnp.arange(P_OWN, dtype=jnp.int32)
    target = jnp.concatenate([4 * P_OWN + own_slots, direction * P_OWN + owner_slot])
    select = (jnp.arange(9 * P_OWN, dtype=jnp.int32)[:, None] == target[None, :]).astype(
        jnp.float32
    )
    outgoing = jnp.dot(select, partial_value, precision=PRECISE).reshape(3, 3, P_OWN, C_OUT)
    border = with_halo(outgoing.astype(jnp.bfloat16), (("row", 0), ("col", 1)), 1).astype(
        outgoing.dtype
    )
    parcel_sums = jnp.sum(border[0::2, 0::2], axis=(0, 1))
    centered = parcel_sums - jnp.mean(parcel_sums, axis=-1, keepdims=True)
    variance = jnp.mean(centered * centered, axis=-1, keepdims=True)
    inverse = lax.rsqrt(variance + EPSILON)
    normed = centered * inverse
    rounded = normed.astype(jnp.bfloat16)
    logits = jnp.dot(rounded, class_weight, preferred_element_type=jnp.float32)
    exp_logits = jnp.exp(logits)
    probability = exp_logits / jnp.sum(exp_logits, axis=-1, keepdims=True)
    label_hot = (
        labels.reshape(P_OWN)[:, None] == jnp.arange(CLASSES, dtype=jnp.int32)[None, :]
    ).astype(jnp.float32)
    parcel_total = P_OWN * lax.axis_size("row") * lax.axis_size("col")
    grad_logits = (probability - label_hot) / parcel_total
    class_term = jnp.dot(rounded.astype(jnp.float32).T, grad_logits, precision=PRECISE)
    grad_normed = jnp.dot(grad_logits, class_weight.astype(jnp.float32).T, precision=PRECISE)
    parcel_grad = (
        inverse
        * (
            grad_normed
            - jnp.mean(grad_normed, axis=-1, keepdims=True)
            - normed * jnp.mean(grad_normed * normed, axis=-1, keepdims=True)
        )
    ).astype(jnp.bfloat16)
    beside_all = with_halo(
        parcel_grad.reshape(1, 1, P_OWN, C_OUT), (("row", 0), ("col", 1)), 1
    ).reshape(9 * P_OWN, C_OUT)
    picker = (target[:, None] == jnp.arange(9 * P_OWN, dtype=jnp.int32)[None, :]).astype(
        jnp.bfloat16
    )
    slot_grad = jnp.dot(picker, beside_all, preferred_element_type=jnp.float32).astype(jnp.bfloat16)
    pixel_grad = jnp.dot(membership.T, slot_grad, preferred_element_type=jnp.float32).reshape(
        tile_rows, tile_cols, C_OUT
    )
    grad_mixed = ((pixel_grad / DATES)[:, :, None, :] * silu_slope(mixed_time)).astype(jnp.bfloat16)
    time_term = group_blocks(
        jnp.stack(
            [
                jnp.einsum(
                    "ijtc,ijtd->cd",
                    padded_hidden[:, :, time_tap : time_tap + DATES],
                    grad_mixed,
                    preferred_element_type=jnp.float32,
                )
                for time_tap in range(3)
            ]
        )
    )
    padded_mixed = jnp.pad(grad_mixed, ((0, 0), (0, 0), (1, 1), (0, 0)))
    grad_hidden = None
    for time_tap in range(3):
        tap_term = jnp.dot(
            padded_mixed[:, :, 2 - time_tap : 2 - time_tap + DATES],
            dense_time[time_tap].T,
            preferred_element_type=jnp.float32,
        )
        grad_hidden = tap_term if grad_hidden is None else grad_hidden + tap_term
    grad_pre = (grad_hidden * silu_slope(pre_act)).astype(jnp.bfloat16)
    conv_term = lax.conv_general_dilated(
        padded_pixels,
        grad_pre,
        window_strides=(1, 1),
        padding="VALID",
        dimension_numbers=("HWCN", "HWIO", "HWNC"),
        preferred_element_type=jnp.float32,
    )
    lanes = C_OUT
    conv_rows, time_rows, class_rows = (
        conv_term.size // lanes,
        time_term.size // lanes,
        class_term.size // lanes,
    )
    used = conv_rows + time_rows + class_rows
    total = -(-used // 32) * 32
    flat, padded_grad = butterfly_sum(
        jnp.concatenate(
            [
                conv_term.reshape(conv_rows, lanes),
                time_term.reshape(time_rows, lanes),
                class_term.reshape(class_rows, lanes),
                jnp.zeros((total - used, lanes), jnp.float32),
            ]
        ),
        grad_pre.reshape(tile_rows, tile_cols, DATES * C_OUT),
    )
    padded_grad = padded_grad.reshape(tile_rows + 2, tile_cols + 2, DATES, C_OUT)
    input_sum = transposed_conv(padded_grad, conv_weight, tile_rows, tile_cols)
    input_grad = input_sum.astype(jnp.bfloat16).reshape(tile_rows, tile_cols, DATES * C_IN)
    low, high = flat
    split = low.shape[0]
    conv_grad = jnp.concatenate([low, high[: conv_rows - split]]).reshape(conv_term.shape)
    time_grad = high[conv_rows - split : conv_rows - split + time_rows].reshape(time_term.shape)
    class_grad = high[conv_rows - split + time_rows : used - split].reshape(class_term.shape)
    return (input_grad, conv_grad, time_grad, class_grad)


def solution(mesh):
    in_specs = (
        P("row", "col", None),
        P(),
        P(),
        P(),
        P("row", "col"),
        P("row", "col", None),
        P("row", "col", None),
        P("row", "col", None),
    )
    out_specs = (P("row", "col", None), P(), P(), P())
    return jax.shard_map(
        per_device, mesh=mesh, in_specs=in_specs, out_specs=out_specs, check_vma=False
    )
```

```python
import jax
import jax.numpy as jnp
from jax import lax
from jax.sharding import PartitionSpec as P

DATES = 12
C_IN = 64
C_OUT = 128
GROUPS = 16
CLASSES = 20
P_OWN = 32
S_STR = 32
CPG = 8


EPSILON = 1e-05
PRECISE = lax.Precision.HIGHEST


def with_halo(cells, sides, width):
    for axis, dim in sides:
        count = lax.axis_size(axis)
        odd = lax.axis_index(axis) % 2 == 1
        last = cells.shape[dim] - width
        inner_piece = lax.dynamic_slice_in_dim(cells, jnp.where(odd, 0, last), width, axis=dim)
        outer_piece = lax.dynamic_slice_in_dim(cells, jnp.where(odd, last, 0), width, axis=dim)
        inner = lax.ppermute(inner_piece, axis, [(i, i ^ 1) for i in range(count)])
        outer = lax.ppermute(
            outer_piece,
            axis,
            [pair for k in range(1, count - 1, 2) for pair in ((k, k + 1), (k + 1, k))],
        )
        cells = jnp.concatenate(
            [jnp.where(odd, inner, outer), cells, jnp.where(odd, outer, inner)], axis=dim
        )
    return cells


def exchange(value, axis, bit):
    size = lax.axis_size(axis)
    return lax.ppermute(value, axis, [(i, i ^ bit) for i in range(size)])


def swap_with(value, axis, bit, extra):
    size = value.shape[0]
    lanes = value.shape[1]
    both = exchange(
        jnp.concatenate([value, extra.astype(value.dtype).reshape(-1, lanes)]), axis, bit
    )
    return both[:size], both[size:].reshape(extra.shape).astype(extra.dtype)


def halo_ends(cells, axis, dim):
    odd = lax.axis_index(axis) % 2 == 1
    last = cells.shape[dim] - 1
    return (
        odd,
        lax.dynamic_slice_in_dim(cells, jnp.where(odd, 0, last), 1, axis=dim),
        lax.dynamic_slice_in_dim(cells, jnp.where(odd, last, 0), 1, axis=dim),
    )


def outer_swap(piece, axis):
    count = lax.axis_size(axis)
    return lax.ppermute(
        piece, axis, [pair for k in range(1, count - 1, 2) for pair in ((k, k + 1), (k + 1, k))]
    )


def halo_join(cells, odd, inner, outer, dim):
    return jnp.concatenate(
        [jnp.where(odd, inner, outer), cells, jnp.where(odd, outer, inner)], axis=dim
    )


def butterfly_sum(flat, cells, halvings=2):
    steps = []
    for axis in ("col", "row"):
        bit = 1
        while bit < lax.axis_size(axis):
            steps.append((axis, bit))
            bit *= 2
    for axis, bit in steps[:halvings]:
        upper = (lax.axis_index(axis) // bit) % 2 == 1
        half = flat.shape[0] // 2
        low, high = flat[:half], flat[half:]
        keep = jnp.where(upper, high, low)
        give = jnp.where(upper, low, high)
        if (axis, bit) == ("col", 1):
            odd, inner_piece, outer_piece = halo_ends(cells, "col", 1)
            outer = outer_swap(outer_piece, "col")
            got, inner = swap_with(give, axis, bit, inner_piece)
            cells = halo_join(cells, odd, inner, outer, 1)
        else:
            got = exchange(give, axis, bit)
        flat = keep + got
    for axis, bit in steps[halvings:]:
        if (axis, bit) == ("row", 1):
            odd, inner_piece, outer_piece = halo_ends(cells, "row", 0)
            outer = outer_swap(outer_piece, "row")
            got, inner = swap_with(flat, axis, bit, inner_piece)
            cells = halo_join(cells, odd, inner, outer, 0)
        else:
            got = exchange(flat, axis, bit)
        flat = flat + got
    for axis, bit in reversed(steps[:halvings]):
        upper = (lax.axis_index(axis) // bit) % 2 == 1
        other = exchange(flat, axis, bit)
        flat = jnp.where(upper, jnp.concatenate([other, flat]), jnp.concatenate([flat, other]))
    return flat, cells


def silu_slope(value):
    sig = jax.nn.sigmoid(value)
    return sig * (1.0 + value * (1.0 - sig))


def spatial_forward(padded, conv_weight, tile_rows, tile_cols):
    running_sum = None
    for row_tap in range(3):
        tap_patch = jnp.concatenate(
            [
                padded[row_tap : row_tap + tile_rows, col_tap : col_tap + tile_cols]
                for col_tap in range(3)
            ],
            axis=-1,
        )
        tap_term = jnp.dot(
            tap_patch,
            conv_weight[row_tap].reshape(3 * C_IN, C_OUT),
            preferred_element_type=jnp.float32,
        )
        running_sum = tap_term if running_sum is None else running_sum + tap_term
    return running_sum


def window_conv(padded, kernel):
    return lax.conv_general_dilated(
        padded,
        kernel,
        window_strides=(1, 1),
        padding="VALID",
        dimension_numbers=("HWNC", "HWIO", "HWNC"),
        preferred_element_type=jnp.float32,
    )


def transposed_conv(padded_grad, conv_weight, out_rows, out_cols):
    input_sum = None
    for row_tap in range(3):
        grad_patch = jnp.concatenate(
            [
                padded_grad[
                    2 - row_tap : 2 - row_tap + out_rows, 2 - col_tap : 2 - col_tap + out_cols
                ]
                for col_tap in range(3)
            ],
            axis=-1,
        )
        flipped = jnp.concatenate([conv_weight[row_tap, col_tap].T for col_tap in range(3)], axis=0)
        tap_term = jnp.dot(grad_patch, flipped, preferred_element_type=jnp.float32)
        input_sum = tap_term if input_sum is None else input_sum + tap_term
    return input_sum


def same_group():
    rows = lax.broadcasted_iota(jnp.int32, (C_OUT, C_OUT), 0) // CPG
    cols = lax.broadcasted_iota(jnp.int32, (C_OUT, C_OUT), 1) // CPG
    return rows == cols


def block_weights(time_weight):
    tiled = jnp.tile(time_weight.reshape(3, C_OUT, CPG), (1, 1, GROUPS))
    return jnp.where(same_group()[None], tiled, jnp.zeros_like(tiled))


def group_blocks(dense):
    masked = jnp.where(same_group()[None], dense, jnp.zeros_like(dense))
    pick = (
        lax.broadcasted_iota(jnp.int32, (C_OUT, CPG), 0) % CPG
        == lax.broadcasted_iota(jnp.int32, (C_OUT, CPG), 1)
    ).astype(jnp.float32)
    return jnp.dot(masked, pick, precision=PRECISE).reshape(3, GROUPS, CPG, CPG)


def per_device(
    pixels, conv_weight, time_weight, class_weight, pixel_slot, straddle_dir, straddle_slot, labels
):
    tile_rows, tile_cols = (pixels.shape[0], pixels.shape[1])
    slot_count = P_OWN + S_STR
    padded_pixels = with_halo(pixels, (("row", 0), ("col", 1)), 1).reshape(
        tile_rows + 2, tile_cols + 2, DATES, C_IN
    )
    pre_act = window_conv(padded_pixels, conv_weight)
    hidden = jax.nn.silu(pre_act).astype(jnp.bfloat16)
    dense_time = block_weights(time_weight)
    padded_hidden = jnp.pad(hidden, ((0, 0), (0, 0), (1, 1), (0, 0)))
    mixed_time = None
    for time_tap in range(3):
        tap_term = jnp.dot(
            padded_hidden[:, :, time_tap : time_tap + DATES],
            dense_time[time_tap],
            preferred_element_type=jnp.float32,
        )
        mixed_time = tap_term if mixed_time is None else mixed_time + tap_term
    embedded = (
        jnp.mean(jax.nn.silu(mixed_time), axis=2)
        .astype(jnp.bfloat16)
        .reshape(tile_rows * tile_cols, C_OUT)
    )
    flat_slot = pixel_slot.reshape(tile_rows * tile_cols)
    membership = (jnp.arange(slot_count, dtype=jnp.int32)[:, None] == flat_slot[None, :]).astype(
        jnp.bfloat16
    )
    partial_value = jnp.dot(membership, embedded, preferred_element_type=jnp.float32)
    direction = straddle_dir.reshape(S_STR)
    owner_slot = straddle_slot.reshape(S_STR)
    own_slots = jnp.arange(P_OWN, dtype=jnp.int32)
    target = jnp.concatenate([4 * P_OWN + own_slots, direction * P_OWN + owner_slot])
    select = (jnp.arange(9 * P_OWN, dtype=jnp.int32)[:, None] == target[None, :]).astype(
        jnp.float32
    )
    outgoing = jnp.dot(select, partial_value, precision=PRECISE).reshape(3, 3, P_OWN, C_OUT)
    border = with_halo(outgoing.astype(jnp.bfloat16), (("row", 0), ("col", 1)), 1).astype(
        outgoing.dtype
    )
    parcel_sums = jnp.sum(border[0::2, 0::2], axis=(0, 1))
    centered = parcel_sums - jnp.mean(parcel_sums, axis=-1, keepdims=True)
    variance = jnp.mean(centered * centered, axis=-1, keepdims=True)
    inverse = lax.rsqrt(variance + EPSILON)
    normed = centered * inverse
    rounded = normed.astype(jnp.bfloat16)
    logits = jnp.dot(rounded, class_weight, preferred_element_type=jnp.float32)
    exp_logits = jnp.exp(logits)
    probability = exp_logits / jnp.sum(exp_logits, axis=-1, keepdims=True)
    label_hot = (
        labels.reshape(P_OWN)[:, None] == jnp.arange(CLASSES, dtype=jnp.int32)[None, :]
    ).astype(jnp.float32)
    parcel_total = P_OWN * lax.axis_size("row") * lax.axis_size("col")
    grad_logits = (probability - label_hot) / parcel_total
    class_term = jnp.dot(rounded.astype(jnp.float32).T, grad_logits, precision=PRECISE)
    grad_normed = jnp.dot(grad_logits, class_weight.astype(jnp.float32).T, precision=PRECISE)
    parcel_grad = (
        inverse
        * (
            grad_normed
            - jnp.mean(grad_normed, axis=-1, keepdims=True)
            - normed * jnp.mean(grad_normed * normed, axis=-1, keepdims=True)
        )
    ).astype(jnp.bfloat16)
    beside_all = with_halo(
        parcel_grad.reshape(1, 1, P_OWN, C_OUT), (("row", 0), ("col", 1)), 1
    ).reshape(9 * P_OWN, C_OUT)
    picker = (target[:, None] == jnp.arange(9 * P_OWN, dtype=jnp.int32)[None, :]).astype(
        jnp.bfloat16
    )
    slot_grad = jnp.dot(picker, beside_all, preferred_element_type=jnp.float32).astype(jnp.bfloat16)
    pixel_grad = jnp.dot(membership.T, slot_grad, preferred_element_type=jnp.float32).reshape(
        tile_rows, tile_cols, C_OUT
    )
    grad_mixed = ((pixel_grad / DATES)[:, :, None, :] * silu_slope(mixed_time)).astype(jnp.bfloat16)
    time_term = group_blocks(
        jnp.stack(
            [
                jnp.einsum(
                    "ijtc,ijtd->cd",
                    padded_hidden[:, :, time_tap : time_tap + DATES],
                    grad_mixed,
                    preferred_element_type=jnp.float32,
                )
                for time_tap in range(3)
            ]
        )
    )
    padded_mixed = jnp.pad(grad_mixed, ((0, 0), (0, 0), (1, 1), (0, 0)))
    grad_hidden = None
    for time_tap in range(3):
        tap_term = jnp.dot(
            padded_mixed[:, :, 2 - time_tap : 2 - time_tap + DATES],
            dense_time[time_tap].T,
            preferred_element_type=jnp.float32,
        )
        grad_hidden = tap_term if grad_hidden is None else grad_hidden + tap_term
    grad_pre = (grad_hidden * silu_slope(pre_act)).astype(jnp.bfloat16)
    conv_term = lax.conv_general_dilated(
        padded_pixels,
        grad_pre,
        window_strides=(1, 1),
        padding="VALID",
        dimension_numbers=("HWCN", "HWIO", "HWNC"),
        preferred_element_type=jnp.float32,
    )
    lanes = C_OUT
    conv_rows, time_rows, class_rows = (
        conv_term.size // lanes,
        time_term.size // lanes,
        class_term.size // lanes,
    )
    used = conv_rows + time_rows + class_rows
    total = -(-used // 32) * 32
    flat, padded_grad = butterfly_sum(
        jnp.concatenate(
            [
                conv_term.reshape(conv_rows, lanes),
                time_term.reshape(time_rows, lanes),
                class_term.reshape(class_rows, lanes),
                jnp.zeros((total - used, lanes), jnp.float32),
            ]
        ),
        grad_pre.reshape(tile_rows, tile_cols, DATES * C_OUT),
    )
    padded_grad = padded_grad.reshape(tile_rows + 2, tile_cols + 2, DATES, C_OUT)
    input_sum = transposed_conv(padded_grad, conv_weight, tile_rows, tile_cols)
    input_grad = input_sum.astype(jnp.bfloat16).reshape(tile_rows, tile_cols, DATES * C_IN)
    conv_grad = flat[:conv_rows].reshape(conv_term.shape)
    time_grad = flat[conv_rows : conv_rows + time_rows].reshape(time_term.shape)
    class_grad = flat[conv_rows + time_rows : used].reshape(class_term.shape)
    return (input_grad, conv_grad, time_grad, class_grad)


def solution(mesh):
    in_specs = (
        P("row", "col", None),
        P(),
        P(),
        P(),
        P("row", "col"),
        P("row", "col", None),
        P("row", "col", None),
        P("row", "col", None),
    )
    out_specs = (P("row", "col", None), P(), P(), P())
    return jax.shard_map(
        per_device, mesh=mesh, in_specs=in_specs, out_specs=out_specs, check_vma=False
    )
```

```python
import jax
import jax.numpy as jnp
from jax import lax
from jax.sharding import PartitionSpec as P

DATES = 12
C_IN = 64
C_OUT = 128
GROUPS = 16
CLASSES = 20
P_OWN = 32
S_STR = 32
CPG = 8


EPSILON = 1e-05
PRECISE = lax.Precision.HIGHEST


def with_halo(cells, sides, width):
    for axis, dim in sides:
        count = lax.axis_size(axis)
        odd = lax.axis_index(axis) % 2 == 1
        head = lax.slice_in_dim(cells, 0, width, axis=dim)
        tail = lax.slice_in_dim(cells, cells.shape[dim] - width, cells.shape[dim], axis=dim)
        inner = lax.ppermute(jnp.where(odd, head, tail), axis, [(i, i ^ 1) for i in range(count)])
        outer = lax.ppermute(
            jnp.where(odd, tail, head),
            axis,
            [pair for k in range(1, count - 1, 2) for pair in ((k, k + 1), (k + 1, k))],
        )
        cells = jnp.concatenate(
            [jnp.where(odd, inner, outer), cells, jnp.where(odd, outer, inner)], axis=dim
        )
    return cells


def exchange(value, axis, bit):
    size = lax.axis_size(axis)
    return lax.ppermute(value, axis, [(i, i ^ bit) for i in range(size)])


def swap_with(value, axis, bit, extra):
    size = value.shape[0]
    lanes = value.shape[1]
    both = exchange(
        jnp.concatenate([value, extra.astype(value.dtype).reshape(-1, lanes)]), axis, bit
    )
    return both[:size], both[size:].reshape(extra.shape).astype(extra.dtype)


def halo_ends(cells, axis, dim):
    odd = lax.axis_index(axis) % 2 == 1
    head = lax.slice_in_dim(cells, 0, 1, axis=dim)
    tail = lax.slice_in_dim(cells, cells.shape[dim] - 1, cells.shape[dim], axis=dim)
    return odd, jnp.where(odd, head, tail), jnp.where(odd, tail, head)


def outer_swap(piece, axis):
    count = lax.axis_size(axis)
    return lax.ppermute(
        piece, axis, [pair for k in range(1, count - 1, 2) for pair in ((k, k + 1), (k + 1, k))]
    )


def halo_join(cells, odd, inner, outer, dim):
    return jnp.concatenate(
        [jnp.where(odd, inner, outer), cells, jnp.where(odd, outer, inner)], axis=dim
    )


def butterfly_sum(flat, cells, halvings=1):
    steps = []
    for axis in ("col", "row"):
        bit = 1
        while bit < lax.axis_size(axis):
            steps.append((axis, bit))
            bit *= 2
    for axis, bit in steps[:halvings]:
        upper = (lax.axis_index(axis) // bit) % 2 == 1
        half = flat.shape[0] // 2
        low, high = flat[:half], flat[half:]
        keep = jnp.where(upper, high, low)
        give = jnp.where(upper, low, high)
        if (axis, bit) == ("col", 1):
            odd, inner_piece, outer_piece = halo_ends(cells, "col", 1)
            outer = outer_swap(outer_piece, "col")
            got, inner = swap_with(give, axis, bit, inner_piece)
            cells = halo_join(cells, odd, inner, outer, 1)
        else:
            got = exchange(give, axis, bit)
        flat = keep + got
    for axis, bit in steps[halvings:]:
        if (axis, bit) == ("row", 1):
            odd, inner_piece, outer_piece = halo_ends(cells, "row", 0)
            outer = outer_swap(outer_piece, "row")
            got, inner = swap_with(flat, axis, bit, inner_piece)
            cells = halo_join(cells, odd, inner, outer, 0)
        else:
            got = exchange(flat, axis, bit)
        flat = flat + got
    for axis, bit in reversed(steps[:halvings]):
        upper = (lax.axis_index(axis) // bit) % 2 == 1
        other = exchange(flat, axis, bit)
        flat = jnp.where(upper, jnp.concatenate([other, flat]), jnp.concatenate([flat, other]))
    return flat, cells


def silu_slope(value):
    sig = jax.nn.sigmoid(value)
    return sig * (1.0 + value * (1.0 - sig))


def spatial_forward(padded, conv_weight, tile_rows, tile_cols):
    running_sum = None
    for row_tap in range(3):
        tap_patch = jnp.concatenate(
            [
                padded[row_tap : row_tap + tile_rows, col_tap : col_tap + tile_cols]
                for col_tap in range(3)
            ],
            axis=-1,
        )
        tap_term = jnp.dot(
            tap_patch,
            conv_weight[row_tap].reshape(3 * C_IN, C_OUT),
            preferred_element_type=jnp.float32,
        )
        running_sum = tap_term if running_sum is None else running_sum + tap_term
    return running_sum


def window_conv(padded, kernel):
    return lax.conv_general_dilated(
        padded,
        kernel,
        window_strides=(1, 1),
        padding="VALID",
        dimension_numbers=("HWNC", "HWIO", "HWNC"),
        preferred_element_type=jnp.float32,
    )


def transposed_conv(padded_grad, conv_weight, out_rows, out_cols):
    input_sum = None
    for row_tap in range(3):
        grad_patch = jnp.concatenate(
            [
                padded_grad[
                    2 - row_tap : 2 - row_tap + out_rows, 2 - col_tap : 2 - col_tap + out_cols
                ]
                for col_tap in range(3)
            ],
            axis=-1,
        )
        flipped = jnp.concatenate([conv_weight[row_tap, col_tap].T for col_tap in range(3)], axis=0)
        tap_term = jnp.dot(grad_patch, flipped, preferred_element_type=jnp.float32)
        input_sum = tap_term if input_sum is None else input_sum + tap_term
    return input_sum


def same_group():
    rows = lax.broadcasted_iota(jnp.int32, (C_OUT, C_OUT), 0) // CPG
    cols = lax.broadcasted_iota(jnp.int32, (C_OUT, C_OUT), 1) // CPG
    return rows == cols


def block_weights(time_weight):
    tiled = jnp.tile(time_weight.reshape(3, C_OUT, CPG), (1, 1, GROUPS))
    return jnp.where(same_group()[None], tiled, jnp.zeros_like(tiled))


def group_blocks(dense):
    masked = jnp.where(same_group()[None], dense, jnp.zeros_like(dense))
    pick = (
        lax.broadcasted_iota(jnp.int32, (C_OUT, CPG), 0) % CPG
        == lax.broadcasted_iota(jnp.int32, (C_OUT, CPG), 1)
    ).astype(jnp.float32)
    return jnp.dot(masked, pick, precision=PRECISE).reshape(3, GROUPS, CPG, CPG)


def per_device(
    pixels, conv_weight, time_weight, class_weight, pixel_slot, straddle_dir, straddle_slot, labels
):
    tile_rows, tile_cols = (pixels.shape[0], pixels.shape[1])
    slot_count = P_OWN + S_STR
    padded_pixels = with_halo(pixels, (("row", 0), ("col", 1)), 1).reshape(
        tile_rows + 2, tile_cols + 2, DATES, C_IN
    )
    pre_act = window_conv(padded_pixels, conv_weight)
    hidden = jax.nn.silu(pre_act).astype(jnp.bfloat16)
    dense_time = block_weights(time_weight)
    padded_hidden = jnp.pad(hidden, ((0, 0), (0, 0), (1, 1), (0, 0)))
    mixed_time = None
    for time_tap in range(3):
        tap_term = jnp.dot(
            padded_hidden[:, :, time_tap : time_tap + DATES],
            dense_time[time_tap],
            preferred_element_type=jnp.float32,
        )
        mixed_time = tap_term if mixed_time is None else mixed_time + tap_term
    embedded = (
        jnp.mean(jax.nn.silu(mixed_time), axis=2)
        .astype(jnp.bfloat16)
        .reshape(tile_rows * tile_cols, C_OUT)
    )
    flat_slot = pixel_slot.reshape(tile_rows * tile_cols)
    membership = (jnp.arange(slot_count, dtype=jnp.int32)[:, None] == flat_slot[None, :]).astype(
        jnp.bfloat16
    )
    partial_value = jnp.dot(membership, embedded, preferred_element_type=jnp.float32)
    direction = straddle_dir.reshape(S_STR)
    owner_slot = straddle_slot.reshape(S_STR)
    own_slots = jnp.arange(P_OWN, dtype=jnp.int32)
    target = jnp.concatenate([4 * P_OWN + own_slots, direction * P_OWN + owner_slot])
    select = (jnp.arange(9 * P_OWN, dtype=jnp.int32)[:, None] == target[None, :]).astype(
        jnp.float32
    )
    outgoing = jnp.dot(select, partial_value, precision=PRECISE).reshape(3, 3, P_OWN, C_OUT)
    border = with_halo(outgoing.astype(jnp.bfloat16), (("row", 0), ("col", 1)), 1).astype(
        outgoing.dtype
    )
    parcel_sums = jnp.sum(border[0::2, 0::2], axis=(0, 1))
    centered = parcel_sums - jnp.mean(parcel_sums, axis=-1, keepdims=True)
    variance = jnp.mean(centered * centered, axis=-1, keepdims=True)
    inverse = lax.rsqrt(variance + EPSILON)
    normed = centered * inverse
    rounded = normed.astype(jnp.bfloat16)
    logits = jnp.dot(rounded, class_weight, preferred_element_type=jnp.float32)
    exp_logits = jnp.exp(logits)
    probability = exp_logits / jnp.sum(exp_logits, axis=-1, keepdims=True)
    label_hot = (
        labels.reshape(P_OWN)[:, None] == jnp.arange(CLASSES, dtype=jnp.int32)[None, :]
    ).astype(jnp.float32)
    parcel_total = P_OWN * lax.axis_size("row") * lax.axis_size("col")
    grad_logits = (probability - label_hot) / parcel_total
    class_term = jnp.dot(rounded.astype(jnp.float32).T, grad_logits, precision=PRECISE)
    grad_normed = jnp.dot(grad_logits, class_weight.astype(jnp.float32).T, precision=PRECISE)
    parcel_grad = (
        inverse
        * (
            grad_normed
            - jnp.mean(grad_normed, axis=-1, keepdims=True)
            - normed * jnp.mean(grad_normed * normed, axis=-1, keepdims=True)
        )
    ).astype(jnp.bfloat16)
    beside_all = with_halo(
        parcel_grad.reshape(1, 1, P_OWN, C_OUT), (("row", 0), ("col", 1)), 1
    ).reshape(9 * P_OWN, C_OUT)
    picker = (target[:, None] == jnp.arange(9 * P_OWN, dtype=jnp.int32)[None, :]).astype(
        jnp.bfloat16
    )
    slot_grad = jnp.dot(picker, beside_all, preferred_element_type=jnp.float32).astype(jnp.bfloat16)
    pixel_grad = jnp.dot(membership.T, slot_grad, preferred_element_type=jnp.float32).reshape(
        tile_rows, tile_cols, C_OUT
    )
    grad_mixed = ((pixel_grad / DATES)[:, :, None, :] * silu_slope(mixed_time)).astype(jnp.bfloat16)
    time_term = group_blocks(
        jnp.stack(
            [
                jnp.einsum(
                    "ijtc,ijtd->cd",
                    padded_hidden[:, :, time_tap : time_tap + DATES],
                    grad_mixed,
                    preferred_element_type=jnp.float32,
                )
                for time_tap in range(3)
            ]
        )
    )
    padded_mixed = jnp.pad(grad_mixed, ((0, 0), (0, 0), (1, 1), (0, 0)))
    grad_hidden = None
    for time_tap in range(3):
        tap_term = jnp.dot(
            padded_mixed[:, :, 2 - time_tap : 2 - time_tap + DATES],
            dense_time[time_tap].T,
            preferred_element_type=jnp.float32,
        )
        grad_hidden = tap_term if grad_hidden is None else grad_hidden + tap_term
    grad_pre = (grad_hidden * silu_slope(pre_act)).astype(jnp.bfloat16)
    conv_term = lax.conv_general_dilated(
        padded_pixels,
        grad_pre,
        window_strides=(1, 1),
        padding="VALID",
        dimension_numbers=("HWCN", "HWIO", "HWNC"),
        preferred_element_type=jnp.float32,
    )
    lanes = C_OUT
    conv_rows, time_rows, class_rows = (
        conv_term.size // lanes,
        time_term.size // lanes,
        class_term.size // lanes,
    )
    used = conv_rows + time_rows + class_rows
    total = -(-used // 32) * 32
    flat, padded_grad = butterfly_sum(
        jnp.concatenate(
            [
                conv_term.reshape(conv_rows, lanes),
                time_term.reshape(time_rows, lanes),
                class_term.reshape(class_rows, lanes),
                jnp.zeros((total - used, lanes), jnp.float32),
            ]
        ),
        grad_pre.reshape(tile_rows, tile_cols, DATES * C_OUT),
    )
    padded_grad = padded_grad.reshape(tile_rows + 2, tile_cols + 2, DATES, C_OUT)
    input_sum = transposed_conv(padded_grad, conv_weight, tile_rows, tile_cols)
    input_grad = input_sum.astype(jnp.bfloat16).reshape(tile_rows, tile_cols, DATES * C_IN)
    conv_grad = flat[:conv_rows].reshape(conv_term.shape)
    time_grad = flat[conv_rows : conv_rows + time_rows].reshape(time_term.shape)
    class_grad = flat[conv_rows + time_rows : used].reshape(class_term.shape)
    return (input_grad, conv_grad, time_grad, class_grad)


def solution(mesh):
    in_specs = (
        P("row", "col", None),
        P(),
        P(),
        P(),
        P("row", "col"),
        P("row", "col", None),
        P("row", "col", None),
        P("row", "col", None),
    )
    out_specs = (P("row", "col", None), P(), P(), P())
    return jax.shard_map(
        per_device, mesh=mesh, in_specs=in_specs, out_specs=out_specs, check_vma=False
    )
```

```python
import jax
import jax.numpy as jnp
from jax import lax
from jax.sharding import PartitionSpec as P

DATES = 12
C_IN = 64
C_OUT = 128
GROUPS = 16
CLASSES = 20
P_OWN = 32
S_STR = 32
CPG = 8


EPSILON = 1e-05
PRECISE = lax.Precision.HIGHEST


def with_halo(cells, sides, width):
    for axis, dim in sides:
        count = lax.axis_size(axis)
        odd = lax.axis_index(axis) % 2 == 1
        head = lax.slice_in_dim(cells, 0, width, axis=dim)
        tail = lax.slice_in_dim(cells, cells.shape[dim] - width, cells.shape[dim], axis=dim)
        inner = lax.ppermute(jnp.where(odd, head, tail), axis, [(i, i ^ 1) for i in range(count)])
        outer = lax.ppermute(
            jnp.where(odd, tail, head),
            axis,
            [pair for k in range(1, count - 1, 2) for pair in ((k, k + 1), (k + 1, k))],
        )
        cells = jnp.concatenate(
            [jnp.where(odd, inner, outer), cells, jnp.where(odd, outer, inner)], axis=dim
        )
    return cells


def exchange(value, axis, bit):
    size = lax.axis_size(axis)
    return lax.ppermute(value, axis, [(i, i ^ bit) for i in range(size)])


def swap_with(value, axis, bit, extra):
    size = value.shape[0]
    lanes = value.shape[1]
    both = exchange(
        jnp.concatenate([value, extra.astype(value.dtype).reshape(-1, lanes)]), axis, bit
    )
    return both[:size], both[size:].reshape(extra.shape).astype(extra.dtype)


def halo_ends(cells, axis, dim):
    odd = lax.axis_index(axis) % 2 == 1
    head = lax.slice_in_dim(cells, 0, 1, axis=dim)
    tail = lax.slice_in_dim(cells, cells.shape[dim] - 1, cells.shape[dim], axis=dim)
    return odd, jnp.where(odd, head, tail), jnp.where(odd, tail, head)


def outer_swap(piece, axis):
    count = lax.axis_size(axis)
    return lax.ppermute(
        piece, axis, [pair for k in range(1, count - 1, 2) for pair in ((k, k + 1), (k + 1, k))]
    )


def halo_join(cells, odd, inner, outer, dim):
    return jnp.concatenate(
        [jnp.where(odd, inner, outer), cells, jnp.where(odd, outer, inner)], axis=dim
    )


def butterfly_sum(flat, cells, halvings=2):
    steps = []
    for axis in ("col", "row"):
        bit = 1
        while bit < lax.axis_size(axis):
            steps.append((axis, bit))
            bit *= 2
    for axis, bit in steps[:halvings]:
        upper = (lax.axis_index(axis) // bit) % 2 == 1
        half = flat.shape[0] // 2
        low, high = flat[:half], flat[half:]
        keep = jnp.where(upper, high, low)
        give = jnp.where(upper, low, high)
        if (axis, bit) == ("col", 1):
            odd, inner_piece, outer_piece = halo_ends(cells, "col", 1)
            outer = outer_swap(outer_piece, "col")
            got, inner = swap_with(give, axis, bit, inner_piece)
            cells = halo_join(cells, odd, inner, outer, 1)
        else:
            got = exchange(give, axis, bit)
        flat = keep + got
    middle = steps[halvings:]
    middle = [step for step in middle if step == ("row", 1)] + [
        step for step in middle if step != ("row", 1)
    ]
    for axis, bit in middle:
        if (axis, bit) == ("row", 1):
            odd, inner_piece, outer_piece = halo_ends(cells, "row", 0)
            outer = outer_swap(outer_piece, "row")
            got, inner = swap_with(flat, axis, bit, inner_piece)
            cells = halo_join(cells, odd, inner, outer, 0)
        else:
            got = exchange(flat, axis, bit)
        flat = flat + got
    for axis, bit in reversed(steps[:halvings]):
        upper = (lax.axis_index(axis) // bit) % 2 == 1
        other = exchange(flat, axis, bit)
        flat = jnp.where(upper, jnp.concatenate([other, flat]), jnp.concatenate([flat, other]))
    return flat, cells


def silu_slope(value):
    sig = jax.nn.sigmoid(value)
    return sig * (1.0 + value * (1.0 - sig))


def spatial_forward(padded, conv_weight, tile_rows, tile_cols):
    running_sum = None
    for row_tap in range(3):
        tap_patch = jnp.concatenate(
            [
                padded[row_tap : row_tap + tile_rows, col_tap : col_tap + tile_cols]
                for col_tap in range(3)
            ],
            axis=-1,
        )
        tap_term = jnp.dot(
            tap_patch,
            conv_weight[row_tap].reshape(3 * C_IN, C_OUT),
            preferred_element_type=jnp.float32,
        )
        running_sum = tap_term if running_sum is None else running_sum + tap_term
    return running_sum


def window_conv(padded, kernel):
    return lax.conv_general_dilated(
        padded,
        kernel,
        window_strides=(1, 1),
        padding="VALID",
        dimension_numbers=("HWNC", "HWIO", "HWNC"),
        preferred_element_type=jnp.float32,
    )


def transposed_conv(padded_grad, conv_weight, out_rows, out_cols):
    input_sum = None
    for row_tap in range(3):
        grad_patch = jnp.concatenate(
            [
                padded_grad[
                    2 - row_tap : 2 - row_tap + out_rows, 2 - col_tap : 2 - col_tap + out_cols
                ]
                for col_tap in range(3)
            ],
            axis=-1,
        )
        flipped = jnp.concatenate([conv_weight[row_tap, col_tap].T for col_tap in range(3)], axis=0)
        tap_term = jnp.dot(grad_patch, flipped, preferred_element_type=jnp.float32)
        input_sum = tap_term if input_sum is None else input_sum + tap_term
    return input_sum


def same_group():
    rows = lax.broadcasted_iota(jnp.int32, (C_OUT, C_OUT), 0) // CPG
    cols = lax.broadcasted_iota(jnp.int32, (C_OUT, C_OUT), 1) // CPG
    return rows == cols


def block_weights(time_weight):
    tiled = jnp.tile(time_weight.reshape(3, C_OUT, CPG), (1, 1, GROUPS))
    return jnp.where(same_group()[None], tiled, jnp.zeros_like(tiled))


def group_blocks(dense):
    masked = jnp.where(same_group()[None], dense, jnp.zeros_like(dense))
    pick = (
        lax.broadcasted_iota(jnp.int32, (C_OUT, CPG), 0) % CPG
        == lax.broadcasted_iota(jnp.int32, (C_OUT, CPG), 1)
    ).astype(jnp.float32)
    return jnp.dot(masked, pick, precision=PRECISE).reshape(3, GROUPS, CPG, CPG)


def per_device(
    pixels, conv_weight, time_weight, class_weight, pixel_slot, straddle_dir, straddle_slot, labels
):
    tile_rows, tile_cols = (pixels.shape[0], pixels.shape[1])
    slot_count = P_OWN + S_STR
    padded_pixels = with_halo(pixels, (("row", 0), ("col", 1)), 1).reshape(
        tile_rows + 2, tile_cols + 2, DATES, C_IN
    )
    pre_act = window_conv(padded_pixels, conv_weight)
    hidden = jax.nn.silu(pre_act).astype(jnp.bfloat16)
    dense_time = block_weights(time_weight)
    padded_hidden = jnp.pad(hidden, ((0, 0), (0, 0), (1, 1), (0, 0)))
    mixed_time = None
    for time_tap in range(3):
        tap_term = jnp.dot(
            padded_hidden[:, :, time_tap : time_tap + DATES],
            dense_time[time_tap],
            preferred_element_type=jnp.float32,
        )
        mixed_time = tap_term if mixed_time is None else mixed_time + tap_term
    embedded = (
        jnp.mean(jax.nn.silu(mixed_time), axis=2)
        .astype(jnp.bfloat16)
        .reshape(tile_rows * tile_cols, C_OUT)
    )
    flat_slot = pixel_slot.reshape(tile_rows * tile_cols)
    membership = (jnp.arange(slot_count, dtype=jnp.int32)[:, None] == flat_slot[None, :]).astype(
        jnp.bfloat16
    )
    partial_value = jnp.dot(membership, embedded, preferred_element_type=jnp.float32)
    direction = straddle_dir.reshape(S_STR)
    owner_slot = straddle_slot.reshape(S_STR)
    own_slots = jnp.arange(P_OWN, dtype=jnp.int32)
    target = jnp.concatenate([4 * P_OWN + own_slots, direction * P_OWN + owner_slot])
    select = (jnp.arange(9 * P_OWN, dtype=jnp.int32)[:, None] == target[None, :]).astype(
        jnp.float32
    )
    outgoing = jnp.dot(select, partial_value, precision=PRECISE).reshape(3, 3, P_OWN, C_OUT)
    border = with_halo(outgoing.astype(jnp.bfloat16), (("row", 0), ("col", 1)), 1).astype(
        outgoing.dtype
    )
    parcel_sums = jnp.sum(border[0::2, 0::2], axis=(0, 1))
    centered = parcel_sums - jnp.mean(parcel_sums, axis=-1, keepdims=True)
    variance = jnp.mean(centered * centered, axis=-1, keepdims=True)
    inverse = lax.rsqrt(variance + EPSILON)
    normed = centered * inverse
    rounded = normed.astype(jnp.bfloat16)
    logits = jnp.dot(rounded, class_weight, preferred_element_type=jnp.float32)
    exp_logits = jnp.exp(logits)
    probability = exp_logits / jnp.sum(exp_logits, axis=-1, keepdims=True)
    label_hot = (
        labels.reshape(P_OWN)[:, None] == jnp.arange(CLASSES, dtype=jnp.int32)[None, :]
    ).astype(jnp.float32)
    parcel_total = P_OWN * lax.axis_size("row") * lax.axis_size("col")
    grad_logits = (probability - label_hot) / parcel_total
    class_term = jnp.dot(rounded.astype(jnp.float32).T, grad_logits, precision=PRECISE)
    grad_normed = jnp.dot(grad_logits, class_weight.astype(jnp.float32).T, precision=PRECISE)
    parcel_grad = (
        inverse
        * (
            grad_normed
            - jnp.mean(grad_normed, axis=-1, keepdims=True)
            - normed * jnp.mean(grad_normed * normed, axis=-1, keepdims=True)
        )
    ).astype(jnp.bfloat16)
    beside_all = with_halo(
        parcel_grad.reshape(1, 1, P_OWN, C_OUT), (("row", 0), ("col", 1)), 1
    ).reshape(9 * P_OWN, C_OUT)
    picker = (target[:, None] == jnp.arange(9 * P_OWN, dtype=jnp.int32)[None, :]).astype(
        jnp.bfloat16
    )
    slot_grad = jnp.dot(picker, beside_all, preferred_element_type=jnp.float32).astype(jnp.bfloat16)
    pixel_grad = jnp.dot(membership.T, slot_grad, preferred_element_type=jnp.float32).reshape(
        tile_rows, tile_cols, C_OUT
    )
    grad_mixed = ((pixel_grad / DATES)[:, :, None, :] * silu_slope(mixed_time)).astype(jnp.bfloat16)
    time_term = group_blocks(
        jnp.stack(
            [
                jnp.einsum(
                    "ijtc,ijtd->cd",
                    padded_hidden[:, :, time_tap : time_tap + DATES],
                    grad_mixed,
                    preferred_element_type=jnp.float32,
                )
                for time_tap in range(3)
            ]
        )
    )
    padded_mixed = jnp.pad(grad_mixed, ((0, 0), (0, 0), (1, 1), (0, 0)))
    grad_hidden = None
    for time_tap in range(3):
        tap_term = jnp.dot(
            padded_mixed[:, :, 2 - time_tap : 2 - time_tap + DATES],
            dense_time[time_tap].T,
            preferred_element_type=jnp.float32,
        )
        grad_hidden = tap_term if grad_hidden is None else grad_hidden + tap_term
    grad_pre = (grad_hidden * silu_slope(pre_act)).astype(jnp.bfloat16)
    conv_term = lax.conv_general_dilated(
        padded_pixels,
        grad_pre,
        window_strides=(1, 1),
        padding="VALID",
        dimension_numbers=("HWCN", "HWIO", "HWNC"),
        preferred_element_type=jnp.float32,
    )
    lanes = C_OUT
    conv_rows, time_rows, class_rows = (
        conv_term.size // lanes,
        time_term.size // lanes,
        class_term.size // lanes,
    )
    used = conv_rows + time_rows + class_rows
    total = -(-used // 32) * 32
    flat, padded_grad = butterfly_sum(
        jnp.concatenate(
            [
                conv_term.reshape(conv_rows, lanes),
                time_term.reshape(time_rows, lanes),
                class_term.reshape(class_rows, lanes),
                jnp.zeros((total - used, lanes), jnp.float32),
            ]
        ),
        grad_pre.reshape(tile_rows, tile_cols, DATES * C_OUT),
    )
    padded_grad = padded_grad.reshape(tile_rows + 2, tile_cols + 2, DATES, C_OUT)
    input_sum = transposed_conv(padded_grad, conv_weight, tile_rows, tile_cols)
    input_grad = input_sum.astype(jnp.bfloat16).reshape(tile_rows, tile_cols, DATES * C_IN)
    conv_grad = flat[:conv_rows].reshape(conv_term.shape)
    time_grad = flat[conv_rows : conv_rows + time_rows].reshape(time_term.shape)
    class_grad = flat[conv_rows + time_rows : used].reshape(class_term.shape)
    return (input_grad, conv_grad, time_grad, class_grad)


def solution(mesh):
    in_specs = (
        P("row", "col", None),
        P(),
        P(),
        P(),
        P("row", "col"),
        P("row", "col", None),
        P("row", "col", None),
        P("row", "col", None),
    )
    out_specs = (P("row", "col", None), P(), P(), P())
    return jax.shard_map(
        per_device, mesh=mesh, in_specs=in_specs, out_specs=out_specs, check_vma=False
    )
```

```python
import jax
import jax.numpy as jnp
from jax import lax
from jax.sharding import PartitionSpec as P

DATES = 12
C_IN = 64
C_OUT = 128
GROUPS = 16
CLASSES = 20
P_OWN = 32
S_STR = 32
CPG = 8


EPSILON = 1e-05
PRECISE = lax.Precision.HIGHEST


def with_halo(cells, sides, width):
    for axis, dim in sides:
        count = lax.axis_size(axis)
        odd = lax.axis_index(axis) % 2 == 1
        head = lax.slice_in_dim(cells, 0, width, axis=dim)
        tail = lax.slice_in_dim(cells, cells.shape[dim] - width, cells.shape[dim], axis=dim)
        inner = lax.ppermute(jnp.where(odd, head, tail), axis, [(i, i ^ 1) for i in range(count)])
        outer = lax.ppermute(
            jnp.where(odd, tail, head),
            axis,
            [pair for k in range(1, count - 1, 2) for pair in ((k, k + 1), (k + 1, k))],
        )
        cells = jnp.concatenate(
            [jnp.where(odd, inner, outer), cells, jnp.where(odd, outer, inner)], axis=dim
        )
    return cells


def exchange(value, axis, bit):
    size = lax.axis_size(axis)
    return lax.ppermute(value, axis, [(i, i ^ bit) for i in range(size)])


def swap_with(value, axis, bit, extra):
    size = value.shape[0]
    lanes = value.shape[1]
    both = exchange(
        jnp.concatenate([value, extra.astype(value.dtype).reshape(-1, lanes)]), axis, bit
    )
    return both[:size], both[size:].reshape(extra.shape).astype(extra.dtype)


def halo_ends(cells, axis, dim):
    odd = lax.axis_index(axis) % 2 == 1
    head = lax.slice_in_dim(cells, 0, 1, axis=dim)
    tail = lax.slice_in_dim(cells, cells.shape[dim] - 1, cells.shape[dim], axis=dim)
    return odd, jnp.where(odd, head, tail), jnp.where(odd, tail, head)


def outer_swap(piece, axis):
    count = lax.axis_size(axis)
    return lax.ppermute(
        piece, axis, [pair for k in range(1, count - 1, 2) for pair in ((k, k + 1), (k + 1, k))]
    )


def halo_join(cells, odd, inner, outer, dim):
    return jnp.concatenate(
        [jnp.where(odd, inner, outer), cells, jnp.where(odd, outer, inner)], axis=dim
    )


def butterfly_sum(flat, cells, halvings=2):
    steps = []
    for axis in ("col", "row"):
        bit = 1
        while bit < lax.axis_size(axis):
            steps.append((axis, bit))
            bit *= 2
    for axis, bit in steps[:halvings]:
        upper = (lax.axis_index(axis) // bit) % 2 == 1
        half = flat.shape[0] // 2
        low, high = flat[:half], flat[half:]
        keep = jnp.where(upper, high, low)
        give = jnp.where(upper, low, high)
        if (axis, bit) == ("col", 1):
            odd, inner_piece, outer_piece = halo_ends(cells, "col", 1)
            outer = outer_swap(outer_piece, "col")
            got, inner = exchange(give, axis, bit), exchange(inner_piece, axis, bit)
            cells = halo_join(cells, odd, inner, outer, 1)
        else:
            got = exchange(give, axis, bit)
        flat = keep + got
    for axis, bit in steps[halvings:]:
        if (axis, bit) == ("row", 1):
            odd, inner_piece, outer_piece = halo_ends(cells, "row", 0)
            outer = outer_swap(outer_piece, "row")
            got, inner = exchange(flat, axis, bit), exchange(inner_piece, axis, bit)
            cells = halo_join(cells, odd, inner, outer, 0)
        else:
            got = exchange(flat, axis, bit)
        flat = flat + got
    for axis, bit in reversed(steps[:halvings]):
        upper = (lax.axis_index(axis) // bit) % 2 == 1
        other = exchange(flat, axis, bit)
        flat = jnp.where(upper, jnp.concatenate([other, flat]), jnp.concatenate([flat, other]))
    return flat, cells


def silu_slope(value):
    sig = jax.nn.sigmoid(value)
    return sig * (1.0 + value * (1.0 - sig))


def spatial_forward(padded, conv_weight, tile_rows, tile_cols):
    running_sum = None
    for row_tap in range(3):
        tap_patch = jnp.concatenate(
            [
                padded[row_tap : row_tap + tile_rows, col_tap : col_tap + tile_cols]
                for col_tap in range(3)
            ],
            axis=-1,
        )
        tap_term = jnp.dot(
            tap_patch,
            conv_weight[row_tap].reshape(3 * C_IN, C_OUT),
            preferred_element_type=jnp.float32,
        )
        running_sum = tap_term if running_sum is None else running_sum + tap_term
    return running_sum


def window_conv(padded, kernel):
    return lax.conv_general_dilated(
        padded,
        kernel,
        window_strides=(1, 1),
        padding="VALID",
        dimension_numbers=("HWNC", "HWIO", "HWNC"),
        preferred_element_type=jnp.float32,
    )


def transposed_conv(padded_grad, conv_weight, out_rows, out_cols):
    input_sum = None
    for row_tap in range(3):
        grad_patch = jnp.concatenate(
            [
                padded_grad[
                    2 - row_tap : 2 - row_tap + out_rows, 2 - col_tap : 2 - col_tap + out_cols
                ]
                for col_tap in range(3)
            ],
            axis=-1,
        )
        flipped = jnp.concatenate([conv_weight[row_tap, col_tap].T for col_tap in range(3)], axis=0)
        tap_term = jnp.dot(grad_patch, flipped, preferred_element_type=jnp.float32)
        input_sum = tap_term if input_sum is None else input_sum + tap_term
    return input_sum


def same_group():
    rows = lax.broadcasted_iota(jnp.int32, (C_OUT, C_OUT), 0) // CPG
    cols = lax.broadcasted_iota(jnp.int32, (C_OUT, C_OUT), 1) // CPG
    return rows == cols


def block_weights(time_weight):
    tiled = jnp.tile(time_weight.reshape(3, C_OUT, CPG), (1, 1, GROUPS))
    return jnp.where(same_group()[None], tiled, jnp.zeros_like(tiled))


def group_blocks(dense):
    masked = jnp.where(same_group()[None], dense, jnp.zeros_like(dense))
    pick = (
        lax.broadcasted_iota(jnp.int32, (C_OUT, CPG), 0) % CPG
        == lax.broadcasted_iota(jnp.int32, (C_OUT, CPG), 1)
    ).astype(jnp.float32)
    return jnp.dot(masked, pick, precision=PRECISE).reshape(3, GROUPS, CPG, CPG)


def per_device(
    pixels, conv_weight, time_weight, class_weight, pixel_slot, straddle_dir, straddle_slot, labels
):
    tile_rows, tile_cols = (pixels.shape[0], pixels.shape[1])
    slot_count = P_OWN + S_STR
    padded_pixels = with_halo(pixels, (("row", 0), ("col", 1)), 1).reshape(
        tile_rows + 2, tile_cols + 2, DATES, C_IN
    )
    pre_act = window_conv(padded_pixels, conv_weight)
    hidden = jax.nn.silu(pre_act).astype(jnp.bfloat16)
    dense_time = block_weights(time_weight)
    padded_hidden = jnp.pad(hidden, ((0, 0), (0, 0), (1, 1), (0, 0)))
    mixed_time = None
    for time_tap in range(3):
        tap_term = jnp.dot(
            padded_hidden[:, :, time_tap : time_tap + DATES],
            dense_time[time_tap],
            preferred_element_type=jnp.float32,
        )
        mixed_time = tap_term if mixed_time is None else mixed_time + tap_term
    embedded = (
        jnp.mean(jax.nn.silu(mixed_time), axis=2)
        .astype(jnp.bfloat16)
        .reshape(tile_rows * tile_cols, C_OUT)
    )
    flat_slot = pixel_slot.reshape(tile_rows * tile_cols)
    membership = (jnp.arange(slot_count, dtype=jnp.int32)[:, None] == flat_slot[None, :]).astype(
        jnp.bfloat16
    )
    partial_value = jnp.dot(membership, embedded, preferred_element_type=jnp.float32)
    direction = straddle_dir.reshape(S_STR)
    owner_slot = straddle_slot.reshape(S_STR)
    own_slots = jnp.arange(P_OWN, dtype=jnp.int32)
    target = jnp.concatenate([4 * P_OWN + own_slots, direction * P_OWN + owner_slot])
    select = (jnp.arange(9 * P_OWN, dtype=jnp.int32)[:, None] == target[None, :]).astype(
        jnp.float32
    )
    outgoing = jnp.dot(select, partial_value, precision=PRECISE).reshape(3, 3, P_OWN, C_OUT)
    border = with_halo(outgoing.astype(jnp.bfloat16), (("row", 0), ("col", 1)), 1).astype(
        outgoing.dtype
    )
    parcel_sums = jnp.sum(border[0::2, 0::2], axis=(0, 1))
    centered = parcel_sums - jnp.mean(parcel_sums, axis=-1, keepdims=True)
    variance = jnp.mean(centered * centered, axis=-1, keepdims=True)
    inverse = lax.rsqrt(variance + EPSILON)
    normed = centered * inverse
    rounded = normed.astype(jnp.bfloat16)
    logits = jnp.dot(rounded, class_weight, preferred_element_type=jnp.float32)
    exp_logits = jnp.exp(logits)
    probability = exp_logits / jnp.sum(exp_logits, axis=-1, keepdims=True)
    label_hot = (
        labels.reshape(P_OWN)[:, None] == jnp.arange(CLASSES, dtype=jnp.int32)[None, :]
    ).astype(jnp.float32)
    parcel_total = P_OWN * lax.axis_size("row") * lax.axis_size("col")
    grad_logits = (probability - label_hot) / parcel_total
    class_term = jnp.dot(rounded.astype(jnp.float32).T, grad_logits, precision=PRECISE)
    grad_normed = jnp.dot(grad_logits, class_weight.astype(jnp.float32).T, precision=PRECISE)
    parcel_grad = (
        inverse
        * (
            grad_normed
            - jnp.mean(grad_normed, axis=-1, keepdims=True)
            - normed * jnp.mean(grad_normed * normed, axis=-1, keepdims=True)
        )
    ).astype(jnp.bfloat16)
    beside_all = with_halo(
        parcel_grad.reshape(1, 1, P_OWN, C_OUT), (("row", 0), ("col", 1)), 1
    ).reshape(9 * P_OWN, C_OUT)
    picker = (target[:, None] == jnp.arange(9 * P_OWN, dtype=jnp.int32)[None, :]).astype(
        jnp.bfloat16
    )
    slot_grad = jnp.dot(picker, beside_all, preferred_element_type=jnp.float32).astype(jnp.bfloat16)
    pixel_grad = jnp.dot(membership.T, slot_grad, preferred_element_type=jnp.float32).reshape(
        tile_rows, tile_cols, C_OUT
    )
    grad_mixed = ((pixel_grad / DATES)[:, :, None, :] * silu_slope(mixed_time)).astype(jnp.bfloat16)
    time_term = group_blocks(
        jnp.stack(
            [
                jnp.einsum(
                    "ijtc,ijtd->cd",
                    padded_hidden[:, :, time_tap : time_tap + DATES],
                    grad_mixed,
                    preferred_element_type=jnp.float32,
                )
                for time_tap in range(3)
            ]
        )
    )
    padded_mixed = jnp.pad(grad_mixed, ((0, 0), (0, 0), (1, 1), (0, 0)))
    grad_hidden = None
    for time_tap in range(3):
        tap_term = jnp.dot(
            padded_mixed[:, :, 2 - time_tap : 2 - time_tap + DATES],
            dense_time[time_tap].T,
            preferred_element_type=jnp.float32,
        )
        grad_hidden = tap_term if grad_hidden is None else grad_hidden + tap_term
    grad_pre = (grad_hidden * silu_slope(pre_act)).astype(jnp.bfloat16)
    conv_term = lax.conv_general_dilated(
        padded_pixels,
        grad_pre,
        window_strides=(1, 1),
        padding="VALID",
        dimension_numbers=("HWCN", "HWIO", "HWNC"),
        preferred_element_type=jnp.float32,
    )
    lanes = C_OUT
    conv_rows, time_rows, class_rows = (
        conv_term.size // lanes,
        time_term.size // lanes,
        class_term.size // lanes,
    )
    used = conv_rows + time_rows + class_rows
    total = -(-used // 32) * 32
    flat, padded_grad = butterfly_sum(
        jnp.concatenate(
            [
                conv_term.reshape(conv_rows, lanes),
                time_term.reshape(time_rows, lanes),
                class_term.reshape(class_rows, lanes),
                jnp.zeros((total - used, lanes), jnp.float32),
            ]
        ),
        grad_pre.reshape(tile_rows, tile_cols, DATES * C_OUT),
    )
    padded_grad = padded_grad.reshape(tile_rows + 2, tile_cols + 2, DATES, C_OUT)
    input_sum = transposed_conv(padded_grad, conv_weight, tile_rows, tile_cols)
    input_grad = input_sum.astype(jnp.bfloat16).reshape(tile_rows, tile_cols, DATES * C_IN)
    conv_grad = flat[:conv_rows].reshape(conv_term.shape)
    time_grad = flat[conv_rows : conv_rows + time_rows].reshape(time_term.shape)
    class_grad = flat[conv_rows + time_rows : used].reshape(class_term.shape)
    return (input_grad, conv_grad, time_grad, class_grad)


def solution(mesh):
    in_specs = (
        P("row", "col", None),
        P(),
        P(),
        P(),
        P("row", "col"),
        P("row", "col", None),
        P("row", "col", None),
        P("row", "col", None),
    )
    out_specs = (P("row", "col", None), P(), P(), P())
    return jax.shard_map(
        per_device, mesh=mesh, in_specs=in_specs, out_specs=out_specs, check_vma=False
    )
```

```python
import jax
import jax.numpy as jnp
from jax import lax
from jax.sharding import PartitionSpec as P

DATES = 12
C_IN = 64
C_OUT = 128
GROUPS = 16
CLASSES = 20
P_OWN = 32
S_STR = 32
CPG = 8


EPSILON = 1e-05
PRECISE = lax.Precision.HIGHEST


def with_halo(cells, sides, width):
    for axis, dim in sides:
        count = lax.axis_size(axis)
        odd = lax.axis_index(axis) % 2 == 1
        head = lax.slice_in_dim(cells, 0, width, axis=dim)
        tail = lax.slice_in_dim(cells, cells.shape[dim] - width, cells.shape[dim], axis=dim)
        inner = lax.ppermute(jnp.where(odd, head, tail), axis, [(i, i ^ 1) for i in range(count)])
        outer = lax.ppermute(
            jnp.where(odd, tail, head),
            axis,
            [pair for k in range(1, count - 1, 2) for pair in ((k, k + 1), (k + 1, k))],
        )
        cells = jnp.concatenate(
            [jnp.where(odd, inner, outer), cells, jnp.where(odd, outer, inner)], axis=dim
        )
    return cells


def ring_partner(i, bit):
    low = i % (bit * 4) // bit
    other = (low + 1) % 4 if low % 2 else (low - 1) % 4
    return i + (other - low) * bit


def exchange(value, axis, bit):
    size = lax.axis_size(axis)
    if axis == "row" and bit in (2, 8):
        return lax.ppermute(value, axis, [(i, ring_partner(i, bit // 2)) for i in range(size)])
    return lax.ppermute(value, axis, [(i, i ^ bit) for i in range(size)])


def swap_with(value, axis, bit, extra):
    size = value.shape[0]
    lanes = value.shape[1]
    both = exchange(
        jnp.concatenate([value, extra.astype(value.dtype).reshape(-1, lanes)]), axis, bit
    )
    return both[:size], both[size:].reshape(extra.shape).astype(extra.dtype)


def halo_ends(cells, axis, dim):
    odd = lax.axis_index(axis) % 2 == 1
    head = lax.slice_in_dim(cells, 0, 1, axis=dim)
    tail = lax.slice_in_dim(cells, cells.shape[dim] - 1, cells.shape[dim], axis=dim)
    return odd, jnp.where(odd, head, tail), jnp.where(odd, tail, head)


def outer_swap(piece, axis):
    count = lax.axis_size(axis)
    return lax.ppermute(
        piece, axis, [pair for k in range(1, count - 1, 2) for pair in ((k, k + 1), (k + 1, k))]
    )


def halo_join(cells, odd, inner, outer, dim):
    return jnp.concatenate(
        [jnp.where(odd, inner, outer), cells, jnp.where(odd, outer, inner)], axis=dim
    )


def butterfly_sum(flat, cells, halvings=2):
    steps = []
    for axis in ("col", "row"):
        bit = 1
        while bit < lax.axis_size(axis):
            steps.append((axis, bit))
            bit *= 2
    for axis, bit in steps[:halvings]:
        upper = (lax.axis_index(axis) // bit) % 2 == 1
        half = flat.shape[0] // 2
        low, high = flat[:half], flat[half:]
        keep = jnp.where(upper, high, low)
        give = jnp.where(upper, low, high)
        if (axis, bit) == ("col", 1):
            odd, inner_piece, outer_piece = halo_ends(cells, "col", 1)
            outer = outer_swap(outer_piece, "col")
            got, inner = swap_with(give, axis, bit, inner_piece)
            cells = halo_join(cells, odd, inner, outer, 1)
        else:
            got = exchange(give, axis, bit)
        flat = keep + got
    for axis, bit in steps[halvings:]:
        if (axis, bit) == ("row", 1):
            odd, inner_piece, outer_piece = halo_ends(cells, "row", 0)
            outer = outer_swap(outer_piece, "row")
            got, inner = swap_with(flat, axis, bit, inner_piece)
            cells = halo_join(cells, odd, inner, outer, 0)
        else:
            got = exchange(flat, axis, bit)
        flat = flat + got
    for axis, bit in reversed(steps[:halvings]):
        upper = (lax.axis_index(axis) // bit) % 2 == 1
        other = exchange(flat, axis, bit)
        flat = jnp.where(upper, jnp.concatenate([other, flat]), jnp.concatenate([flat, other]))
    return flat, cells


def silu_slope(value):
    sig = jax.nn.sigmoid(value)
    return sig * (1.0 + value * (1.0 - sig))


def spatial_forward(padded, conv_weight, tile_rows, tile_cols):
    running_sum = None
    for row_tap in range(3):
        tap_patch = jnp.concatenate(
            [
                padded[row_tap : row_tap + tile_rows, col_tap : col_tap + tile_cols]
                for col_tap in range(3)
            ],
            axis=-1,
        )
        tap_term = jnp.dot(
            tap_patch,
            conv_weight[row_tap].reshape(3 * C_IN, C_OUT),
            preferred_element_type=jnp.float32,
        )
        running_sum = tap_term if running_sum is None else running_sum + tap_term
    return running_sum


def window_conv(padded, kernel):
    return lax.conv_general_dilated(
        padded,
        kernel,
        window_strides=(1, 1),
        padding="VALID",
        dimension_numbers=("HWNC", "HWIO", "HWNC"),
        preferred_element_type=jnp.float32,
    )


def transposed_conv(padded_grad, conv_weight, out_rows, out_cols):
    input_sum = None
    for row_tap in range(3):
        grad_patch = jnp.concatenate(
            [
                padded_grad[
                    2 - row_tap : 2 - row_tap + out_rows, 2 - col_tap : 2 - col_tap + out_cols
                ]
                for col_tap in range(3)
            ],
            axis=-1,
        )
        flipped = jnp.concatenate([conv_weight[row_tap, col_tap].T for col_tap in range(3)], axis=0)
        tap_term = jnp.dot(grad_patch, flipped, preferred_element_type=jnp.float32)
        input_sum = tap_term if input_sum is None else input_sum + tap_term
    return input_sum


def same_group():
    rows = lax.broadcasted_iota(jnp.int32, (C_OUT, C_OUT), 0) // CPG
    cols = lax.broadcasted_iota(jnp.int32, (C_OUT, C_OUT), 1) // CPG
    return rows == cols


def block_weights(time_weight):
    tiled = jnp.tile(time_weight.reshape(3, C_OUT, CPG), (1, 1, GROUPS))
    return jnp.where(same_group()[None], tiled, jnp.zeros_like(tiled))


def group_blocks(dense):
    masked = jnp.where(same_group()[None], dense, jnp.zeros_like(dense))
    pick = (
        lax.broadcasted_iota(jnp.int32, (C_OUT, CPG), 0) % CPG
        == lax.broadcasted_iota(jnp.int32, (C_OUT, CPG), 1)
    ).astype(jnp.float32)
    return jnp.dot(masked, pick, precision=PRECISE).reshape(3, GROUPS, CPG, CPG)


def per_device(
    pixels, conv_weight, time_weight, class_weight, pixel_slot, straddle_dir, straddle_slot, labels
):
    tile_rows, tile_cols = (pixels.shape[0], pixels.shape[1])
    slot_count = P_OWN + S_STR
    padded_pixels = with_halo(pixels, (("row", 0), ("col", 1)), 1).reshape(
        tile_rows + 2, tile_cols + 2, DATES, C_IN
    )
    pre_act = window_conv(padded_pixels, conv_weight)
    hidden = jax.nn.silu(pre_act).astype(jnp.bfloat16)
    dense_time = block_weights(time_weight)
    padded_hidden = jnp.pad(hidden, ((0, 0), (0, 0), (1, 1), (0, 0)))
    mixed_time = None
    for time_tap in range(3):
        tap_term = jnp.dot(
            padded_hidden[:, :, time_tap : time_tap + DATES],
            dense_time[time_tap],
            preferred_element_type=jnp.float32,
        )
        mixed_time = tap_term if mixed_time is None else mixed_time + tap_term
    embedded = (
        jnp.mean(jax.nn.silu(mixed_time), axis=2)
        .astype(jnp.bfloat16)
        .reshape(tile_rows * tile_cols, C_OUT)
    )
    flat_slot = pixel_slot.reshape(tile_rows * tile_cols)
    membership = (jnp.arange(slot_count, dtype=jnp.int32)[:, None] == flat_slot[None, :]).astype(
        jnp.bfloat16
    )
    partial_value = jnp.dot(membership, embedded, preferred_element_type=jnp.float32)
    direction = straddle_dir.reshape(S_STR)
    owner_slot = straddle_slot.reshape(S_STR)
    own_slots = jnp.arange(P_OWN, dtype=jnp.int32)
    target = jnp.concatenate([4 * P_OWN + own_slots, direction * P_OWN + owner_slot])
    select = (jnp.arange(9 * P_OWN, dtype=jnp.int32)[:, None] == target[None, :]).astype(
        jnp.float32
    )
    outgoing = jnp.dot(select, partial_value, precision=PRECISE).reshape(3, 3, P_OWN, C_OUT)
    border = with_halo(outgoing.astype(jnp.bfloat16), (("row", 0), ("col", 1)), 1).astype(
        outgoing.dtype
    )
    parcel_sums = jnp.sum(border[0::2, 0::2], axis=(0, 1))
    centered = parcel_sums - jnp.mean(parcel_sums, axis=-1, keepdims=True)
    variance = jnp.mean(centered * centered, axis=-1, keepdims=True)
    inverse = lax.rsqrt(variance + EPSILON)
    normed = centered * inverse
    rounded = normed.astype(jnp.bfloat16)
    logits = jnp.dot(rounded, class_weight, preferred_element_type=jnp.float32)
    exp_logits = jnp.exp(logits)
    probability = exp_logits / jnp.sum(exp_logits, axis=-1, keepdims=True)
    label_hot = (
        labels.reshape(P_OWN)[:, None] == jnp.arange(CLASSES, dtype=jnp.int32)[None, :]
    ).astype(jnp.float32)
    parcel_total = P_OWN * lax.axis_size("row") * lax.axis_size("col")
    grad_logits = (probability - label_hot) / parcel_total
    class_term = jnp.dot(rounded.astype(jnp.float32).T, grad_logits, precision=PRECISE)
    grad_normed = jnp.dot(grad_logits, class_weight.astype(jnp.float32).T, precision=PRECISE)
    parcel_grad = (
        inverse
        * (
            grad_normed
            - jnp.mean(grad_normed, axis=-1, keepdims=True)
            - normed * jnp.mean(grad_normed * normed, axis=-1, keepdims=True)
        )
    ).astype(jnp.bfloat16)
    beside_all = with_halo(
        parcel_grad.reshape(1, 1, P_OWN, C_OUT), (("row", 0), ("col", 1)), 1
    ).reshape(9 * P_OWN, C_OUT)
    picker = (target[:, None] == jnp.arange(9 * P_OWN, dtype=jnp.int32)[None, :]).astype(
        jnp.bfloat16
    )
    slot_grad = jnp.dot(picker, beside_all, preferred_element_type=jnp.float32).astype(jnp.bfloat16)
    pixel_grad = jnp.dot(membership.T, slot_grad, preferred_element_type=jnp.float32).reshape(
        tile_rows, tile_cols, C_OUT
    )
    grad_mixed = ((pixel_grad / DATES)[:, :, None, :] * silu_slope(mixed_time)).astype(jnp.bfloat16)
    time_term = group_blocks(
        jnp.stack(
            [
                jnp.einsum(
                    "ijtc,ijtd->cd",
                    padded_hidden[:, :, time_tap : time_tap + DATES],
                    grad_mixed,
                    preferred_element_type=jnp.float32,
                )
                for time_tap in range(3)
            ]
        )
    )
    padded_mixed = jnp.pad(grad_mixed, ((0, 0), (0, 0), (1, 1), (0, 0)))
    grad_hidden = None
    for time_tap in range(3):
        tap_term = jnp.dot(
            padded_mixed[:, :, 2 - time_tap : 2 - time_tap + DATES],
            dense_time[time_tap].T,
            preferred_element_type=jnp.float32,
        )
        grad_hidden = tap_term if grad_hidden is None else grad_hidden + tap_term
    grad_pre = (grad_hidden * silu_slope(pre_act)).astype(jnp.bfloat16)
    conv_term = lax.conv_general_dilated(
        padded_pixels,
        grad_pre,
        window_strides=(1, 1),
        padding="VALID",
        dimension_numbers=("HWCN", "HWIO", "HWNC"),
        preferred_element_type=jnp.float32,
    )
    lanes = C_OUT
    conv_rows, time_rows, class_rows = (
        conv_term.size // lanes,
        time_term.size // lanes,
        class_term.size // lanes,
    )
    used = conv_rows + time_rows + class_rows
    total = -(-used // 32) * 32
    flat, padded_grad = butterfly_sum(
        jnp.concatenate(
            [
                conv_term.reshape(conv_rows, lanes),
                time_term.reshape(time_rows, lanes),
                class_term.reshape(class_rows, lanes),
                jnp.zeros((total - used, lanes), jnp.float32),
            ]
        ),
        grad_pre.reshape(tile_rows, tile_cols, DATES * C_OUT),
    )
    padded_grad = padded_grad.reshape(tile_rows + 2, tile_cols + 2, DATES, C_OUT)
    input_sum = transposed_conv(padded_grad, conv_weight, tile_rows, tile_cols)
    input_grad = input_sum.astype(jnp.bfloat16).reshape(tile_rows, tile_cols, DATES * C_IN)
    conv_grad = flat[:conv_rows].reshape(conv_term.shape)
    time_grad = flat[conv_rows : conv_rows + time_rows].reshape(time_term.shape)
    class_grad = flat[conv_rows + time_rows : used].reshape(class_term.shape)
    return (input_grad, conv_grad, time_grad, class_grad)


def solution(mesh):
    in_specs = (
        P("row", "col", None),
        P(),
        P(),
        P(),
        P("row", "col"),
        P("row", "col", None),
        P("row", "col", None),
        P("row", "col", None),
    )
    out_specs = (P("row", "col", None), P(), P(), P())
    return jax.shard_map(
        per_device, mesh=mesh, in_specs=in_specs, out_specs=out_specs, check_vma=False
    )
```
